256 devices in a mesh: seq: 16 (over y_lo, z), tm: 8 (over x, core), dp: 2 (over y_hi).
Axes of the slice: x: 4, y: 4 (y_hi: 2, y_lo: 2; y = y_hi * 2 + y_lo), z: 8, core: 2. Of those that a mesh axis runs over, the one named last changes fastest.
Arguments:
- queries: bfloat16 [16384, 8, 128], P(('dp', 'seq'), 'tm'), parts along dimension 0, may hold values from -6 to 6
- keys: bfloat16 [16384, 8, 128], P(('dp', 'seq'), 'tm'), parts along dimension 0, may hold values from -6 to 6
- values: bfloat16 [16384, 8, 128], P(('dp', 'seq'), 'tm'), parts along dimension 0, may hold values from -6 to 6
- token_cell: int32 [512], P('seq'), may hold values from 0 to 511, each once
- head_weight: bfloat16 [8, 128, 384], P('tm'), may hold values from -2 to 2
- norm_gain: float32 [384], replicated, may hold values from 0.1 to 1.9
- time_weight: bfloat16 [3, 384, 768], replicated, may hold values from -0.1875 to 0.1875
- frame_clip: int32 [32], P('dp'), parts along dimension 0, may hold values from 0 to 2, never falling along the last dimension, each value on 1 to 8 neighbouring positions
- cotangent: bfloat16 [32, 512, 768], P(('dp', 'tm'), 'seq'), parts along dimension 0, may hold values from -6 to 6
Outputs:
- grad_queries: bfloat16 [16384, 8, 128], P(('dp', 'seq'), 'tm'), parts along dimension 0
- grad_keys: bfloat16 [16384, 8, 128], P(('dp', 'seq'), 'tm'), parts along dimension 0
- grad_values: bfloat16 [16384, 8, 128], P(('dp', 'seq'), 'tm'), parts along dimension 0
The draws below stay inside these ranges and needn't reach their ends.
There are 2 independent parts, one for each index of `dp`. The reference program is written for one: setup_inputs(seed, part) draws one part's arguments, and reference() takes and returns one part's arrays. A program takes and returns all parts, laid end to end along the dimension named above; an argument that names none is the same for every part. Nothing has to cross between parts.
Inputs may be any that keep to these rules, and one draw needn't show every extreme that they name: `token_cell`: a permutation of the 512 cells. `frame_clip`: never falls along the frames.
All inputs are finite; a program needn't handle non-finite values.
Results may differ from the reference program's by a relative error of at most 0.023.
Values may be sent and summed in bfloat16 or wider, within the bound.
No kernel may reach another device: no remote copies, remote signals or barrier semaphores. Data moves between devices by JAX's collectives and lax.ppermute only.
A program may use at most 64 MiB of HBM per device.

```python
import math
import jax
import jax.numpy as jnp
import numpy as np
from jax import lax

HD = 128
CH = 384
OUT = 768
SLAB = 32
GRID_W = 32
HEADS = 8
FRAMES = 16
CELLS = 512
TOK_DEV = 512
TOKENS = 8192
N_SEQ = 16


def draw_queries(key, part):
    layout = (TOKENS, HEADS, HD)
    return jnp.clip(jax.random.normal(jax.random.fold_in(key, 21), layout), -6.0, 6.0).astype(jnp.bfloat16)


def draw_keys(key, part):
    layout = (TOKENS, HEADS, HD)
    return jnp.clip(jax.random.normal(jax.random.fold_in(key, 31), layout), -6.0, 6.0).astype(jnp.bfloat16)


def draw_head_weight(key, part):
    layout = (HEADS, HD, CH)
    fan_scale = (HEADS * HD) ** (-0.5)
    column_scale = jnp.exp(jax.random.uniform(jax.random.fold_in(key, 41), (1, 1, CH), minval=0.0, maxval=2.302585))
    base = jnp.clip(jax.random.normal(jax.random.fold_in(key, 43), layout), -5.0, 5.0)
    return jnp.clip(base * fan_scale * column_scale, -2.0, 2.0).astype(jnp.bfloat16)


def shard_levels(own_key, dims, cuts, smallest, top_value):
    loudness, own = 1.0, jax.random.fold_in(own_key, 6)
    for position, blocks in cuts:
        steps = jnp.exp(jax.random.uniform(jax.random.fold_in(own, position), (blocks,), jnp.float32, smallest / len(cuts), top_value / len(cuts)))
        loudness = loudness * jnp.repeat(steps, dims[position] // blocks).reshape([-1 if axis == position else 1 for axis in range(len(dims))])
    return loudness


def profile(amount, total, reach, skew):
    loads = [(1 << 20) // math.isqrt(grade ** skew) + 1 for grade in range(2, amount + 1)]
    surplus, counts = total - reach - (amount - 1), [1] * (amount - 1)
    while surplus > 0:
        free = [i for i in range(amount - 1) if counts[i] < reach]
        mass, remaining = sum([loads[i] for i in free]), surplus
        for i in free:
            more = min(reach - counts[i], max(1, remaining * loads[i] // mass), surplus)
            counts[i] = counts[i] + more
            surplus = surplus - more
    return np.array([reach] + counts)


def ragged(key, number_of, total, limit, lean):
    if number_of == 2:
        one = jax.random.randint(key, (), max(1, total - limit), min(limit, total - 1) + 1)
        return jnp.stack([one, total - one])
    tallies = jnp.asarray(profile(number_of, total, limit, lean), jnp.int32)
    twos = (number_of - 1) // 2
    giver, receiver = tallies[1:1 + 2 * twos:2], tallies[2:2 + 2 * twos:2]
    margin = jnp.minimum(giver - 1, limit - receiver)
    passed = jax.random.randint(jax.random.fold_in(key, 1), (twos,), 0, 1 << 20) % (margin + 1)
    tallies = tallies.at[1:1 + 2 * twos:2].set(giver - passed).at[2:2 + 2 * twos:2].set(receiver + passed)
    return tallies[jax.random.permutation(jax.random.fold_in(key, 2), number_of)]


def gaussian(stream_key, dims, scale, reach, cuts=(), kind=jnp.bfloat16):
    entries = jax.random.normal(stream_key, dims, jnp.float32) * scale
    if len(cuts) > 0:
        entries = shard_levels(stream_key, dims, cuts, -0.22, 0.18) * entries
    return jnp.clip(entries, min=-reach, max=reach).astype(kind)


def setup_inputs(seed: int = 0, part: int = 0) -> dict:
    streams_of = jax.random.split(jax.random.key(seed), 10)
    part_splits = jax.random.split(jax.random.fold_in(streams_of[9], part), 10)
    queries = draw_queries(jax.random.fold_in(jax.random.fold_in(streams_of[9], part), 71), part)
    keys = draw_keys(jax.random.fold_in(jax.random.fold_in(streams_of[9], part), 71), part)
    values = gaussian(part_splits[2], (TOKENS, HEADS, HD), 1.0, 6.0, ((0, 16), (1, 8)))
    token_cell = jax.random.permutation(streams_of[3], CELLS).astype(jnp.int32)
    head_weight = draw_head_weight(jax.random.fold_in(streams_of[9], 71), part)
    norm_gain = jnp.clip(1.0 + 0.18 * jax.random.normal(streams_of[5], (CH,), jnp.float32), 0.1, 1.9)
    time_weight = gaussian(streams_of[6], (3, CH, OUT), (3 * CH) ** -0.5, 0.1875)
    frame_clip = jnp.searchsorted(jnp.cumsum(ragged(part_splits[7], 3, FRAMES, FRAMES // 2, 0)), jnp.arange(FRAMES), side="right").astype(jnp.int32)
    cotangent = gaussian(part_splits[8], (FRAMES, CELLS, OUT), 1.0, 6.0, ((0, 8), (1, 16)))
    return dict(queries=queries, keys=keys, values=values, token_cell=token_cell, head_weight=head_weight, norm_gain=norm_gain, time_weight=time_weight, frame_clip=frame_clip, cotangent=cotangent)


def frequencies(pair_count):
    return 1.0 / 10000.0 ** (jnp.arange(pair_count, dtype=jnp.float32) / pair_count)

def rope_tables(frame_pos, cell_ids):
    pair_count = HD // 2
    part_side = pair_count // 3
    part_time = pair_count - 2 * part_side
    grid_row = (cell_ids // GRID_W).astype(jnp.float32)
    grid_col = (cell_ids % GRID_W).astype(jnp.float32)
    angles = jnp.concatenate([frame_pos.astype(jnp.float32)[:, None] * frequencies(part_time)[None, :], grid_row[:, None] * frequencies(part_side)[None, :], grid_col[:, None] * frequencies(part_side)[None, :]], axis=1)
    return (jnp.cos(angles), jnp.sin(angles))

def rotate(vectors, cos_table, sin_table, direction):
    layout = vectors.shape
    paired = vectors.reshape(layout[:-1] + (layout[-1] // 2, 2))
    former = paired[..., 0]
    latter = paired[..., 1]
    out_former = former * cos_table - direction * latter * sin_table
    out_latter = direction * former * sin_table + latter * cos_table
    return jnp.stack([out_former, out_latter], axis=-1).reshape(layout)

def tap_mask(frame_clip):
    frame_total = frame_clip.shape[0]
    frame_ids = jnp.arange(frame_total, dtype=jnp.int32)
    columns = []
    for offset in range(3):
        target = frame_ids + offset
        inside = target < frame_total
        same_clip = frame_clip[jnp.minimum(target, frame_total - 1)] == frame_clip
        columns.append(jnp.logical_and(inside, same_clip).astype(jnp.float32))
    return jnp.stack(columns, axis=1)

def head_forward(q_head, k_head, v_head, score_scale, block_rows):

    def one_block(query_block):
        scores = jnp.dot(query_block, k_head.T, preferred_element_type=jnp.float32) * score_scale
        row_top = lax.optimization_barrier(jnp.max(scores, axis=1, keepdims=True))
        weights = jnp.exp(scores - row_top)
        row_total = lax.optimization_barrier(jnp.sum(weights, axis=1, keepdims=True))
        summed = jnp.dot(weights.astype(jnp.bfloat16), v_head, preferred_element_type=jnp.float32) / row_total
        return (summed.astype(jnp.bfloat16), (row_top + jnp.log(row_total))[:, 0])
    attended, log_total = lax.map(one_block, q_head.reshape(TOKENS // block_rows, block_rows, HD))
    return (attended.reshape(TOKENS, HD), log_total.reshape(TOKENS))

def head_backward(q_head, k_head, v_head, out_head, grad_head, log_head, score_scale, block_rows):
    row_delta = lax.optimization_barrier(jnp.sum(grad_head.astype(jnp.float32) * out_head.astype(jnp.float32), axis=1))

    def one_block(carried, pieces):
        grad_k, grad_v = carried
        query_block, grad_block, log_block, delta_block = pieces
        scores = jnp.dot(query_block, k_head.T, preferred_element_type=jnp.float32) * score_scale
        weights = jnp.exp(scores - log_block[:, None])
        grad_w = jnp.dot(grad_block, v_head.T, preferred_element_type=jnp.float32)
        grad_s = (weights * (grad_w - delta_block[:, None])).astype(jnp.bfloat16)
        grad_q = jnp.dot(grad_s, k_head, preferred_element_type=jnp.float32) * score_scale
        grad_k = grad_k + jnp.dot(grad_s.T, query_block, preferred_element_type=jnp.float32) * score_scale
        grad_v = grad_v + jnp.dot(weights.astype(jnp.bfloat16).T, grad_block, preferred_element_type=jnp.float32)
        return ((grad_k, grad_v), grad_q)
    block_count = TOKENS // block_rows
    start_state = (jnp.zeros((TOKENS, HD), jnp.float32), jnp.zeros((TOKENS, HD), jnp.float32))
    (grad_k, grad_v), grad_q = lax.scan(one_block, start_state, (q_head.reshape(block_count, block_rows, HD), grad_head.reshape(block_count, block_rows, HD), log_head.reshape(block_count, block_rows), row_delta.reshape(block_count, block_rows)))
    return (grad_q.reshape(TOKENS, HD), grad_k, grad_v)

def reference(queries, keys, values, token_cell, head_weight, norm_gain, time_weight, frame_clip, cotangent):
    score_scale = HD ** (-0.5)
    token_ids = jnp.arange(TOKENS, dtype=jnp.int32)
    device_pos = token_ids // TOK_DEV
    local_pos = token_ids % TOK_DEV
    frame_pos = local_pos // SLAB
    cell_ids = token_cell[device_pos * SLAB + local_pos % SLAB]
    cos_table, sin_table = rope_tables(frame_pos, cell_ids)
    cos_wide = cos_table[:, None, :]
    sin_wide = sin_table[:, None, :]
    rot_q = rotate(queries.astype(jnp.float32), cos_wide, sin_wide, 1.0).astype(jnp.bfloat16)
    rot_k = rotate(keys.astype(jnp.float32), cos_wide, sin_wide, 1.0).astype(jnp.bfloat16)
    block_rows = math.gcd(TOKENS, 1024)
    q_heads = jnp.transpose(rot_q, (1, 0, 2))
    k_heads = jnp.transpose(rot_k, (1, 0, 2))
    v_heads = jnp.transpose(values, (1, 0, 2))
    out_heads, log_heads = lax.map(lambda triple: head_forward(triple[0], triple[1], triple[2], score_scale, block_rows), (q_heads, k_heads, v_heads))
    attended = jnp.transpose(out_heads, (1, 0, 2))
    grid_order = attended.reshape(N_SEQ, FRAMES, SLAB, HEADS, HD).transpose(1, 0, 2, 3, 4).reshape(FRAMES, CELLS, HEADS, HD)
    mixed = jnp.einsum('fchd,hde->fce', grid_order.astype(jnp.float32), head_weight.astype(jnp.float32))
    inverse = lax.rsqrt(lax.optimization_barrier(jnp.mean(mixed * mixed, axis=2, keepdims=True)) + 1e-06)
    normed = mixed * inverse * norm_gain
    mask_table = tap_mask(frame_clip)
    padded = jnp.concatenate([cotangent, jnp.zeros((2, CELLS, OUT), jnp.bfloat16)], axis=0)
    grad_act = jnp.zeros((FRAMES, CELLS, CH), jnp.float32)
    for offset in range(3):
        term = jnp.einsum('fco,io->fci', padded[offset:offset + FRAMES].astype(jnp.float32), time_weight[offset].astype(jnp.float32))
        grad_act = grad_act + mask_table[:, offset][:, None, None] * term
    sigmoid_n = jax.nn.sigmoid(normed)
    grad_normed = grad_act * sigmoid_n * (1.0 + normed * (1.0 - sigmoid_n))
    gained = grad_normed * norm_gain
    grad_mixed = (inverse * gained - inverse * inverse * inverse * mixed * lax.optimization_barrier(jnp.mean(gained * mixed, axis=2, keepdims=True))).astype(jnp.bfloat16)
    grad_grid = jnp.einsum('fce,hde->fchd', grad_mixed.astype(jnp.float32), head_weight.astype(jnp.float32)).astype(jnp.bfloat16)
    grad_att = grad_grid.reshape(FRAMES, N_SEQ, SLAB, HEADS, HD).transpose(1, 0, 2, 3, 4).reshape(TOKENS, HEADS, HD)
    grad_heads = jnp.transpose(grad_att, (1, 0, 2))
    grad_q, grad_k, grad_v = lax.map(lambda group: head_backward(group[0], group[1], group[2], group[3], group[4], group[5], score_scale, block_rows), (q_heads, k_heads, v_heads, out_heads, grad_heads, log_heads))
    grad_q = jnp.transpose(grad_q, (1, 0, 2))
    grad_k = jnp.transpose(grad_k, (1, 0, 2))
    grad_v = jnp.transpose(grad_v, (1, 0, 2))
    grad_queries = rotate(grad_q, cos_wide, sin_wide, -1.0).astype(jnp.bfloat16)
    grad_keys = rotate(grad_k, cos_wide, sin_wide, -1.0).astype(jnp.bfloat16)
    return (grad_queries, grad_keys, grad_v.astype(jnp.bfloat16))
```

```python
import math

import jax
import jax.numpy as jnp
from jax import lax
from jax.sharding import PartitionSpec as P

HD = 128
GRID_W = 32


def shifted(value, axis, steps):
    count = lax.axis_size(axis)
    initial, last = (max(0, -steps), min(count, count - steps))
    return lax.ppermute(value, axis, [(source, source + steps) for source in range(initial, last)])


def frequencies(pair_count):
    return 1.0 / 10000.0 ** (jnp.arange(pair_count, dtype=jnp.float32) / pair_count)


def rope_tables(frame_pos, cell_ids):
    pair_count = HD // 2
    part_side = pair_count // 3
    part_time = pair_count - 2 * part_side
    grid_row = (cell_ids // GRID_W).astype(jnp.float32)
    grid_col = (cell_ids % GRID_W).astype(jnp.float32)
    angles = jnp.concatenate(
        [
            frame_pos.astype(jnp.float32)[:, None] * frequencies(part_time)[None, :],
            grid_row[:, None] * frequencies(part_side)[None, :],
            grid_col[:, None] * frequencies(part_side)[None, :],
        ],
        axis=1,
    )
    return (jnp.cos(angles), jnp.sin(angles))


def rotate(vectors, cos_table, sin_table, direction):
    layout = vectors.shape
    paired = vectors.reshape(layout[:-1] + (layout[-1] // 2, 2))
    former = paired[..., 0]
    latter = paired[..., 1]
    out_former = former * cos_table - direction * latter * sin_table
    out_latter = direction * former * sin_table + latter * cos_table
    return jnp.stack([out_former, out_latter], axis=-1).reshape(layout)


def tap_mask(frame_clip):
    frame_total = frame_clip.shape[0]
    frame_ids = jnp.arange(frame_total, dtype=jnp.int32)
    columns = []
    for offset in range(3):
        target = frame_ids + offset
        inside = target < frame_total
        same_clip = frame_clip[jnp.minimum(target, frame_total - 1)] == frame_clip
        columns.append(jnp.logical_and(inside, same_clip).astype(jnp.float32))
    return jnp.stack(columns, axis=1)


def split_exact(values):
    high = lax.reduce_precision(values, exponent_bits=8, mantissa_bits=7)
    rest = values - high
    middle = lax.reduce_precision(rest, exponent_bits=8, mantissa_bits=7)
    low = rest - middle
    return jnp.stack([high, middle, low]).astype(jnp.bfloat16)


def cross(left, right):
    return lax.dot_general(
        left, right, (((1,), (1,)), ((), ())), preferred_element_type=jnp.float32
    )


def inner(left, right):
    return lax.dot_general(
        left, right, (((0,), (0,)), ((), ())), preferred_element_type=jnp.float32
    )


def on_device(
    queries, keys, values, token_cell, head_weight, norm_gain, time_weight, frame_clip, cotangent
):
    score_scale = HD ** (-0.5)
    tok_local = queries.shape[0]
    slab_cells = token_cell.shape[0]
    span_frames = cotangent.shape[0]
    channels = head_weight.shape[2]
    frame_pos = jnp.arange(tok_local, dtype=jnp.int32) // slab_cells
    cell_ids = jnp.tile(token_cell, tok_local // slab_cells)
    cos_table, sin_table = rope_tables(frame_pos, cell_ids)
    rot_q = rotate(queries[:, 0, :].astype(jnp.float32), cos_table, sin_table, 1.0).astype(
        jnp.bfloat16
    )
    rot_k = rotate(keys[:, 0, :].astype(jnp.float32), cos_table, sin_table, 1.0).astype(
        jnp.bfloat16
    )
    plain_v = values[:, 0, :]
    pair_all = lax.all_gather(jnp.concatenate([rot_k, plain_v], axis=1), "seq", axis=0, tiled=True)
    keys_all, values_all = pair_all[:, :HD], pair_all[:, HD:]
    total_tokens = keys_all.shape[0]
    key_block = math.gcd(total_tokens, 1024)
    block_count = total_tokens // key_block

    def forward_step(block_id, state):
        running_top, running_total, running_sum = state
        key_piece = lax.dynamic_slice_in_dim(keys_all, block_id * key_block, key_block, 0)
        value_piece = lax.dynamic_slice_in_dim(values_all, block_id * key_block, key_block, 0)
        scores = cross(rot_q, key_piece) * score_scale
        new_top = jnp.maximum(running_top, jnp.max(scores, axis=1))
        factor = jnp.exp(running_top - new_top)
        weights = jnp.exp(scores - new_top[:, None])
        running_total = running_total * factor + jnp.sum(weights, axis=1)
        running_sum = running_sum * factor[:, None] + jnp.dot(
            weights.astype(jnp.bfloat16), value_piece, preferred_element_type=jnp.float32
        )
        return (new_top, running_total, running_sum)

    start_state = (
        jnp.full((tok_local,), -1e30, jnp.float32),
        jnp.zeros((tok_local,), jnp.float32),
        jnp.zeros((tok_local, HD), jnp.float32),
    )
    row_top, row_total, summed = lax.fori_loop(0, block_count, forward_step, start_state)
    attended = (summed / row_total[:, None]).astype(jnp.bfloat16)
    log_total = row_top + jnp.log(row_total)
    span_rows = span_frames * slab_cells
    mixed = (
        lax.psum_scatter(
            jnp.dot(attended, head_weight[0], preferred_element_type=jnp.float32).astype(
                jnp.bfloat16
            ),
            "tm",
            scatter_dimension=0,
            tiled=True,
        )
        .astype(jnp.float32)
        .reshape(span_frames, slab_cells, channels)
    )
    inverse = lax.rsqrt(jnp.mean(mixed * mixed, axis=2, keepdims=True) + 1e-06)
    normed = mixed * inverse * norm_gain
    mask_table = tap_mask(frame_clip)
    first_frame = lax.axis_index("tm") * span_frames
    local_mask = lax.dynamic_slice_in_dim(mask_table, first_frame, span_frames, 0)
    following = shifted(cotangent, "tm", -1)
    extended = jnp.concatenate([cotangent, following], axis=0)
    grad_act = jnp.zeros((span_frames, slab_cells, channels), jnp.float32)
    for offset in range(3):
        term = jnp.einsum(
            "fco,io->fci",
            extended[offset : offset + span_frames],
            time_weight[offset],
            preferred_element_type=jnp.float32,
        )
        grad_act = grad_act + local_mask[:, offset][:, None, None] * term
    sigmoid_n = jax.nn.sigmoid(normed)
    grad_normed = grad_act * sigmoid_n * (1.0 + normed * (1.0 - sigmoid_n))
    gained = grad_normed * norm_gain
    grad_mixed = (
        inverse * gained
        - inverse * inverse * inverse * mixed * jnp.mean(gained * mixed, axis=2, keepdims=True)
    ).astype(jnp.bfloat16)
    grad_mixed = grad_mixed.reshape(span_rows, channels)
    grad_out = cross(lax.all_gather(grad_mixed, "tm", axis=0, tiled=True), head_weight[0]).astype(
        jnp.bfloat16
    )
    row_delta = jnp.sum(grad_out.astype(jnp.float32) * attended.astype(jnp.float32), axis=1)

    def score_block(block_id):
        key_piece = lax.dynamic_slice_in_dim(keys_all, block_id * key_block, key_block, 0)
        value_piece = lax.dynamic_slice_in_dim(values_all, block_id * key_block, key_block, 0)
        scores = cross(rot_q, key_piece) * score_scale
        weights = jnp.exp(scores - log_total[:, None])
        grad_w = cross(grad_out, value_piece)
        grad_s = (weights * (grad_w - row_delta[:, None])).astype(jnp.bfloat16)
        return (key_piece, weights, grad_s)

    def query_step(block_id, grad_q):
        key_piece, weights, grad_s = score_block(block_id)
        return grad_q + jnp.dot(grad_s, key_piece, preferred_element_type=jnp.float32) * score_scale

    grad_q = lax.fori_loop(0, block_count, query_step, jnp.zeros((tok_local, HD), jnp.float32))
    fold_start = (jnp.zeros((tok_local, HD), jnp.float32), jnp.zeros((tok_local, HD), jnp.float32))
    stat_rows = split_exact(jnp.stack([log_total, row_delta]))
    stat_rows = stat_rows.reshape(-1, 2 * HD)
    stat_pad = (-stat_rows.shape[0]) % 16
    stat_rows = jnp.pad(stat_rows, ((0, stat_pad), (0, 0)))
    packed = jnp.concatenate([jnp.concatenate([rot_q, grad_out], axis=1), stat_rows], axis=0)
    block_rows = packed.shape[0]
    seq_count = lax.axis_size("seq")
    gathered = lax.all_gather(packed, "seq", axis=0, tiled=True).reshape(
        seq_count, block_rows, 2 * HD
    )
    body_rows = gathered[:, :tok_local, :].reshape(seq_count * tok_local, 2 * HD)
    piece_q = body_rows[:, :HD]
    piece_grad = body_rows[:, HD:]
    stat_all = gathered[:, tok_local:, :].reshape(seq_count, -1)[:, : 6 * tok_local]
    stat_all = stat_all.reshape(seq_count, 3, 2, tok_local).astype(jnp.float32)
    stat_all = (stat_all[:, 0] + stat_all[:, 1]) + stat_all[:, 2]
    piece_log = stat_all[:, 0, :].reshape(-1)
    piece_delta = stat_all[:, 1, :].reshape(-1)
    piece_count = piece_q.shape[0]
    sub_rows = math.gcd(piece_count, 1024)

    def sub_step(sub_id, inner_carry):
        grad_k, grad_v = inner_carry
        offset = sub_id * sub_rows
        query_block = lax.dynamic_slice_in_dim(piece_q, offset, sub_rows, 0).astype(jnp.bfloat16)
        grad_rows = lax.dynamic_slice_in_dim(piece_grad, offset, sub_rows, 0).astype(jnp.bfloat16)
        log_block = lax.dynamic_slice_in_dim(piece_log, offset, sub_rows, 0)
        delta_block = lax.dynamic_slice_in_dim(piece_delta, offset, sub_rows, 0)
        scores = cross(query_block, rot_k) * score_scale
        weights = jnp.exp(scores - log_block[:, None])
        grad_w = cross(grad_rows, plain_v)
        grad_s = (weights * (grad_w - delta_block[:, None])).astype(jnp.bfloat16)
        grad_k = grad_k + inner(grad_s, query_block) * score_scale
        grad_v = grad_v + inner(weights.astype(jnp.bfloat16), grad_rows)
        return (grad_k, grad_v)

    grad_k, grad_v = lax.fori_loop(0, piece_count // sub_rows, sub_step, fold_start)
    grad_queries = rotate(grad_q, cos_table, sin_table, -1.0).astype(jnp.bfloat16)[:, None, :]
    grad_keys = rotate(grad_k, cos_table, sin_table, -1.0).astype(jnp.bfloat16)[:, None, :]
    grad_values = grad_v.astype(jnp.bfloat16)[:, None, :]
    return (grad_queries, grad_keys, grad_values)


def solution(mesh):
    in_specs = (
        P(("dp", "seq"), "tm", None),
        P(("dp", "seq"), "tm", None),
        P(("dp", "seq"), "tm", None),
        P("seq"),
        P("tm", None, None),
        P(),
        P(),
        P("dp"),
        P(("dp", "tm"), "seq", None),
    )
    out_specs = (
        P(("dp", "seq"), "tm", None),
        P(("dp", "seq"), "tm", None),
        P(("dp", "seq"), "tm", None),
    )
    return jax.shard_map(
        on_device, mesh=mesh, in_specs=in_specs, out_specs=out_specs, check_vma=False
    )
```

```python
import functools
import math

import jax
import jax.numpy as jnp
from jax import lax
from jax.experimental import pallas as pl
from jax.experimental.pallas import tpu as pltpu
from jax.sharding import PartitionSpec as P

HD = 128
GRID_W = 32
SCALE = HD ** (-0.5)


def forward_kernel(key_block, q_ref, kv_ref, out_ref, lse_ref):
    q = q_ref[...]
    rows = q.shape[0]
    steps = kv_ref.shape[0] // key_block

    def body(step, carry):
        top, total, acc = carry
        start = pl.multiple_of(step * key_block, key_block)
        k = kv_ref[pl.ds(start, key_block), :HD]
        v = kv_ref[pl.ds(start, key_block), HD:]
        s = lax.dot_general(q, k, (((1,), (1,)), ((), ())), preferred_element_type=jnp.float32) * SCALE
        new_top = jnp.maximum(top, jnp.max(s, axis=1, keepdims=True))
        factor = jnp.exp(top - new_top)
        w = jnp.exp(s - new_top)
        total = total * factor + jnp.sum(w, axis=1, keepdims=True)
        acc = acc * factor + jnp.dot(w.astype(jnp.bfloat16), v, preferred_element_type=jnp.float32)
        return new_top, total, acc

    start_state = (
        jnp.full((rows, 1), -1e30, jnp.float32),
        jnp.zeros((rows, 1), jnp.float32),
        jnp.zeros((rows, HD), jnp.float32),
    )
    top, total, acc = lax.fori_loop(0, steps, body, start_state)
    out_ref[...] = (acc / total).astype(out_ref.dtype)
    lse_ref[...] = top + jnp.log(total)


def attention_forward(q, kv_all, query_block=256, key_block=512):
    rows = q.shape[0]
    keys = kv_all.shape[0]
    cost = pl.CostEstimate(
        flops=4 * rows * keys * HD, transcendentals=rows * keys, bytes_accessed=2 * HD * (2 * rows + 2 * keys)
    )
    return pl.pallas_call(
        functools.partial(forward_kernel, key_block),
        grid=(rows // query_block,),
        in_specs=[
            pl.BlockSpec((query_block, HD), lambda i: (i, 0)),
            pl.BlockSpec((keys, 2 * HD), lambda i: (0, 0)),
        ],
        out_specs=[
            pl.BlockSpec((query_block, HD), lambda i: (i, 0)),
            pl.BlockSpec((query_block, 1), lambda i: (i, 0)),
        ],
        out_shape=[
            jax.ShapeDtypeStruct((rows, HD), jnp.bfloat16),
            jax.ShapeDtypeStruct((rows, 1), jnp.float32),
        ],
        compiler_params=pltpu.CompilerParams(dimension_semantics=("arbitrary",)),
        cost_estimate=cost,
    )(q, kv_all)


def query_grad_kernel(key_block, q_ref, g_ref, lse_ref, delta_ref, kv_ref, dq_ref):
    q = q_ref[...]
    g = g_ref[...]
    lse = lse_ref[...]
    delta = delta_ref[...]
    steps = kv_ref.shape[0] // key_block

    def body(step, acc):
        start = pl.multiple_of(step * key_block, key_block)
        k = kv_ref[pl.ds(start, key_block), :HD]
        v = kv_ref[pl.ds(start, key_block), HD:]
        s = lax.dot_general(q, k, (((1,), (1,)), ((), ())), preferred_element_type=jnp.float32) * SCALE
        w = jnp.exp(s - lse)
        gw = lax.dot_general(g, v, (((1,), (1,)), ((), ())), preferred_element_type=jnp.float32)
        gs = (w * (gw - delta)).astype(jnp.bfloat16)
        return acc + jnp.dot(gs, k, preferred_element_type=jnp.float32)

    acc = lax.fori_loop(0, steps, body, jnp.zeros(dq_ref.shape, jnp.float32))
    dq_ref[...] = acc * SCALE


def attention_query_grad(q, g, lse_col, delta_col, kv_all, query_block=256, key_block=512):
    rows = q.shape[0]
    keys = kv_all.shape[0]
    cost = pl.CostEstimate(
        flops=6 * rows * keys * HD, transcendentals=rows * keys, bytes_accessed=2 * HD * (3 * rows + 2 * keys)
    )
    row_spec = pl.BlockSpec((query_block, HD), lambda i: (i, 0))
    col_spec = pl.BlockSpec((query_block, 1), lambda i: (i, 0))
    whole = pl.BlockSpec((keys, 2 * HD), lambda i: (0, 0))
    return pl.pallas_call(
        functools.partial(query_grad_kernel, key_block),
        grid=(rows // query_block,),
        in_specs=[row_spec, row_spec, col_spec, col_spec, whole],
        out_specs=pl.BlockSpec((query_block, HD), lambda i: (i, 0)),
        out_shape=jax.ShapeDtypeStruct((rows, HD), jnp.float32),
        compiler_params=pltpu.CompilerParams(dimension_semantics=("arbitrary",)),
        cost_estimate=cost,
    )(q, g, lse_col, delta_col, kv_all)


def key_grad_kernel(query_block, block_stride, k_ref, v_ref, qg_ref, lse_ref, delta_ref, dk_ref, dv_ref):
    k = k_ref[...]
    v = v_ref[...]
    steps = lse_ref.shape[1] // query_block

    def body(step, carry):
        dk, dv = carry
        start = pl.multiple_of(step * block_stride, 16)
        column = pl.multiple_of(step * query_block, query_block)
        q = qg_ref[pl.ds(start, query_block), :HD]
        g = qg_ref[pl.ds(start, query_block), HD:]
        lse = lse_ref[:, pl.ds(column, query_block)]
        delta = delta_ref[:, pl.ds(column, query_block)]
        s = lax.dot_general(k, q, (((1,), (1,)), ((), ())), preferred_element_type=jnp.float32) * SCALE
        w = jnp.exp(s - lse)
        gw = lax.dot_general(v, g, (((1,), (1,)), ((), ())), preferred_element_type=jnp.float32)
        gs = (w * (gw - delta)).astype(jnp.bfloat16)
        dk = dk + jnp.dot(gs, q, preferred_element_type=jnp.float32)
        dv = dv + jnp.dot(w.astype(jnp.bfloat16), g, preferred_element_type=jnp.float32)
        return dk, dv

    zero = jnp.zeros(dk_ref.shape, jnp.float32)
    dk, dv = lax.fori_loop(0, steps, body, (zero, zero))
    dk_ref[...] = dk * SCALE
    dv_ref[...] = dv


def attention_key_grad(k, v, qg_all, lse_row, delta_row, query_block, block_stride, key_rows=256):
    rows = k.shape[0]
    queries = lse_row.shape[1]
    cost = pl.CostEstimate(
        flops=8 * rows * queries * HD, transcendentals=rows * queries, bytes_accessed=2 * HD * (2 * rows + 2 * queries)
    )
    row_spec = pl.BlockSpec((key_rows, HD), lambda i: (i, 0))
    whole = pl.BlockSpec(qg_all.shape, lambda i: (0, 0))
    stat = pl.BlockSpec((1, queries), lambda i: (0, 0))
    return pl.pallas_call(
        functools.partial(key_grad_kernel, query_block, block_stride),
        grid=(rows // key_rows,),
        in_specs=[row_spec, row_spec, whole, stat, stat],
        out_specs=[row_spec, row_spec],
        out_shape=[jax.ShapeDtypeStruct((rows, HD), jnp.float32)] * 2,
        compiler_params=pltpu.CompilerParams(dimension_semantics=("arbitrary",)),
        cost_estimate=cost,
    )(k, v, qg_all, lse_row, delta_row)


def shifted(value, axis, steps):
    count = lax.axis_size(axis)
    initial, last = (max(0, -steps), min(count, count - steps))
    return lax.ppermute(value, axis, [(source, source + steps) for source in range(initial, last)])


def frequencies(pair_count):
    return 1.0 / 10000.0 ** (jnp.arange(pair_count, dtype=jnp.float32) / pair_count)


def rope_tables(frame_pos, cell_ids):
    pair_count = HD // 2
    part_side = pair_count // 3
    part_time = pair_count - 2 * part_side
    grid_row = (cell_ids // GRID_W).astype(jnp.float32)
    grid_col = (cell_ids % GRID_W).astype(jnp.float32)
    angles = jnp.concatenate(
        [
            frame_pos.astype(jnp.float32)[:, None] * frequencies(part_time)[None, :],
            grid_row[:, None] * frequencies(part_side)[None, :],
            grid_col[:, None] * frequencies(part_side)[None, :],
        ],
        axis=1,
    )
    return (jnp.cos(angles), jnp.sin(angles))


def rotate(vectors, cos_table, sin_table, direction):
    layout = vectors.shape
    paired = vectors.reshape(layout[:-1] + (layout[-1] // 2, 2))
    former = paired[..., 0]
    latter = paired[..., 1]
    out_former = former * cos_table - direction * latter * sin_table
    out_latter = direction * former * sin_table + latter * cos_table
    return jnp.stack([out_former, out_latter], axis=-1).reshape(layout)


def tap_mask(frame_clip):
    frame_total = frame_clip.shape[0]
    frame_ids = jnp.arange(frame_total, dtype=jnp.int32)
    columns = []
    for offset in range(3):
        target = frame_ids + offset
        inside = target < frame_total
        same_clip = frame_clip[jnp.minimum(target, frame_total - 1)] == frame_clip
        columns.append(jnp.logical_and(inside, same_clip).astype(jnp.float32))
    return jnp.stack(columns, axis=1)


def split_exact(values):
    high = lax.reduce_precision(values, exponent_bits=8, mantissa_bits=7)
    rest = values - high
    middle = lax.reduce_precision(rest, exponent_bits=8, mantissa_bits=7)
    low = rest - middle
    return jnp.stack([high, middle, low]).astype(jnp.bfloat16)


def cross(left, right):
    return lax.dot_general(
        left, right, (((1,), (1,)), ((), ())), preferred_element_type=jnp.float32
    )


def inner(left, right):
    return lax.dot_general(
        left, right, (((0,), (0,)), ((), ())), preferred_element_type=jnp.float32
    )


def on_device(
    queries, keys, values, token_cell, head_weight, norm_gain, time_weight, frame_clip, cotangent
):
    score_scale = HD ** (-0.5)
    tok_local = queries.shape[0]
    slab_cells = token_cell.shape[0]
    span_frames = cotangent.shape[0]
    channels = head_weight.shape[2]
    frame_pos = jnp.arange(tok_local, dtype=jnp.int32) // slab_cells
    cell_ids = jnp.tile(token_cell, tok_local // slab_cells)
    cos_table, sin_table = rope_tables(frame_pos, cell_ids)
    rot_q = rotate(queries[:, 0, :].astype(jnp.float32), cos_table, sin_table, 1.0).astype(
        jnp.bfloat16
    )
    rot_k = rotate(keys[:, 0, :].astype(jnp.float32), cos_table, sin_table, 1.0).astype(
        jnp.bfloat16
    )
    plain_v = values[:, 0, :]
    pair_all = lax.all_gather(jnp.concatenate([rot_k, plain_v], axis=1), "seq", axis=0, tiled=True)
    attended, log_col = attention_forward(rot_q, pair_all)
    log_total = log_col[:, 0]
    span_rows = span_frames * slab_cells
    mixed = (
        lax.psum_scatter(
            jnp.dot(attended, head_weight[0], preferred_element_type=jnp.float32).astype(
                jnp.bfloat16
            ),
            "tm",
            scatter_dimension=0,
            tiled=True,
        )
        .astype(jnp.float32)
        .reshape(span_frames, slab_cells, channels)
    )
    inverse = lax.rsqrt(jnp.mean(mixed * mixed, axis=2, keepdims=True) + 1e-06)
    normed = mixed * inverse * norm_gain
    mask_table = tap_mask(frame_clip)
    first_frame = lax.axis_index("tm") * span_frames
    local_mask = lax.dynamic_slice_in_dim(mask_table, first_frame, span_frames, 0)
    following = shifted(cotangent, "tm", -1)
    extended = jnp.concatenate([cotangent, following], axis=0)
    grad_act = jnp.zeros((span_frames, slab_cells, channels), jnp.float32)
    for offset in range(3):
        term = jnp.einsum(
            "fco,io->fci",
            extended[offset : offset + span_frames],
            time_weight[offset],
            preferred_element_type=jnp.float32,
        )
        grad_act = grad_act + local_mask[:, offset][:, None, None] * term
    sigmoid_n = jax.nn.sigmoid(normed)
    grad_normed = grad_act * sigmoid_n * (1.0 + normed * (1.0 - sigmoid_n))
    gained = grad_normed * norm_gain
    grad_mixed = (
        inverse * gained
        - inverse * inverse * inverse * mixed * jnp.mean(gained * mixed, axis=2, keepdims=True)
    ).astype(jnp.bfloat16)
    grad_mixed = grad_mixed.reshape(span_rows, channels)
    grad_out = cross(lax.all_gather(grad_mixed, "tm", axis=0, tiled=True), head_weight[0]).astype(
        jnp.bfloat16
    )
    row_delta = jnp.sum(grad_out.astype(jnp.float32) * attended.astype(jnp.float32), axis=1)

    grad_q = attention_query_grad(rot_q, grad_out, log_col, row_delta[:, None], pair_all)
    stat_rows = split_exact(jnp.stack([log_total, row_delta]))
    stat_rows = stat_rows.reshape(-1, 2 * HD)
    stat_pad = (-stat_rows.shape[0]) % 16
    stat_rows = jnp.pad(stat_rows, ((0, stat_pad), (0, 0)))
    packed = jnp.concatenate([jnp.concatenate([rot_q, grad_out], axis=1), stat_rows], axis=0)
    block_rows = packed.shape[0]
    seq_count = lax.axis_size("seq")
    gathered = lax.all_gather(packed, "seq", axis=0, tiled=True).reshape(
        seq_count, block_rows, 2 * HD
    )
    stat_all = gathered[:, tok_local:, :].reshape(seq_count, -1)[:, : 6 * tok_local]
    stat_all = stat_all.reshape(seq_count, 3, 2, tok_local).astype(jnp.float32)
    stat_all = (stat_all[:, 0] + stat_all[:, 1]) + stat_all[:, 2]
    piece_log = stat_all[:, 0, :].reshape(-1)
    piece_delta = stat_all[:, 1, :].reshape(-1)
    grad_k, grad_v = attention_key_grad(
        rot_k,
        plain_v,
        gathered.reshape(seq_count * block_rows, 2 * HD),
        piece_log[None, :],
        piece_delta[None, :],
        tok_local,
        block_rows,
    )
    grad_queries = rotate(grad_q, cos_table, sin_table, -1.0).astype(jnp.bfloat16)[:, None, :]
    grad_keys = rotate(grad_k, cos_table, sin_table, -1.0).astype(jnp.bfloat16)[:, None, :]
    grad_values = grad_v.astype(jnp.bfloat16)[:, None, :]
    return (grad_queries, grad_keys, grad_values)


def solution(mesh):
    in_specs = (
        P(("dp", "seq"), "tm", None),
        P(("dp", "seq"), "tm", None),
        P(("dp", "seq"), "tm", None),
        P("seq"),
        P("tm", None, None),
        P(),
        P(),
        P("dp"),
        P(("dp", "tm"), "seq", None),
    )
    out_specs = (
        P(("dp", "seq"), "tm", None),
        P(("dp", "seq"), "tm", None),
        P(("dp", "seq"), "tm", None),
    )
    return jax.shard_map(
        on_device, mesh=mesh, in_specs=in_specs, out_specs=out_specs, check_vma=False
    )
```

```python
import functools
import math

import jax
import jax.numpy as jnp
from jax import lax
from jax.experimental import pallas as pl
from jax.experimental.pallas import tpu as pltpu
from jax.sharding import PartitionSpec as P

HD = 128
GRID_W = 32
SCALE = HD ** (-0.5)


def forward_kernel(key_block, q_ref, kv_ref, out_ref, lse_ref):
    q = q_ref[...]
    rows = q.shape[0]
    steps = kv_ref.shape[0] // key_block

    def body(step, carry):
        top, total, acc = carry
        start = pl.multiple_of(step * key_block, key_block)
        k = kv_ref[pl.ds(start, key_block), :HD]
        v = kv_ref[pl.ds(start, key_block), HD:]
        s = lax.dot_general(q, k, (((1,), (1,)), ((), ())), preferred_element_type=jnp.float32) * SCALE
        new_top = jnp.maximum(top, jnp.max(s, axis=1, keepdims=True))
        factor = jnp.exp(top - new_top)
        w = jnp.exp(s - new_top)
        total = total * factor + jnp.sum(w, axis=1, keepdims=True)
        acc = acc * factor + jnp.dot(w.astype(jnp.bfloat16), v, preferred_element_type=jnp.float32)
        return new_top, total, acc

    start_state = (
        jnp.full((rows, 1), -1e30, jnp.float32),
        jnp.zeros((rows, 1), jnp.float32),
        jnp.zeros((rows, HD), jnp.float32),
    )
    top, total, acc = lax.fori_loop(0, steps, body, start_state)
    out_ref[...] = (acc / total).astype(out_ref.dtype)
    lse_ref[...] = top + jnp.log(total)


def attention_forward(q, kv_all, query_block=256, key_block=512):
    rows = q.shape[0]
    keys = kv_all.shape[0]
    cost = pl.CostEstimate(
        flops=4 * rows * keys * HD, transcendentals=rows * keys, bytes_accessed=2 * HD * (2 * rows + 2 * keys)
    )
    return pl.pallas_call(
        functools.partial(forward_kernel, key_block),
        grid=(rows // query_block,),
        in_specs=[
            pl.BlockSpec((query_block, HD), lambda i: (i, 0)),
            pl.BlockSpec((keys, 2 * HD), lambda i: (0, 0)),
        ],
        out_specs=[
            pl.BlockSpec((query_block, HD), lambda i: (i, 0)),
            pl.BlockSpec((query_block, 1), lambda i: (i, 0)),
        ],
        out_shape=[
            jax.ShapeDtypeStruct((rows, HD), jnp.bfloat16),
            jax.ShapeDtypeStruct((rows, 1), jnp.float32),
        ],
        compiler_params=pltpu.CompilerParams(dimension_semantics=("arbitrary",)),
        cost_estimate=cost,
    )(q, kv_all)


def query_grad_kernel(key_block, q_ref, g_ref, lse_ref, delta_ref, kv_ref, dq_ref):
    q = q_ref[...]
    g = g_ref[...]
    lse = lse_ref[...]
    delta = delta_ref[...]
    steps = kv_ref.shape[0] // key_block

    def body(step, acc):
        start = pl.multiple_of(step * key_block, key_block)
        k = kv_ref[pl.ds(start, key_block), :HD]
        v = kv_ref[pl.ds(start, key_block), HD:]
        s = lax.dot_general(q, k, (((1,), (1,)), ((), ())), preferred_element_type=jnp.float32) * SCALE
        w = jnp.exp(s - lse)
        gw = lax.dot_general(g, v, (((1,), (1,)), ((), ())), preferred_element_type=jnp.float32)
        gs = (w * (gw - delta)).astype(jnp.bfloat16)
        return acc + jnp.dot(gs, k, preferred_element_type=jnp.float32)

    acc = lax.fori_loop(0, steps, body, jnp.zeros(dq_ref.shape, jnp.float32))
    dq_ref[...] = acc * SCALE


def attention_query_grad(q, g, lse_col, delta_col, kv_all, query_block=256, key_block=512):
    rows = q.shape[0]
    keys = kv_all.shape[0]
    cost = pl.CostEstimate(
        flops=6 * rows * keys * HD, transcendentals=rows * keys, bytes_accessed=2 * HD * (3 * rows + 2 * keys)
    )
    row_spec = pl.BlockSpec((query_block, HD), lambda i: (i, 0))
    col_spec = pl.BlockSpec((query_block, 1), lambda i: (i, 0))
    whole = pl.BlockSpec((keys, 2 * HD), lambda i: (0, 0))
    return pl.pallas_call(
        functools.partial(query_grad_kernel, key_block),
        grid=(rows // query_block,),
        in_specs=[row_spec, row_spec, col_spec, col_spec, whole],
        out_specs=pl.BlockSpec((query_block, HD), lambda i: (i, 0)),
        out_shape=jax.ShapeDtypeStruct((rows, HD), jnp.float32),
        compiler_params=pltpu.CompilerParams(dimension_semantics=("arbitrary",)),
        cost_estimate=cost,
    )(q, g, lse_col, delta_col, kv_all)


def key_grad_kernel(query_block, block_stride, k_ref, v_ref, qg_ref, lse_ref, delta_ref, dk_ref, dv_ref):
    k = k_ref[...]
    v = v_ref[...]
    steps = lse_ref.shape[1] // query_block

    def body(step, carry):
        dk, dv = carry
        start = pl.multiple_of(step * block_stride, 16)
        column = pl.multiple_of(step * query_block, query_block)
        q = qg_ref[pl.ds(start, query_block), :HD]
        g = qg_ref[pl.ds(start, query_block), HD:]
        lse = lse_ref[:, pl.ds(column, query_block)]
        delta = delta_ref[:, pl.ds(column, query_block)]
        s = lax.dot_general(k, q, (((1,), (1,)), ((), ())), preferred_element_type=jnp.float32) * SCALE
        w = jnp.exp(s - lse)
        gw = lax.dot_general(v, g, (((1,), (1,)), ((), ())), preferred_element_type=jnp.float32)
        gs = (w * (gw - delta)).astype(jnp.bfloat16)
        dk = dk + jnp.dot(gs, q, preferred_element_type=jnp.float32)
        dv = dv + jnp.dot(w.astype(jnp.bfloat16), g, preferred_element_type=jnp.float32)
        return dk, dv

    zero = jnp.zeros(dk_ref.shape, jnp.float32)
    dk, dv = lax.fori_loop(0, steps, body, (zero, zero))
    dk_ref[...] = dk * SCALE
    dv_ref[...] = dv


def attention_key_grad(k, v, qg_all, lse_row, delta_row, query_block, block_stride, key_rows=256):
    rows = k.shape[0]
    queries = lse_row.shape[1]
    cost = pl.CostEstimate(
        flops=8 * rows * queries * HD, transcendentals=rows * queries, bytes_accessed=2 * HD * (2 * rows + 2 * queries)
    )
    row_spec = pl.BlockSpec((key_rows, HD), lambda i: (i, 0))
    whole = pl.BlockSpec(qg_all.shape, lambda i: (0, 0))
    stat = pl.BlockSpec((1, queries), lambda i: (0, 0))
    return pl.pallas_call(
        functools.partial(key_grad_kernel, query_block, block_stride),
        grid=(rows // key_rows,),
        in_specs=[row_spec, row_spec, whole, stat, stat],
        out_specs=[row_spec, row_spec],
        out_shape=[jax.ShapeDtypeStruct((rows, HD), jnp.float32)] * 2,
        compiler_params=pltpu.CompilerParams(dimension_semantics=("arbitrary",)),
        cost_estimate=cost,
    )(k, v, qg_all, lse_row, delta_row)


def shifted(value, axis, steps):
    count = lax.axis_size(axis)
    initial, last = (max(0, -steps), min(count, count - steps))
    return lax.ppermute(value, axis, [(source, source + steps) for source in range(initial, last)])


def frequencies(pair_count):
    return 1.0 / 10000.0 ** (jnp.arange(pair_count, dtype=jnp.float32) / pair_count)


def rope_tables(frame_pos, cell_ids):
    pair_count = HD // 2
    part_side = pair_count // 3
    part_time = pair_count - 2 * part_side
    grid_row = (cell_ids // GRID_W).astype(jnp.float32)
    grid_col = (cell_ids % GRID_W).astype(jnp.float32)
    angles = jnp.concatenate(
        [
            frame_pos.astype(jnp.float32)[:, None] * frequencies(part_time)[None, :],
            grid_row[:, None] * frequencies(part_side)[None, :],
            grid_col[:, None] * frequencies(part_side)[None, :],
        ],
        axis=1,
    )
    return (jnp.cos(angles), jnp.sin(angles))


def rotate(vectors, cos_table, sin_table, direction):
    layout = vectors.shape
    paired = vectors.reshape(layout[:-1] + (layout[-1] // 2, 2))
    former = paired[..., 0]
    latter = paired[..., 1]
    out_former = former * cos_table - direction * latter * sin_table
    out_latter = direction * former * sin_table + latter * cos_table
    return jnp.stack([out_former, out_latter], axis=-1).reshape(layout)


def tap_mask(frame_clip):
    frame_total = frame_clip.shape[0]
    frame_ids = jnp.arange(frame_total, dtype=jnp.int32)
    columns = []
    for offset in range(3):
        target = frame_ids + offset
        inside = target < frame_total
        same_clip = frame_clip[jnp.minimum(target, frame_total - 1)] == frame_clip
        columns.append(jnp.logical_and(inside, same_clip).astype(jnp.float32))
    return jnp.stack(columns, axis=1)


def split_exact(values):
    high = lax.reduce_precision(values, exponent_bits=8, mantissa_bits=7)
    rest = values - high
    middle = lax.reduce_precision(rest, exponent_bits=8, mantissa_bits=7)
    low = rest - middle
    return jnp.stack([high, middle, low]).astype(jnp.bfloat16)


def cross(left, right):
    return lax.dot_general(
        left, right, (((1,), (1,)), ((), ())), preferred_element_type=jnp.float32
    )


def inner(left, right):
    return lax.dot_general(
        left, right, (((0,), (0,)), ((), ())), preferred_element_type=jnp.float32
    )


def on_device(
    queries, keys, values, token_cell, head_weight, norm_gain, time_weight, frame_clip, cotangent
):
    score_scale = HD ** (-0.5)
    tok_local = queries.shape[0]
    slab_cells = token_cell.shape[0]
    span_frames = cotangent.shape[0]
    channels = head_weight.shape[2]
    frame_pos = jnp.arange(tok_local, dtype=jnp.int32) // slab_cells
    cell_ids = jnp.tile(token_cell, tok_local // slab_cells)
    cos_table, sin_table = rope_tables(frame_pos, cell_ids)
    rot_q = rotate(queries[:, 0, :].astype(jnp.float32), cos_table, sin_table, 1.0).astype(
        jnp.bfloat16
    )
    rot_k = rotate(keys[:, 0, :].astype(jnp.float32), cos_table, sin_table, 1.0).astype(
        jnp.bfloat16
    )
    plain_v = values[:, 0, :]
    pair_all = lax.all_gather(jnp.concatenate([rot_k, plain_v], axis=1), "seq", axis=0, tiled=True)
    attended, log_col = attention_forward(rot_q, pair_all)
    log_total = log_col[:, 0]
    span_rows = span_frames * slab_cells
    head_count = lax.axis_size("tm")
    projected = jnp.dot(attended, head_weight[0], preferred_element_type=jnp.float32).astype(
        jnp.bfloat16
    )
    exchanged = lax.all_to_all(
        projected.reshape(head_count, span_frames * slab_cells, channels), "tm", 0, 0, tiled=False
    )
    mixed = jnp.sum(exchanged.astype(jnp.float32), axis=0).reshape(
        span_frames, slab_cells, channels
    )
    inverse = lax.rsqrt(jnp.mean(mixed * mixed, axis=2, keepdims=True) + 1e-06)
    normed = mixed * inverse * norm_gain
    mask_table = tap_mask(frame_clip)
    first_frame = lax.axis_index("tm") * span_frames
    local_mask = lax.dynamic_slice_in_dim(mask_table, first_frame, span_frames, 0)
    following = shifted(cotangent, "tm", -1)
    extended = jnp.concatenate([cotangent, following], axis=0)
    grad_act = jnp.zeros((span_frames, slab_cells, channels), jnp.float32)
    for offset in range(3):
        term = jnp.einsum(
            "fco,io->fci",
            extended[offset : offset + span_frames],
            time_weight[offset],
            preferred_element_type=jnp.float32,
        )
        grad_act = grad_act + local_mask[:, offset][:, None, None] * term
    sigmoid_n = jax.nn.sigmoid(normed)
    grad_normed = grad_act * sigmoid_n * (1.0 + normed * (1.0 - sigmoid_n))
    gained = grad_normed * norm_gain
    grad_mixed = (
        inverse * gained
        - inverse * inverse * inverse * mixed * jnp.mean(gained * mixed, axis=2, keepdims=True)
    ).astype(jnp.bfloat16)
    grad_mixed = grad_mixed.reshape(span_rows, channels)
    grad_out = cross(lax.all_gather(grad_mixed, "tm", axis=0, tiled=True), head_weight[0]).astype(
        jnp.bfloat16
    )
    row_delta = jnp.sum(grad_out.astype(jnp.float32) * attended.astype(jnp.float32), axis=1)

    grad_q = attention_query_grad(rot_q, grad_out, log_col, row_delta[:, None], pair_all)
    stat_rows = split_exact(jnp.stack([log_total, row_delta]))
    stat_rows = stat_rows.reshape(-1, 2 * HD)
    stat_pad = (-stat_rows.shape[0]) % 16
    stat_rows = jnp.pad(stat_rows, ((0, stat_pad), (0, 0)))
    packed = jnp.concatenate([jnp.concatenate([rot_q, grad_out], axis=1), stat_rows], axis=0)
    block_rows = packed.shape[0]
    seq_count = lax.axis_size("seq")
    gathered = lax.all_gather(packed, "seq", axis=0, tiled=True).reshape(
        seq_count, block_rows, 2 * HD
    )
    stat_all = gathered[:, tok_local:, :].reshape(seq_count, -1)[:, : 6 * tok_local]
    stat_all = stat_all.reshape(seq_count, 3, 2, tok_local).astype(jnp.float32)
    stat_all = (stat_all[:, 0] + stat_all[:, 1]) + stat_all[:, 2]
    piece_log = stat_all[:, 0, :].reshape(-1)
    piece_delta = stat_all[:, 1, :].reshape(-1)
    grad_k, grad_v = attention_key_grad(
        rot_k,
        plain_v,
        gathered.reshape(seq_count * block_rows, 2 * HD),
        piece_log[None, :],
        piece_delta[None, :],
        tok_local,
        block_rows,
    )
    grad_queries = rotate(grad_q, cos_table, sin_table, -1.0).astype(jnp.bfloat16)[:, None, :]
    grad_keys = rotate(grad_k, cos_table, sin_table, -1.0).astype(jnp.bfloat16)[:, None, :]
    grad_values = grad_v.astype(jnp.bfloat16)[:, None, :]
    return (grad_queries, grad_keys, grad_values)


def solution(mesh):
    in_specs = (
        P(("dp", "seq"), "tm", None),
        P(("dp", "seq"), "tm", None),
        P(("dp", "seq"), "tm", None),
        P("seq"),
        P("tm", None, None),
        P(),
        P(),
        P("dp"),
        P(("dp", "tm"), "seq", None),
    )
    out_specs = (
        P(("dp", "seq"), "tm", None),
        P(("dp", "seq"), "tm", None),
        P(("dp", "seq"), "tm", None),
    )
    return jax.shard_map(
        on_device, mesh=mesh, in_specs=in_specs, out_specs=out_specs, check_vma=False
    )
```

```python
import functools
import math

import jax
import jax.numpy as jnp
from jax import lax
from jax.experimental import pallas as pl
from jax.experimental.pallas import tpu as pltpu
from jax.sharding import PartitionSpec as P

HD = 128
GRID_W = 32
SCALE = HD ** (-0.5)


def forward_kernel(key_block, q_ref, kv_ref, out_ref, lse_ref):
    q = q_ref[...]
    rows = q.shape[0]
    steps = kv_ref.shape[0] // key_block

    def body(step, carry):
        top, total, acc = carry
        start = pl.multiple_of(step * key_block, key_block)
        k = kv_ref[pl.ds(start, key_block), :HD]
        v = kv_ref[pl.ds(start, key_block), HD:]
        s = lax.dot_general(q, k, (((1,), (1,)), ((), ())), preferred_element_type=jnp.float32) * SCALE
        new_top = jnp.maximum(top, jnp.max(s, axis=1, keepdims=True))
        factor = jnp.exp(top - new_top)
        w = jnp.exp(s - new_top)
        total = total * factor + jnp.sum(w, axis=1, keepdims=True)
        acc = acc * factor + jnp.dot(w.astype(jnp.bfloat16), v, preferred_element_type=jnp.float32)
        return new_top, total, acc

    start_state = (
        jnp.full((rows, 1), -1e30, jnp.float32),
        jnp.zeros((rows, 1), jnp.float32),
        jnp.zeros((rows, HD), jnp.float32),
    )
    top, total, acc = lax.fori_loop(0, steps, body, start_state, unroll=2)
    out_ref[...] = (acc / total).astype(out_ref.dtype)
    lse_ref[...] = top + jnp.log(total)


def attention_forward(q, kv_all, query_block=512, key_block=2048):
    rows = q.shape[0]
    keys = kv_all.shape[0]
    cost = pl.CostEstimate(
        flops=4 * rows * keys * HD, transcendentals=rows * keys, bytes_accessed=2 * HD * (2 * rows + 2 * keys)
    )
    return pl.pallas_call(
        functools.partial(forward_kernel, key_block),
        grid=(rows // query_block,),
        in_specs=[
            pl.BlockSpec((query_block, HD), lambda i: (i, 0)),
            pl.BlockSpec((keys, 2 * HD), lambda i: (0, 0)),
        ],
        out_specs=[
            pl.BlockSpec((query_block, HD), lambda i: (i, 0)),
            pl.BlockSpec((query_block, 1), lambda i: (i, 0)),
        ],
        out_shape=[
            jax.ShapeDtypeStruct((rows, HD), jnp.bfloat16),
            jax.ShapeDtypeStruct((rows, 1), jnp.float32),
        ],
        compiler_params=pltpu.CompilerParams(dimension_semantics=("arbitrary",)),
        cost_estimate=cost,
    )(q, kv_all)


def query_grad_kernel(key_block, q_ref, g_ref, lse_ref, delta_ref, kv_ref, dq_ref):
    q = q_ref[...]
    g = g_ref[...]
    lse = lse_ref[...]
    delta = delta_ref[...]
    steps = kv_ref.shape[0] // key_block

    def body(step, acc):
        start = pl.multiple_of(step * key_block, key_block)
        k = kv_ref[pl.ds(start, key_block), :HD]
        v = kv_ref[pl.ds(start, key_block), HD:]
        s = lax.dot_general(q, k, (((1,), (1,)), ((), ())), preferred_element_type=jnp.float32) * SCALE
        w = jnp.exp(s - lse)
        gw = lax.dot_general(g, v, (((1,), (1,)), ((), ())), preferred_element_type=jnp.float32)
        gs = (w * (gw - delta)).astype(jnp.bfloat16)
        return acc + jnp.dot(gs, k, preferred_element_type=jnp.float32)

    acc = lax.fori_loop(0, steps, body, jnp.zeros(dq_ref.shape, jnp.float32), unroll=2)
    dq_ref[...] = acc * SCALE


def attention_query_grad(q, g, lse_col, delta_col, kv_all, query_block=512, key_block=1024):
    rows = q.shape[0]
    keys = kv_all.shape[0]
    cost = pl.CostEstimate(
        flops=6 * rows * keys * HD, transcendentals=rows * keys, bytes_accessed=2 * HD * (3 * rows + 2 * keys)
    )
    row_spec = pl.BlockSpec((query_block, HD), lambda i: (i, 0))
    col_spec = pl.BlockSpec((query_block, 1), lambda i: (i, 0))
    whole = pl.BlockSpec((keys, 2 * HD), lambda i: (0, 0))
    return pl.pallas_call(
        functools.partial(query_grad_kernel, key_block),
        grid=(rows // query_block,),
        in_specs=[row_spec, row_spec, col_spec, col_spec, whole],
        out_specs=pl.BlockSpec((query_block, HD), lambda i: (i, 0)),
        out_shape=jax.ShapeDtypeStruct((rows, HD), jnp.float32),
        compiler_params=pltpu.CompilerParams(dimension_semantics=("arbitrary",)),
        cost_estimate=cost,
    )(q, g, lse_col, delta_col, kv_all)


def key_grad_kernel(query_block, block_stride, k_ref, v_ref, qg_ref, lse_ref, delta_ref, dk_ref, dv_ref):
    k = k_ref[...]
    v = v_ref[...]
    steps = lse_ref.shape[1] // query_block

    def body(step, carry):
        dk, dv = carry
        start = pl.multiple_of(step * block_stride, 16)
        column = pl.multiple_of(step * query_block, query_block)
        q = qg_ref[pl.ds(start, query_block), :HD]
        g = qg_ref[pl.ds(start, query_block), HD:]
        lse = lse_ref[:, pl.ds(column, query_block)]
        delta = delta_ref[:, pl.ds(column, query_block)]
        s = lax.dot_general(k, q, (((1,), (1,)), ((), ())), preferred_element_type=jnp.float32) * SCALE
        w = jnp.exp(s - lse)
        gw = lax.dot_general(v, g, (((1,), (1,)), ((), ())), preferred_element_type=jnp.float32)
        gs = (w * (gw - delta)).astype(jnp.bfloat16)
        dk = dk + jnp.dot(gs, q, preferred_element_type=jnp.float32)
        dv = dv + jnp.dot(w.astype(jnp.bfloat16), g, preferred_element_type=jnp.float32)
        return dk, dv

    zero = jnp.zeros(dk_ref.shape, jnp.float32)
    dk, dv = lax.fori_loop(0, steps, body, (zero, zero), unroll=2)
    dk_ref[...] = dk * SCALE
    dv_ref[...] = dv


def attention_key_grad(k, v, qg_all, lse_row, delta_row, query_block, block_stride, key_rows=512):
    rows = k.shape[0]
    queries = lse_row.shape[1]
    cost = pl.CostEstimate(
        flops=8 * rows * queries * HD, transcendentals=rows * queries, bytes_accessed=2 * HD * (2 * rows + 2 * queries)
    )
    row_spec = pl.BlockSpec((key_rows, HD), lambda i: (i, 0))
    whole = pl.BlockSpec(qg_all.shape, lambda i: (0, 0))
    stat = pl.BlockSpec((1, queries), lambda i: (0, 0))
    return pl.pallas_call(
        functools.partial(key_grad_kernel, query_block, block_stride),
        grid=(rows // key_rows,),
        in_specs=[row_spec, row_spec, whole, stat, stat],
        out_specs=[row_spec, row_spec],
        out_shape=[jax.ShapeDtypeStruct((rows, HD), jnp.float32)] * 2,
        compiler_params=pltpu.CompilerParams(dimension_semantics=("arbitrary",)),
        cost_estimate=cost,
    )(k, v, qg_all, lse_row, delta_row)


def shifted(value, axis, steps):
    count = lax.axis_size(axis)
    initial, last = (max(0, -steps), min(count, count - steps))
    return lax.ppermute(value, axis, [(source, source + steps) for source in range(initial, last)])


def frequencies(pair_count):
    return 1.0 / 10000.0 ** (jnp.arange(pair_count, dtype=jnp.float32) / pair_count)


def rope_tables(frame_pos, cell_ids):
    pair_count = HD // 2
    part_side = pair_count // 3
    part_time = pair_count - 2 * part_side
    grid_row = (cell_ids // GRID_W).astype(jnp.float32)
    grid_col = (cell_ids % GRID_W).astype(jnp.float32)
    angles = jnp.concatenate(
        [
            frame_pos.astype(jnp.float32)[:, None] * frequencies(part_time)[None, :],
            grid_row[:, None] * frequencies(part_side)[None, :],
            grid_col[:, None] * frequencies(part_side)[None, :],
        ],
        axis=1,
    )
    return (jnp.cos(angles), jnp.sin(angles))


def rotate(vectors, cos_table, sin_table, direction):
    layout = vectors.shape
    paired = vectors.reshape(layout[:-1] + (layout[-1] // 2, 2))
    former = paired[..., 0]
    latter = paired[..., 1]
    out_former = former * cos_table - direction * latter * sin_table
    out_latter = direction * former * sin_table + latter * cos_table
    return jnp.stack([out_former, out_latter], axis=-1).reshape(layout)


def tap_mask(frame_clip):
    frame_total = frame_clip.shape[0]
    frame_ids = jnp.arange(frame_total, dtype=jnp.int32)
    columns = []
    for offset in range(3):
        target = frame_ids + offset
        inside = target < frame_total
        same_clip = frame_clip[jnp.minimum(target, frame_total - 1)] == frame_clip
        columns.append(jnp.logical_and(inside, same_clip).astype(jnp.float32))
    return jnp.stack(columns, axis=1)


def split_exact(values):
    high = lax.reduce_precision(values, exponent_bits=8, mantissa_bits=7)
    rest = values - high
    middle = lax.reduce_precision(rest, exponent_bits=8, mantissa_bits=7)
    low = rest - middle
    return jnp.stack([high, middle, low]).astype(jnp.bfloat16)


def cross(left, right):
    return lax.dot_general(
        left, right, (((1,), (1,)), ((), ())), preferred_element_type=jnp.float32
    )


def inner(left, right):
    return lax.dot_general(
        left, right, (((0,), (0,)), ((), ())), preferred_element_type=jnp.float32
    )


def on_device(
    queries, keys, values, token_cell, head_weight, norm_gain, time_weight, frame_clip, cotangent
):
    score_scale = HD ** (-0.5)
    tok_local = queries.shape[0]
    slab_cells = token_cell.shape[0]
    span_frames = cotangent.shape[0]
    channels = head_weight.shape[2]
    frame_pos = jnp.arange(tok_local, dtype=jnp.int32) // slab_cells
    cell_ids = jnp.tile(token_cell, tok_local // slab_cells)
    cos_table, sin_table = rope_tables(frame_pos, cell_ids)
    rot_q = rotate(queries[:, 0, :].astype(jnp.float32), cos_table, sin_table, 1.0).astype(
        jnp.bfloat16
    )
    rot_k = rotate(keys[:, 0, :].astype(jnp.float32), cos_table, sin_table, 1.0).astype(
        jnp.bfloat16
    )
    plain_v = values[:, 0, :]
    pair_all = lax.all_gather(jnp.concatenate([rot_k, plain_v], axis=1), "seq", axis=0, tiled=True)
    attended, log_col = attention_forward(rot_q, pair_all)
    log_total = log_col[:, 0]
    span_rows = span_frames * slab_cells
    head_count = lax.axis_size("tm")
    projected = jnp.dot(attended, head_weight[0], preferred_element_type=jnp.float32).astype(
        jnp.bfloat16
    )
    exchanged = lax.all_to_all(
        projected.reshape(head_count, span_frames * slab_cells, channels), "tm", 0, 0, tiled=False
    )
    mixed = jnp.sum(exchanged.astype(jnp.float32), axis=0).reshape(
        span_frames, slab_cells, channels
    )
    inverse = lax.rsqrt(jnp.mean(mixed * mixed, axis=2, keepdims=True) + 1e-06)
    normed = mixed * inverse * norm_gain
    mask_table = tap_mask(frame_clip)
    first_frame = lax.axis_index("tm") * span_frames
    local_mask = lax.dynamic_slice_in_dim(mask_table, first_frame, span_frames, 0)
    following = shifted(cotangent, "tm", -1)
    extended = jnp.concatenate([cotangent, following], axis=0)
    grad_act = jnp.zeros((span_frames, slab_cells, channels), jnp.float32)
    for offset in range(3):
        term = jnp.einsum(
            "fco,io->fci",
            extended[offset : offset + span_frames],
            time_weight[offset],
            preferred_element_type=jnp.float32,
        )
        grad_act = grad_act + local_mask[:, offset][:, None, None] * term
    sigmoid_n = jax.nn.sigmoid(normed)
    grad_normed = grad_act * sigmoid_n * (1.0 + normed * (1.0 - sigmoid_n))
    gained = grad_normed * norm_gain
    grad_mixed = (
        inverse * gained
        - inverse * inverse * inverse * mixed * jnp.mean(gained * mixed, axis=2, keepdims=True)
    ).astype(jnp.bfloat16)
    grad_mixed = grad_mixed.reshape(span_rows, channels)
    grad_out = cross(lax.all_gather(grad_mixed, "tm", axis=0, tiled=True), head_weight[0]).astype(
        jnp.bfloat16
    )
    row_delta = jnp.sum(grad_out.astype(jnp.float32) * attended.astype(jnp.float32), axis=1)

    grad_q = attention_query_grad(rot_q, grad_out, log_col, row_delta[:, None], pair_all)
    stat_rows = split_exact(jnp.stack([log_total, row_delta]))
    stat_rows = stat_rows.reshape(-1, 2 * HD)
    stat_pad = (-stat_rows.shape[0]) % 16
    stat_rows = jnp.pad(stat_rows, ((0, stat_pad), (0, 0)))
    packed = jnp.concatenate([jnp.concatenate([rot_q, grad_out], axis=1), stat_rows], axis=0)
    block_rows = packed.shape[0]
    seq_count = lax.axis_size("seq")
    gathered = lax.all_gather(packed, "seq", axis=0, tiled=True).reshape(
        seq_count, block_rows, 2 * HD
    )
    stat_all = gathered[:, tok_local:, :].reshape(seq_count, -1)[:, : 6 * tok_local]
    stat_all = stat_all.reshape(seq_count, 3, 2, tok_local).astype(jnp.float32)
    stat_all = (stat_all[:, 0] + stat_all[:, 1]) + stat_all[:, 2]
    piece_log = stat_all[:, 0, :].reshape(-1)
    piece_delta = stat_all[:, 1, :].reshape(-1)
    grad_k, grad_v = attention_key_grad(
        rot_k,
        plain_v,
        gathered.reshape(seq_count * block_rows, 2 * HD),
        piece_log[None, :],
        piece_delta[None, :],
        tok_local,
        block_rows,
    )
    grad_queries = rotate(grad_q, cos_table, sin_table, -1.0).astype(jnp.bfloat16)[:, None, :]
    grad_keys = rotate(grad_k, cos_table, sin_table, -1.0).astype(jnp.bfloat16)[:, None, :]
    grad_values = grad_v.astype(jnp.bfloat16)[:, None, :]
    return (grad_queries, grad_keys, grad_values)


def solution(mesh):
    in_specs = (
        P(("dp", "seq"), "tm", None),
        P(("dp", "seq"), "tm", None),
        P(("dp", "seq"), "tm", None),
        P("seq"),
        P("tm", None, None),
        P(),
        P(),
        P("dp"),
        P(("dp", "tm"), "seq", None),
    )
    out_specs = (
        P(("dp", "seq"), "tm", None),
        P(("dp", "seq"), "tm", None),
        P(("dp", "seq"), "tm", None),
    )
    return jax.shard_map(
        on_device, mesh=mesh, in_specs=in_specs, out_specs=out_specs, check_vma=False
    )
```

```python
import functools
import math

import jax
import jax.numpy as jnp
from jax import lax
from jax.experimental import pallas as pl
from jax.experimental.pallas import tpu as pltpu
from jax.sharding import PartitionSpec as P

HD = 128
GRID_W = 32
SCALE = HD ** (-0.5)
LOG2E = 1.4426950408889634
LN2 = 0.6931471805599453


def forward_kernel(key_block, q_ref, kv_ref, out_ref, lse_ref):
    q = q_ref[...]
    rows = q.shape[0]
    steps = kv_ref.shape[0] // key_block

    def body(step, carry):
        top, total, acc = carry
        start = pl.multiple_of(step * key_block, key_block)
        k = kv_ref[pl.ds(start, key_block), :HD]
        v = kv_ref[pl.ds(start, key_block), HD:]
        s = lax.dot_general(q, k, (((1,), (1,)), ((), ())), preferred_element_type=jnp.float32) * (SCALE * LOG2E)
        new_top = jnp.maximum(top, jnp.max(s, axis=1, keepdims=True))
        factor = jnp.exp2(top - new_top)
        w = jnp.exp2(s - new_top)
        total = total * factor + jnp.sum(w, axis=1, keepdims=True)
        acc = acc * factor + jnp.dot(w.astype(jnp.bfloat16), v, preferred_element_type=jnp.float32)
        return new_top, total, acc

    start_state = (
        jnp.full((rows, 1), -1e30, jnp.float32),
        jnp.zeros((rows, 1), jnp.float32),
        jnp.zeros((rows, HD), jnp.float32),
    )
    top, total, acc = lax.fori_loop(0, steps, body, start_state, unroll=4)
    out_ref[...] = (acc / total).astype(out_ref.dtype)
    lse_ref[...] = top * LN2 + jnp.log(total)


def attention_forward(q, kv_all, query_block=512, key_block=2048):
    rows = q.shape[0]
    keys = kv_all.shape[0]
    cost = pl.CostEstimate(
        flops=4 * rows * keys * HD, transcendentals=rows * keys, bytes_accessed=2 * HD * (2 * rows + 2 * keys)
    )
    return pl.pallas_call(
        functools.partial(forward_kernel, key_block),
        grid=(rows // query_block,),
        in_specs=[
            pl.BlockSpec((query_block, HD), lambda i: (i, 0)),
            pl.BlockSpec((keys, 2 * HD), lambda i: (0, 0)),
        ],
        out_specs=[
            pl.BlockSpec((query_block, HD), lambda i: (i, 0)),
            pl.BlockSpec((query_block, 1), lambda i: (i, 0)),
        ],
        out_shape=[
            jax.ShapeDtypeStruct((rows, HD), jnp.bfloat16),
            jax.ShapeDtypeStruct((rows, 1), jnp.float32),
        ],
        compiler_params=pltpu.CompilerParams(dimension_semantics=("arbitrary",)),
        cost_estimate=cost,
    )(q, kv_all)


def query_grad_kernel(key_block, q_ref, g_ref, lse_ref, delta_ref, kv_ref, dq_ref):
    q = q_ref[...]
    g = g_ref[...]
    lse = lse_ref[...] * LOG2E
    delta = delta_ref[...]
    steps = kv_ref.shape[0] // key_block

    def body(step, acc):
        start = pl.multiple_of(step * key_block, key_block)
        k = kv_ref[pl.ds(start, key_block), :HD]
        v = kv_ref[pl.ds(start, key_block), HD:]
        s = lax.dot_general(q, k, (((1,), (1,)), ((), ())), preferred_element_type=jnp.float32) * (SCALE * LOG2E)
        w = jnp.exp2(s - lse)
        gw = lax.dot_general(g, v, (((1,), (1,)), ((), ())), preferred_element_type=jnp.float32)
        gs = (w * (gw - delta)).astype(jnp.bfloat16)
        return acc + jnp.dot(gs, k, preferred_element_type=jnp.float32)

    acc = lax.fori_loop(0, steps, body, jnp.zeros(dq_ref.shape, jnp.float32), unroll=4)
    dq_ref[...] = acc * SCALE


def attention_query_grad(q, g, lse_col, delta_col, kv_all, query_block=512, key_block=1024):
    rows = q.shape[0]
    keys = kv_all.shape[0]
    cost = pl.CostEstimate(
        flops=6 * rows * keys * HD, transcendentals=rows * keys, bytes_accessed=2 * HD * (3 * rows + 2 * keys)
    )
    row_spec = pl.BlockSpec((query_block, HD), lambda i: (i, 0))
    col_spec = pl.BlockSpec((query_block, 1), lambda i: (i, 0))
    whole = pl.BlockSpec((keys, 2 * HD), lambda i: (0, 0))
    return pl.pallas_call(
        functools.partial(query_grad_kernel, key_block),
        grid=(rows // query_block,),
        in_specs=[row_spec, row_spec, col_spec, col_spec, whole],
        out_specs=pl.BlockSpec((query_block, HD), lambda i: (i, 0)),
        out_shape=jax.ShapeDtypeStruct((rows, HD), jnp.float32),
        compiler_params=pltpu.CompilerParams(dimension_semantics=("arbitrary",)),
        cost_estimate=cost,
    )(q, g, lse_col, delta_col, kv_all)


def key_grad_kernel(query_block, block_stride, k_ref, v_ref, qg_ref, lse_ref, delta_ref, dk_ref, dv_ref):
    k = k_ref[...]
    v = v_ref[...]
    steps = lse_ref.shape[1] // query_block

    def body(step, carry):
        dk, dv = carry
        start = pl.multiple_of(step * block_stride, 16)
        column = pl.multiple_of(step * query_block, query_block)
        q = qg_ref[pl.ds(start, query_block), :HD]
        g = qg_ref[pl.ds(start, query_block), HD:]
        lse = lse_ref[:, pl.ds(column, query_block)]
        delta = delta_ref[:, pl.ds(column, query_block)]
        s = lax.dot_general(k, q, (((1,), (1,)), ((), ())), preferred_element_type=jnp.float32) * (SCALE * LOG2E)
        w = jnp.exp2(s - lse * LOG2E)
        gw = lax.dot_general(v, g, (((1,), (1,)), ((), ())), preferred_element_type=jnp.float32)
        gs = (w * (gw - delta)).astype(jnp.bfloat16)
        dk = dk + jnp.dot(gs, q, preferred_element_type=jnp.float32)
        dv = dv + jnp.dot(w.astype(jnp.bfloat16), g, preferred_element_type=jnp.float32)
        return dk, dv

    zero = jnp.zeros(dk_ref.shape, jnp.float32)
    dk, dv = lax.fori_loop(0, steps, body, (zero, zero), unroll=4)
    dk_ref[...] = dk * SCALE
    dv_ref[...] = dv


def attention_key_grad(k, v, qg_all, lse_row, delta_row, query_block, block_stride, key_rows=512):
    rows = k.shape[0]
    queries = lse_row.shape[1]
    cost = pl.CostEstimate(
        flops=8 * rows * queries * HD, transcendentals=rows * queries, bytes_accessed=2 * HD * (2 * rows + 2 * queries)
    )
    row_spec = pl.BlockSpec((key_rows, HD), lambda i: (i, 0))
    whole = pl.BlockSpec(qg_all.shape, lambda i: (0, 0))
    stat = pl.BlockSpec((1, queries), lambda i: (0, 0))
    return pl.pallas_call(
        functools.partial(key_grad_kernel, query_block, block_stride),
        grid=(rows // key_rows,),
        in_specs=[row_spec, row_spec, whole, stat, stat],
        out_specs=[row_spec, row_spec],
        out_shape=[jax.ShapeDtypeStruct((rows, HD), jnp.float32)] * 2,
        compiler_params=pltpu.CompilerParams(dimension_semantics=("arbitrary",)),
        cost_estimate=cost,
    )(k, v, qg_all, lse_row, delta_row)


def shifted(value, axis, steps):
    count = lax.axis_size(axis)
    initial, last = (max(0, -steps), min(count, count - steps))
    return lax.ppermute(value, axis, [(source, source + steps) for source in range(initial, last)])


def frequencies(pair_count):
    return 1.0 / 10000.0 ** (jnp.arange(pair_count, dtype=jnp.float32) / pair_count)


def rope_tables(frame_pos, cell_ids):
    pair_count = HD // 2
    part_side = pair_count // 3
    part_time = pair_count - 2 * part_side
    grid_row = (cell_ids // GRID_W).astype(jnp.float32)
    grid_col = (cell_ids % GRID_W).astype(jnp.float32)
    angles = jnp.concatenate(
        [
            frame_pos.astype(jnp.float32)[:, None] * frequencies(part_time)[None, :],
            grid_row[:, None] * frequencies(part_side)[None, :],
            grid_col[:, None] * frequencies(part_side)[None, :],
        ],
        axis=1,
    )
    return (jnp.cos(angles), jnp.sin(angles))


def rotate(vectors, cos_table, sin_table, direction):
    layout = vectors.shape
    paired = vectors.reshape(layout[:-1] + (layout[-1] // 2, 2))
    former = paired[..., 0]
    latter = paired[..., 1]
    out_former = former * cos_table - direction * latter * sin_table
    out_latter = direction * former * sin_table + latter * cos_table
    return jnp.stack([out_former, out_latter], axis=-1).reshape(layout)


def tap_mask(frame_clip):
    frame_total = frame_clip.shape[0]
    frame_ids = jnp.arange(frame_total, dtype=jnp.int32)
    columns = []
    for offset in range(3):
        target = frame_ids + offset
        inside = target < frame_total
        same_clip = frame_clip[jnp.minimum(target, frame_total - 1)] == frame_clip
        columns.append(jnp.logical_and(inside, same_clip).astype(jnp.float32))
    return jnp.stack(columns, axis=1)


def split_exact(values):
    high = lax.reduce_precision(values, exponent_bits=8, mantissa_bits=7)
    rest = values - high
    middle = lax.reduce_precision(rest, exponent_bits=8, mantissa_bits=7)
    low = rest - middle
    return jnp.stack([high, middle, low]).astype(jnp.bfloat16)


def cross(left, right):
    return lax.dot_general(
        left, right, (((1,), (1,)), ((), ())), preferred_element_type=jnp.float32
    )


def inner(left, right):
    return lax.dot_general(
        left, right, (((0,), (0,)), ((), ())), preferred_element_type=jnp.float32
    )


def on_device(
    queries, keys, values, token_cell, head_weight, norm_gain, time_weight, frame_clip, cotangent
):
    score_scale = HD ** (-0.5)
    tok_local = queries.shape[0]
    slab_cells = token_cell.shape[0]
    span_frames = cotangent.shape[0]
    channels = head_weight.shape[2]
    frame_pos = jnp.arange(tok_local, dtype=jnp.int32) // slab_cells
    cell_ids = jnp.tile(token_cell, tok_local // slab_cells)
    cos_table, sin_table = rope_tables(frame_pos, cell_ids)
    rot_q = rotate(queries[:, 0, :].astype(jnp.float32), cos_table, sin_table, 1.0).astype(
        jnp.bfloat16
    )
    rot_k = rotate(keys[:, 0, :].astype(jnp.float32), cos_table, sin_table, 1.0).astype(
        jnp.bfloat16
    )
    plain_v = values[:, 0, :]
    pair_all = lax.all_gather(jnp.concatenate([rot_k, plain_v], axis=1), "seq", axis=0, tiled=True)
    attended, log_col = attention_forward(rot_q, pair_all)
    log_total = log_col[:, 0]
    span_rows = span_frames * slab_cells
    head_count = lax.axis_size("tm")
    projected = jnp.dot(attended, head_weight[0], preferred_element_type=jnp.float32).astype(
        jnp.bfloat16
    )
    exchanged = lax.all_to_all(
        projected.reshape(head_count, span_frames * slab_cells, channels), "tm", 0, 0, tiled=False
    )
    mixed = jnp.sum(exchanged.astype(jnp.float32), axis=0).reshape(
        span_frames, slab_cells, channels
    )
    inverse = lax.rsqrt(jnp.mean(mixed * mixed, axis=2, keepdims=True) + 1e-06)
    normed = mixed * inverse * norm_gain
    mask_table = tap_mask(frame_clip)
    first_frame = lax.axis_index("tm") * span_frames
    local_mask = lax.dynamic_slice_in_dim(mask_table, first_frame, span_frames, 0)
    following = shifted(cotangent, "tm", -1)
    extended = jnp.concatenate([cotangent, following], axis=0)
    grad_act = jnp.zeros((span_frames, slab_cells, channels), jnp.float32)
    for offset in range(3):
        term = jnp.einsum(
            "fco,io->fci",
            extended[offset : offset + span_frames],
            time_weight[offset],
            preferred_element_type=jnp.float32,
        )
        grad_act = grad_act + local_mask[:, offset][:, None, None] * term
    sigmoid_n = jax.nn.sigmoid(normed)
    grad_normed = grad_act * sigmoid_n * (1.0 + normed * (1.0 - sigmoid_n))
    gained = grad_normed * norm_gain
    grad_mixed = (
        inverse * gained
        - inverse * inverse * inverse * mixed * jnp.mean(gained * mixed, axis=2, keepdims=True)
    ).astype(jnp.bfloat16)
    grad_mixed = grad_mixed.reshape(span_rows, channels)
    grad_out = cross(lax.all_gather(grad_mixed, "tm", axis=0, tiled=True), head_weight[0]).astype(
        jnp.bfloat16
    )
    row_delta = jnp.sum(grad_out.astype(jnp.float32) * attended.astype(jnp.float32), axis=1)

    grad_q = attention_query_grad(rot_q, grad_out, log_col, row_delta[:, None], pair_all)
    stat_rows = split_exact(jnp.stack([log_total, row_delta]))
    stat_rows = stat_rows.reshape(-1, 2 * HD)
    stat_pad = (-stat_rows.shape[0]) % 16
    stat_rows = jnp.pad(stat_rows, ((0, stat_pad), (0, 0)))
    packed = jnp.concatenate([jnp.concatenate([rot_q, grad_out], axis=1), stat_rows], axis=0)
    block_rows = packed.shape[0]
    seq_count = lax.axis_size("seq")
    gathered = lax.all_gather(packed, "seq", axis=0, tiled=True).reshape(
        seq_count, block_rows, 2 * HD
    )
    stat_all = gathered[:, tok_local:, :].reshape(seq_count, -1)[:, : 6 * tok_local]
    stat_all = stat_all.reshape(seq_count, 3, 2, tok_local).astype(jnp.float32)
    stat_all = (stat_all[:, 0] + stat_all[:, 1]) + stat_all[:, 2]
    piece_log = stat_all[:, 0, :].reshape(-1)
    piece_delta = stat_all[:, 1, :].reshape(-1)
    grad_k, grad_v = attention_key_grad(
        rot_k,
        plain_v,
        gathered.reshape(seq_count * block_rows, 2 * HD),
        piece_log[None, :],
        piece_delta[None, :],
        tok_local,
        block_rows,
    )
    grad_queries = rotate(grad_q, cos_table, sin_table, -1.0).astype(jnp.bfloat16)[:, None, :]
    grad_keys = rotate(grad_k, cos_table, sin_table, -1.0).astype(jnp.bfloat16)[:, None, :]
    grad_values = grad_v.astype(jnp.bfloat16)[:, None, :]
    return (grad_queries, grad_keys, grad_values)


def solution(mesh):
    in_specs = (
        P(("dp", "seq"), "tm", None),
        P(("dp", "seq"), "tm", None),
        P(("dp", "seq"), "tm", None),
        P("seq"),
        P("tm", None, None),
        P(),
        P(),
        P("dp"),
        P(("dp", "tm"), "seq", None),
    )
    out_specs = (
        P(("dp", "seq"), "tm", None),
        P(("dp", "seq"), "tm", None),
        P(("dp", "seq"), "tm", None),
    )
    return jax.shard_map(
        on_device, mesh=mesh, in_specs=in_specs, out_specs=out_specs, check_vma=False
    )
```

```python
import functools
import math

import jax
import jax.numpy as jnp
from jax import lax
from jax.experimental import pallas as pl
from jax.experimental.pallas import tpu as pltpu
from jax.sharding import PartitionSpec as P

HD = 128
GRID_W = 32
SCALE = HD ** (-0.5)
LOG2E = 1.4426950408889634
LN2 = 0.6931471805599453


def rotate_back_rows(x, cos_ref, sin_ref):
    lanes = lax.broadcasted_iota(jnp.int32, x.shape, 1)
    ahead = pltpu.roll(x, x.shape[1] - 1, 1)
    behind = pltpu.roll(x, 1, 1)
    ahead_lane = pltpu.roll(lanes, x.shape[1] - 1, 1)
    partner_lane = jnp.where(lanes % 2 == 0, lanes + 1, lanes - 1)
    partner = jnp.where(ahead_lane == partner_lane, ahead, behind)
    return x * cos_ref[...] + partner * sin_ref[...]


def forward_kernel(key_block, q_ref, kv_ref, out_ref, lse_ref):
    q = q_ref[...]
    rows = q.shape[0]
    steps = kv_ref.shape[0] // key_block

    def body(step, carry):
        top, total, acc = carry
        start = pl.multiple_of(step * key_block, key_block)
        k = kv_ref[pl.ds(start, key_block), :HD]
        v = kv_ref[pl.ds(start, key_block), HD:]
        s = lax.dot_general(q, k, (((1,), (1,)), ((), ())), preferred_element_type=jnp.float32) * (SCALE * LOG2E)
        new_top = jnp.maximum(top, jnp.max(s, axis=1, keepdims=True))
        factor = jnp.exp2(top - new_top)
        w = jnp.exp2(s - new_top)
        total = total * factor + jnp.sum(w, axis=1, keepdims=True)
        acc = acc * factor + jnp.dot(w.astype(jnp.bfloat16), v, preferred_element_type=jnp.float32)
        return new_top, total, acc

    start_state = (
        jnp.full((rows, 1), -1e30, jnp.float32),
        jnp.zeros((rows, 1), jnp.float32),
        jnp.zeros((rows, HD), jnp.float32),
    )
    top, total, acc = lax.fori_loop(0, steps, body, start_state, unroll=4)
    out_ref[...] = (acc / total).astype(out_ref.dtype)
    lse_ref[...] = top * LN2 + jnp.log(total)


def attention_forward(q, kv_all, query_block=512, key_block=2048):
    rows = q.shape[0]
    keys = kv_all.shape[0]
    cost = pl.CostEstimate(
        flops=4 * rows * keys * HD, transcendentals=rows * keys, bytes_accessed=2 * HD * (2 * rows + 2 * keys)
    )
    return pl.pallas_call(
        functools.partial(forward_kernel, key_block),
        grid=(rows // query_block,),
        in_specs=[
            pl.BlockSpec((query_block, HD), lambda i: (i, 0)),
            pl.BlockSpec((keys, 2 * HD), lambda i: (0, 0)),
        ],
        out_specs=[
            pl.BlockSpec((query_block, HD), lambda i: (i, 0)),
            pl.BlockSpec((query_block, 1), lambda i: (i, 0)),
        ],
        out_shape=[
            jax.ShapeDtypeStruct((rows, HD), jnp.bfloat16),
            jax.ShapeDtypeStruct((rows, 1), jnp.float32),
        ],
        compiler_params=pltpu.CompilerParams(dimension_semantics=("arbitrary",)),
        cost_estimate=cost,
    )(q, kv_all)


def query_grad_kernel(key_block, q_ref, g_ref, lse_ref, delta_ref, kv_ref, cos_ref, sin_ref, dq_ref):
    q = q_ref[...]
    g = g_ref[...]
    lse = lse_ref[...] * LOG2E
    delta = delta_ref[...]
    steps = kv_ref.shape[0] // key_block

    def body(step, acc):
        start = pl.multiple_of(step * key_block, key_block)
        k = kv_ref[pl.ds(start, key_block), :HD]
        v = kv_ref[pl.ds(start, key_block), HD:]
        s = lax.dot_general(q, k, (((1,), (1,)), ((), ())), preferred_element_type=jnp.float32) * (SCALE * LOG2E)
        w = jnp.exp2(s - lse)
        gw = lax.dot_general(g, v, (((1,), (1,)), ((), ())), preferred_element_type=jnp.float32)
        gs = (w * (gw - delta)).astype(jnp.bfloat16)
        return acc + jnp.dot(gs, k, preferred_element_type=jnp.float32)

    acc = lax.fori_loop(0, steps, body, jnp.zeros(dq_ref.shape, jnp.float32), unroll=4)
    dq_ref[...] = rotate_back_rows(acc * SCALE, cos_ref, sin_ref).astype(dq_ref.dtype)


def attention_query_grad(q, g, lse_col, delta_col, kv_all, cos_wide, sin_wide, query_block=512, key_block=1024):
    rows = q.shape[0]
    keys = kv_all.shape[0]
    cost = pl.CostEstimate(
        flops=6 * rows * keys * HD, transcendentals=rows * keys, bytes_accessed=2 * HD * (3 * rows + 2 * keys)
    )
    row_spec = pl.BlockSpec((query_block, HD), lambda i: (i, 0))
    col_spec = pl.BlockSpec((query_block, 1), lambda i: (i, 0))
    whole = pl.BlockSpec((keys, 2 * HD), lambda i: (0, 0))
    return pl.pallas_call(
        functools.partial(query_grad_kernel, key_block),
        grid=(rows // query_block,),
        in_specs=[row_spec, row_spec, col_spec, col_spec, whole, row_spec, row_spec],
        out_specs=pl.BlockSpec((query_block, HD), lambda i: (i, 0)),
        out_shape=jax.ShapeDtypeStruct((rows, HD), jnp.bfloat16),
        compiler_params=pltpu.CompilerParams(dimension_semantics=("arbitrary",)),
        cost_estimate=cost,
    )(q, g, lse_col, delta_col, kv_all, cos_wide, sin_wide)


def key_grad_kernel(query_block, block_stride, k_ref, v_ref, qg_ref, lse_ref, delta_ref, cos_ref, sin_ref, dk_ref, dv_ref):
    k = k_ref[...]
    v = v_ref[...]
    steps = lse_ref.shape[1] // query_block

    def body(step, carry):
        dk, dv = carry
        start = pl.multiple_of(step * block_stride, 16)
        column = pl.multiple_of(step * query_block, query_block)
        q = qg_ref[pl.ds(start, query_block), :HD]
        g = qg_ref[pl.ds(start, query_block), HD:]
        lse = lse_ref[:, pl.ds(column, query_block)]
        delta = delta_ref[:, pl.ds(column, query_block)]
        s = lax.dot_general(k, q, (((1,), (1,)), ((), ())), preferred_element_type=jnp.float32) * (SCALE * LOG2E)
        w = jnp.exp2(s - lse * LOG2E)
        gw = lax.dot_general(v, g, (((1,), (1,)), ((), ())), preferred_element_type=jnp.float32)
        gs = (w * (gw - delta)).astype(jnp.bfloat16)
        dk = dk + jnp.dot(gs, q, preferred_element_type=jnp.float32)
        dv = dv + jnp.dot(w.astype(jnp.bfloat16), g, preferred_element_type=jnp.float32)
        return dk, dv

    zero = jnp.zeros(dk_ref.shape, jnp.float32)
    dk, dv = lax.fori_loop(0, steps, body, (zero, zero), unroll=4)
    dk_ref[...] = rotate_back_rows(dk * SCALE, cos_ref, sin_ref).astype(dk_ref.dtype)
    dv_ref[...] = dv.astype(dv_ref.dtype)


def attention_key_grad(k, v, qg_all, lse_row, delta_row, cos_wide, sin_wide, query_block, block_stride, key_rows=512):
    rows = k.shape[0]
    queries = lse_row.shape[1]
    cost = pl.CostEstimate(
        flops=8 * rows * queries * HD, transcendentals=rows * queries, bytes_accessed=2 * HD * (2 * rows + 2 * queries)
    )
    row_spec = pl.BlockSpec((key_rows, HD), lambda i: (i, 0))
    whole = pl.BlockSpec(qg_all.shape, lambda i: (0, 0))
    stat = pl.BlockSpec((1, queries), lambda i: (0, 0))
    return pl.pallas_call(
        functools.partial(key_grad_kernel, query_block, block_stride),
        grid=(rows // key_rows,),
        in_specs=[row_spec, row_spec, whole, stat, stat, row_spec, row_spec],
        out_specs=[row_spec, row_spec],
        out_shape=[jax.ShapeDtypeStruct((rows, HD), jnp.bfloat16)] * 2,
        compiler_params=pltpu.CompilerParams(dimension_semantics=("arbitrary",)),
        cost_estimate=cost,
    )(k, v, qg_all, lse_row, delta_row, cos_wide, sin_wide)


def shifted(value, axis, steps):
    count = lax.axis_size(axis)
    initial, last = (max(0, -steps), min(count, count - steps))
    return lax.ppermute(value, axis, [(source, source + steps) for source in range(initial, last)])


def frequencies(pair_count):
    return 1.0 / 10000.0 ** (jnp.arange(pair_count, dtype=jnp.float32) / pair_count)


def rope_tables(frame_pos, cell_ids):
    pair_count = HD // 2
    part_side = pair_count // 3
    part_time = pair_count - 2 * part_side
    grid_row = (cell_ids // GRID_W).astype(jnp.float32)
    grid_col = (cell_ids % GRID_W).astype(jnp.float32)
    angles = jnp.concatenate(
        [
            frame_pos.astype(jnp.float32)[:, None] * frequencies(part_time)[None, :],
            grid_row[:, None] * frequencies(part_side)[None, :],
            grid_col[:, None] * frequencies(part_side)[None, :],
        ],
        axis=1,
    )
    return (jnp.cos(angles), jnp.sin(angles))


def rotate(vectors, cos_table, sin_table, direction):
    layout = vectors.shape
    paired = vectors.reshape(layout[:-1] + (layout[-1] // 2, 2))
    former = paired[..., 0]
    latter = paired[..., 1]
    out_former = former * cos_table - direction * latter * sin_table
    out_latter = direction * former * sin_table + latter * cos_table
    return jnp.stack([out_former, out_latter], axis=-1).reshape(layout)


def tap_mask(frame_clip):
    frame_total = frame_clip.shape[0]
    frame_ids = jnp.arange(frame_total, dtype=jnp.int32)
    columns = []
    for offset in range(3):
        target = frame_ids + offset
        inside = target < frame_total
        same_clip = frame_clip[jnp.minimum(target, frame_total - 1)] == frame_clip
        columns.append(jnp.logical_and(inside, same_clip).astype(jnp.float32))
    return jnp.stack(columns, axis=1)


def split_exact(values):
    high = lax.reduce_precision(values, exponent_bits=8, mantissa_bits=7)
    rest = values - high
    middle = lax.reduce_precision(rest, exponent_bits=8, mantissa_bits=7)
    low = rest - middle
    return jnp.stack([high, middle, low]).astype(jnp.bfloat16)


def cross(left, right):
    return lax.dot_general(
        left, right, (((1,), (1,)), ((), ())), preferred_element_type=jnp.float32
    )


def inner(left, right):
    return lax.dot_general(
        left, right, (((0,), (0,)), ((), ())), preferred_element_type=jnp.float32
    )


def on_device(
    queries, keys, values, token_cell, head_weight, norm_gain, time_weight, frame_clip, cotangent
):
    score_scale = HD ** (-0.5)
    tok_local = queries.shape[0]
    slab_cells = token_cell.shape[0]
    span_frames = cotangent.shape[0]
    channels = head_weight.shape[2]
    frame_pos = jnp.arange(tok_local, dtype=jnp.int32) // slab_cells
    cell_ids = jnp.tile(token_cell, tok_local // slab_cells)
    cos_table, sin_table = rope_tables(frame_pos, cell_ids)
    rot_q = rotate(queries[:, 0, :].astype(jnp.float32), cos_table, sin_table, 1.0).astype(
        jnp.bfloat16
    )
    rot_k = rotate(keys[:, 0, :].astype(jnp.float32), cos_table, sin_table, 1.0).astype(
        jnp.bfloat16
    )
    plain_v = values[:, 0, :]
    pair_all = lax.all_gather(jnp.concatenate([rot_k, plain_v], axis=1), "seq", axis=0, tiled=True)
    attended, log_col = attention_forward(rot_q, pair_all)
    log_total = log_col[:, 0]
    span_rows = span_frames * slab_cells
    head_count = lax.axis_size("tm")
    projected = jnp.dot(attended, head_weight[0], preferred_element_type=jnp.float32).astype(
        jnp.bfloat16
    )
    exchanged = lax.all_to_all(
        projected.reshape(head_count, span_frames * slab_cells, channels), "tm", 0, 0, tiled=False
    )
    mixed = jnp.sum(exchanged.astype(jnp.float32), axis=0).reshape(
        span_frames, slab_cells, channels
    )
    inverse = lax.rsqrt(jnp.mean(mixed * mixed, axis=2, keepdims=True) + 1e-06)
    normed = mixed * inverse * norm_gain
    mask_table = tap_mask(frame_clip)
    first_frame = lax.axis_index("tm") * span_frames
    local_mask = lax.dynamic_slice_in_dim(mask_table, first_frame, span_frames, 0)
    following = shifted(cotangent, "tm", -1)
    extended = jnp.concatenate([cotangent, following], axis=0)
    grad_act = jnp.zeros((span_frames, slab_cells, channels), jnp.float32)
    for offset in range(3):
        term = jnp.einsum(
            "fco,io->fci",
            extended[offset : offset + span_frames],
            time_weight[offset],
            preferred_element_type=jnp.float32,
        )
        grad_act = grad_act + local_mask[:, offset][:, None, None] * term
    sigmoid_n = jax.nn.sigmoid(normed)
    grad_normed = grad_act * sigmoid_n * (1.0 + normed * (1.0 - sigmoid_n))
    gained = grad_normed * norm_gain
    grad_mixed = (
        inverse * gained
        - inverse * inverse * inverse * mixed * jnp.mean(gained * mixed, axis=2, keepdims=True)
    ).astype(jnp.bfloat16)
    grad_mixed = grad_mixed.reshape(span_rows, channels)
    grad_out = cross(lax.all_gather(grad_mixed, "tm", axis=0, tiled=True), head_weight[0]).astype(
        jnp.bfloat16
    )
    row_delta = jnp.sum(grad_out.astype(jnp.float32) * attended.astype(jnp.float32), axis=1)

    cos_wide = jnp.stack([cos_table, cos_table], axis=-1).reshape(tok_local, HD)
    sin_wide = jnp.stack([sin_table, -sin_table], axis=-1).reshape(tok_local, HD)
    grad_q = attention_query_grad(
        rot_q, grad_out, log_col, row_delta[:, None], pair_all, cos_wide, sin_wide
    )
    stat_rows = split_exact(jnp.stack([log_total, row_delta]))
    stat_rows = stat_rows.reshape(-1, 2 * HD)
    stat_pad = (-stat_rows.shape[0]) % 16
    stat_rows = jnp.pad(stat_rows, ((0, stat_pad), (0, 0)))
    packed = jnp.concatenate([jnp.concatenate([rot_q, grad_out], axis=1), stat_rows], axis=0)
    block_rows = packed.shape[0]
    seq_count = lax.axis_size("seq")
    gathered = lax.all_gather(packed, "seq", axis=0, tiled=True).reshape(
        seq_count, block_rows, 2 * HD
    )
    stat_all = gathered[:, tok_local:, :].reshape(seq_count, -1)[:, : 6 * tok_local]
    stat_all = stat_all.reshape(seq_count, 3, 2, tok_local).astype(jnp.float32)
    stat_all = (stat_all[:, 0] + stat_all[:, 1]) + stat_all[:, 2]
    piece_log = stat_all[:, 0, :].reshape(-1)
    piece_delta = stat_all[:, 1, :].reshape(-1)
    grad_k, grad_v = attention_key_grad(
        rot_k,
        plain_v,
        gathered.reshape(seq_count * block_rows, 2 * HD),
        piece_log[None, :],
        piece_delta[None, :],
        cos_wide,
        sin_wide,
        tok_local,
        block_rows,
    )
    grad_queries = grad_q[:, None, :]
    grad_keys = grad_k[:, None, :]
    grad_values = grad_v[:, None, :]
    return (grad_queries, grad_keys, grad_values)


def solution(mesh):
    in_specs = (
        P(("dp", "seq"), "tm", None),
        P(("dp", "seq"), "tm", None),
        P(("dp", "seq"), "tm", None),
        P("seq"),
        P("tm", None, None),
        P(),
        P(),
        P("dp"),
        P(("dp", "tm"), "seq", None),
    )
    out_specs = (
        P(("dp", "seq"), "tm", None),
        P(("dp", "seq"), "tm", None),
        P(("dp", "seq"), "tm", None),
    )
    return jax.shard_map(
        on_device, mesh=mesh, in_specs=in_specs, out_specs=out_specs, check_vma=False
    )
```

```python
import functools
import math

import jax
import jax.numpy as jnp
from jax import lax
from jax.experimental import pallas as pl
from jax.experimental.pallas import tpu as pltpu
from jax.sharding import PartitionSpec as P

HD = 128
GRID_W = 32
SCALE = HD ** (-0.5)
LOG2E = 1.4426950408889634
LN2 = 0.6931471805599453


def rotate_back_rows(x, cos_ref, sin_ref):
    lanes = lax.broadcasted_iota(jnp.int32, x.shape, 1)
    ahead = pltpu.roll(x, x.shape[1] - 1, 1)
    behind = pltpu.roll(x, 1, 1)
    ahead_lane = pltpu.roll(lanes, x.shape[1] - 1, 1)
    partner_lane = jnp.where(lanes % 2 == 0, lanes + 1, lanes - 1)
    partner = jnp.where(ahead_lane == partner_lane, ahead, behind)
    return x * cos_ref[...] + partner * sin_ref[...]


def prepare_kernel(q_ref, k_ref, v_ref, cos_ref, sin_ref, rq_ref, kv_ref):
    rq_ref[...] = rotate_back_rows(q_ref[...].astype(jnp.float32), cos_ref, sin_ref).astype(
        rq_ref.dtype
    )
    kv_ref[:, :HD] = rotate_back_rows(k_ref[...].astype(jnp.float32), cos_ref, sin_ref).astype(
        kv_ref.dtype
    )
    kv_ref[:, HD:] = v_ref[...]


def prepare(q, k, v, cos_wide, sin_forward):
    rows = q.shape[0]
    return pl.pallas_call(
        prepare_kernel,
        out_shape=[
            jax.ShapeDtypeStruct((rows, HD), jnp.bfloat16),
            jax.ShapeDtypeStruct((rows, 2 * HD), jnp.bfloat16),
        ],
        cost_estimate=pl.CostEstimate(flops=8 * rows * HD, transcendentals=0, bytes_accessed=14 * rows * HD),
    )(q, k, v, cos_wide, sin_forward)


def forward_kernel(key_block, q_ref, kv_ref, out_ref, lse_ref):
    q = q_ref[...]
    rows = q.shape[0]
    steps = kv_ref.shape[0] // key_block

    def body(step, carry):
        top, total, acc = carry
        start = pl.multiple_of(step * key_block, key_block)
        k = kv_ref[pl.ds(start, key_block), :HD]
        v = kv_ref[pl.ds(start, key_block), HD:]
        s = lax.dot_general(q, k, (((1,), (1,)), ((), ())), preferred_element_type=jnp.float32) * (SCALE * LOG2E)
        new_top = jnp.maximum(top, jnp.max(s, axis=1, keepdims=True))
        factor = jnp.exp2(top - new_top)
        w = jnp.exp2(s - new_top)
        total = total * factor + jnp.sum(w, axis=1, keepdims=True)
        acc = acc * factor + jnp.dot(w.astype(jnp.bfloat16), v, preferred_element_type=jnp.float32)
        return new_top, total, acc

    start_state = (
        jnp.full((rows, 1), -1e30, jnp.float32),
        jnp.zeros((rows, 1), jnp.float32),
        jnp.zeros((rows, HD), jnp.float32),
    )
    top, total, acc = lax.fori_loop(0, steps, body, start_state, unroll=4)
    out_ref[...] = (acc / total).astype(out_ref.dtype)
    lse_ref[...] = top * LN2 + jnp.log(total)


def attention_forward(q, kv_all, query_block=512, key_block=2048):
    rows = q.shape[0]
    keys = kv_all.shape[0]
    cost = pl.CostEstimate(
        flops=4 * rows * keys * HD, transcendentals=rows * keys, bytes_accessed=2 * HD * (2 * rows + 2 * keys)
    )
    return pl.pallas_call(
        functools.partial(forward_kernel, key_block),
        grid=(rows // query_block,),
        in_specs=[
            pl.BlockSpec((query_block, HD), lambda i: (i, 0)),
            pl.BlockSpec((keys, 2 * HD), lambda i: (0, 0)),
        ],
        out_specs=[
            pl.BlockSpec((query_block, HD), lambda i: (i, 0)),
            pl.BlockSpec((query_block, 1), lambda i: (i, 0)),
        ],
        out_shape=[
            jax.ShapeDtypeStruct((rows, HD), jnp.bfloat16),
            jax.ShapeDtypeStruct((rows, 1), jnp.float32),
        ],
        compiler_params=pltpu.CompilerParams(dimension_semantics=("arbitrary",)),
        cost_estimate=cost,
    )(q, kv_all)


def query_grad_kernel(key_block, q_ref, g_ref, lse_ref, delta_ref, kv_ref, cos_ref, sin_ref, dq_ref):
    q = q_ref[...]
    g = g_ref[...]
    lse = lse_ref[...] * LOG2E
    delta = delta_ref[...]
    steps = kv_ref.shape[0] // key_block

    def body(step, acc):
        start = pl.multiple_of(step * key_block, key_block)
        k = kv_ref[pl.ds(start, key_block), :HD]
        v = kv_ref[pl.ds(start, key_block), HD:]
        s = lax.dot_general(q, k, (((1,), (1,)), ((), ())), preferred_element_type=jnp.float32) * (SCALE * LOG2E)
        w = jnp.exp2(s - lse)
        gw = lax.dot_general(g, v, (((1,), (1,)), ((), ())), preferred_element_type=jnp.float32)
        gs = (w * (gw - delta)).astype(jnp.bfloat16)
        return acc + jnp.dot(gs, k, preferred_element_type=jnp.float32)

    acc = lax.fori_loop(0, steps, body, jnp.zeros(dq_ref.shape, jnp.float32), unroll=4)
    dq_ref[...] = rotate_back_rows(acc * SCALE, cos_ref, sin_ref).astype(dq_ref.dtype)


def attention_query_grad(q, g, lse_col, delta_col, kv_all, cos_wide, sin_wide, query_block=512, key_block=1024):
    rows = q.shape[0]
    keys = kv_all.shape[0]
    cost = pl.CostEstimate(
        flops=6 * rows * keys * HD, transcendentals=rows * keys, bytes_accessed=2 * HD * (3 * rows + 2 * keys)
    )
    row_spec = pl.BlockSpec((query_block, HD), lambda i: (i, 0))
    col_spec = pl.BlockSpec((query_block, 1), lambda i: (i, 0))
    whole = pl.BlockSpec((keys, 2 * HD), lambda i: (0, 0))
    return pl.pallas_call(
        functools.partial(query_grad_kernel, key_block),
        grid=(rows // query_block,),
        in_specs=[row_spec, row_spec, col_spec, col_spec, whole, row_spec, row_spec],
        out_specs=pl.BlockSpec((query_block, HD), lambda i: (i, 0)),
        out_shape=jax.ShapeDtypeStruct((rows, HD), jnp.bfloat16),
        compiler_params=pltpu.CompilerParams(dimension_semantics=("arbitrary",)),
        cost_estimate=cost,
    )(q, g, lse_col, delta_col, kv_all, cos_wide, sin_wide)


def key_grad_kernel(query_block, block_stride, k_ref, v_ref, qg_ref, lse_ref, delta_ref, cos_ref, sin_ref, dk_ref, dv_ref):
    k = k_ref[...]
    v = v_ref[...]
    steps = lse_ref.shape[1] // query_block

    def body(step, carry):
        dk, dv = carry
        start = pl.multiple_of(step * block_stride, 16)
        column = pl.multiple_of(step * query_block, query_block)
        q = qg_ref[pl.ds(start, query_block), :HD]
        g = qg_ref[pl.ds(start, query_block), HD:]
        lse = lse_ref[:, pl.ds(column, query_block)]
        delta = delta_ref[:, pl.ds(column, query_block)]
        s = lax.dot_general(k, q, (((1,), (1,)), ((), ())), preferred_element_type=jnp.float32) * (SCALE * LOG2E)
        w = jnp.exp2(s - lse * LOG2E)
        gw = lax.dot_general(v, g, (((1,), (1,)), ((), ())), preferred_element_type=jnp.float32)
        gs = (w * (gw - delta)).astype(jnp.bfloat16)
        dk = dk + jnp.dot(gs, q, preferred_element_type=jnp.float32)
        dv = dv + jnp.dot(w.astype(jnp.bfloat16), g, preferred_element_type=jnp.float32)
        return dk, dv

    zero = jnp.zeros(dk_ref.shape, jnp.float32)
    dk, dv = lax.fori_loop(0, steps, body, (zero, zero), unroll=4)
    dk_ref[...] = rotate_back_rows(dk * SCALE, cos_ref, sin_ref).astype(dk_ref.dtype)
    dv_ref[...] = dv.astype(dv_ref.dtype)


def attention_key_grad(k, v, qg_all, lse_row, delta_row, cos_wide, sin_wide, query_block, block_stride, key_rows=512):
    rows = k.shape[0]
    queries = lse_row.shape[1]
    cost = pl.CostEstimate(
        flops=8 * rows * queries * HD, transcendentals=rows * queries, bytes_accessed=2 * HD * (2 * rows + 2 * queries)
    )
    row_spec = pl.BlockSpec((key_rows, HD), lambda i: (i, 0))
    whole = pl.BlockSpec(qg_all.shape, lambda i: (0, 0))
    stat = pl.BlockSpec((1, queries), lambda i: (0, 0))
    return pl.pallas_call(
        functools.partial(key_grad_kernel, query_block, block_stride),
        grid=(rows // key_rows,),
        in_specs=[row_spec, row_spec, whole, stat, stat, row_spec, row_spec],
        out_specs=[row_spec, row_spec],
        out_shape=[jax.ShapeDtypeStruct((rows, HD), jnp.bfloat16)] * 2,
        compiler_params=pltpu.CompilerParams(dimension_semantics=("arbitrary",)),
        cost_estimate=cost,
    )(k, v, qg_all, lse_row, delta_row, cos_wide, sin_wide)


def shifted(value, axis, steps):
    count = lax.axis_size(axis)
    initial, last = (max(0, -steps), min(count, count - steps))
    return lax.ppermute(value, axis, [(source, source + steps) for source in range(initial, last)])


def frequencies(pair_count):
    return 1.0 / 10000.0 ** (jnp.arange(pair_count, dtype=jnp.float32) / pair_count)


def rope_tables(frame_pos, cell_ids):
    pair_count = HD // 2
    part_side = pair_count // 3
    part_time = pair_count - 2 * part_side
    grid_row = (cell_ids // GRID_W).astype(jnp.float32)
    grid_col = (cell_ids % GRID_W).astype(jnp.float32)
    angles = jnp.concatenate(
        [
            frame_pos.astype(jnp.float32)[:, None] * frequencies(part_time)[None, :],
            grid_row[:, None] * frequencies(part_side)[None, :],
            grid_col[:, None] * frequencies(part_side)[None, :],
        ],
        axis=1,
    )
    return (jnp.cos(angles), jnp.sin(angles))


def wide_tables(frame_pos, cell_ids):
    pair_count = HD // 2
    part_side = pair_count // 3
    part_time = pair_count - 2 * part_side
    freq = jnp.repeat(
        jnp.concatenate(
            [frequencies(part_time), frequencies(part_side), frequencies(part_side)]
        ),
        2,
    )
    pair = jnp.arange(HD, dtype=jnp.int32)[None, :] // 2
    grid_row = (cell_ids // GRID_W).astype(jnp.float32)[:, None]
    grid_col = (cell_ids % GRID_W).astype(jnp.float32)[:, None]
    position = jnp.where(
        pair < part_time,
        frame_pos.astype(jnp.float32)[:, None],
        jnp.where(pair < part_time + part_side, grid_row, grid_col),
    )
    angles = position * freq[None, :]
    even = jnp.arange(HD, dtype=jnp.int32)[None, :] % 2 == 0
    sin_angles = jnp.sin(angles)
    return (jnp.cos(angles), jnp.where(even, sin_angles, -sin_angles))


def rotate(vectors, cos_table, sin_table, direction):
    layout = vectors.shape
    paired = vectors.reshape(layout[:-1] + (layout[-1] // 2, 2))
    former = paired[..., 0]
    latter = paired[..., 1]
    out_former = former * cos_table - direction * latter * sin_table
    out_latter = direction * former * sin_table + latter * cos_table
    return jnp.stack([out_former, out_latter], axis=-1).reshape(layout)


def tap_mask(frame_clip):
    frame_total = frame_clip.shape[0]
    frame_ids = jnp.arange(frame_total, dtype=jnp.int32)
    columns = []
    for offset in range(3):
        target = frame_ids + offset
        inside = target < frame_total
        same_clip = frame_clip[jnp.minimum(target, frame_total - 1)] == frame_clip
        columns.append(jnp.logical_and(inside, same_clip).astype(jnp.float32))
    return jnp.stack(columns, axis=1)


def split_exact(values):
    high = lax.reduce_precision(values, exponent_bits=8, mantissa_bits=7)
    rest = values - high
    middle = lax.reduce_precision(rest, exponent_bits=8, mantissa_bits=7)
    low = rest - middle
    return jnp.stack([high, middle, low]).astype(jnp.bfloat16)


def cross(left, right):
    return lax.dot_general(
        left, right, (((1,), (1,)), ((), ())), preferred_element_type=jnp.float32
    )


def inner(left, right):
    return lax.dot_general(
        left, right, (((0,), (0,)), ((), ())), preferred_element_type=jnp.float32
    )


def on_device(
    queries, keys, values, token_cell, head_weight, norm_gain, time_weight, frame_clip, cotangent
):
    score_scale = HD ** (-0.5)
    tok_local = queries.shape[0]
    slab_cells = token_cell.shape[0]
    span_frames = cotangent.shape[0]
    channels = head_weight.shape[2]
    frame_pos = jnp.arange(tok_local, dtype=jnp.int32) // slab_cells
    cell_ids = jnp.tile(token_cell, tok_local // slab_cells)
    cos_wide, sin_wide = wide_tables(frame_pos, cell_ids)
    rot_q, pair = prepare(queries[:, 0, :], keys[:, 0, :], values[:, 0, :], cos_wide, -sin_wide)
    pair_all = lax.all_gather(pair, "seq", axis=0, tiled=True)
    rot_k = pair[:, :HD]
    plain_v = values[:, 0, :]
    attended, log_col = attention_forward(rot_q, pair_all)
    log_total = log_col[:, 0]
    span_rows = span_frames * slab_cells
    head_count = lax.axis_size("tm")
    projected = jnp.dot(attended, head_weight[0], preferred_element_type=jnp.float32).astype(
        jnp.bfloat16
    )
    exchanged = lax.all_to_all(
        projected.reshape(head_count, span_frames * slab_cells, channels), "tm", 0, 0, tiled=False
    )
    mixed = jnp.sum(exchanged.astype(jnp.float32), axis=0).reshape(
        span_frames, slab_cells, channels
    )
    inverse = lax.rsqrt(jnp.mean(mixed * mixed, axis=2, keepdims=True) + 1e-06)
    normed = mixed * inverse * norm_gain
    mask_table = tap_mask(frame_clip)
    first_frame = lax.axis_index("tm") * span_frames
    local_mask = lax.dynamic_slice_in_dim(mask_table, first_frame, span_frames, 0)
    following = shifted(cotangent, "tm", -1)
    extended = jnp.concatenate([cotangent, following], axis=0)
    grad_act = jnp.zeros((span_frames, slab_cells, channels), jnp.float32)
    for offset in range(3):
        term = jnp.einsum(
            "fco,io->fci",
            extended[offset : offset + span_frames],
            time_weight[offset],
            preferred_element_type=jnp.float32,
        )
        grad_act = grad_act + local_mask[:, offset][:, None, None] * term
    sigmoid_n = jax.nn.sigmoid(normed)
    grad_normed = grad_act * sigmoid_n * (1.0 + normed * (1.0 - sigmoid_n))
    gained = grad_normed * norm_gain
    grad_mixed = (
        inverse * gained
        - inverse * inverse * inverse * mixed * jnp.mean(gained * mixed, axis=2, keepdims=True)
    ).astype(jnp.bfloat16)
    grad_mixed = grad_mixed.reshape(span_rows, channels)
    grad_out = cross(lax.all_gather(grad_mixed, "tm", axis=0, tiled=True), head_weight[0]).astype(
        jnp.bfloat16
    )
    row_delta = jnp.sum(grad_out.astype(jnp.float32) * attended.astype(jnp.float32), axis=1)

    grad_q = attention_query_grad(
        rot_q, grad_out, log_col, row_delta[:, None], pair_all, cos_wide, sin_wide
    )
    stat_rows = split_exact(jnp.stack([log_total, row_delta]))
    stat_rows = stat_rows.reshape(-1, 2 * HD)
    stat_pad = (-stat_rows.shape[0]) % 16
    stat_rows = jnp.pad(stat_rows, ((0, stat_pad), (0, 0)))
    packed = jnp.concatenate([jnp.concatenate([rot_q, grad_out], axis=1), stat_rows], axis=0)
    block_rows = packed.shape[0]
    seq_count = lax.axis_size("seq")
    gathered = lax.all_gather(packed, "seq", axis=0, tiled=True).reshape(
        seq_count, block_rows, 2 * HD
    )
    stat_all = gathered[:, tok_local:, :].reshape(seq_count, -1)[:, : 6 * tok_local]
    stat_all = stat_all.reshape(seq_count, 3, 2, tok_local).astype(jnp.float32)
    stat_all = (stat_all[:, 0] + stat_all[:, 1]) + stat_all[:, 2]
    piece_log = stat_all[:, 0, :].reshape(-1)
    piece_delta = stat_all[:, 1, :].reshape(-1)
    grad_k, grad_v = attention_key_grad(
        rot_k,
        plain_v,
        gathered.reshape(seq_count * block_rows, 2 * HD),
        piece_log[None, :],
        piece_delta[None, :],
        cos_wide,
        sin_wide,
        tok_local,
        block_rows,
    )
    grad_queries = grad_q[:, None, :]
    grad_keys = grad_k[:, None, :]
    grad_values = grad_v[:, None, :]
    return (grad_queries, grad_keys, grad_values)


def solution(mesh):
    in_specs = (
        P(("dp", "seq"), "tm", None),
        P(("dp", "seq"), "tm", None),
        P(("dp", "seq"), "tm", None),
        P("seq"),
        P("tm", None, None),
        P(),
        P(),
        P("dp"),
        P(("dp", "tm"), "seq", None),
    )
    out_specs = (
        P(("dp", "seq"), "tm", None),
        P(("dp", "seq"), "tm", None),
        P(("dp", "seq"), "tm", None),
    )
    return jax.shard_map(
        on_device, mesh=mesh, in_specs=in_specs, out_specs=out_specs, check_vma=False
    )
```

```python
import functools
import math

import jax
import jax.numpy as jnp
from jax import lax
from jax.experimental import pallas as pl
from jax.experimental.pallas import tpu as pltpu
from jax.sharding import PartitionSpec as P

HD = 128
GRID_W = 32
SCALE = HD ** (-0.5)
LOG2E = 1.4426950408889634
LN2 = 0.6931471805599453


def rotate_back_rows(x, cos_ref, sin_ref):
    lanes = lax.broadcasted_iota(jnp.int32, x.shape, 1)
    ahead = pltpu.roll(x, x.shape[1] - 1, 1)
    behind = pltpu.roll(x, 1, 1)
    ahead_lane = pltpu.roll(lanes, x.shape[1] - 1, 1)
    partner_lane = jnp.where(lanes % 2 == 0, lanes + 1, lanes - 1)
    partner = jnp.where(ahead_lane == partner_lane, ahead, behind)
    return x * cos_ref[...] + partner * sin_ref[...]


def prepare_kernel(q_ref, k_ref, v_ref, cos_ref, sin_ref, rq_ref, kv_ref):
    rq_ref[...] = rotate_back_rows(q_ref[...].astype(jnp.float32), cos_ref, sin_ref).astype(
        rq_ref.dtype
    )
    kv_ref[:, :HD] = rotate_back_rows(k_ref[...].astype(jnp.float32), cos_ref, sin_ref).astype(
        kv_ref.dtype
    )
    kv_ref[:, HD:] = v_ref[...]


def prepare(q, k, v, cos_wide, sin_forward):
    rows = q.shape[0]
    return pl.pallas_call(
        prepare_kernel,
        out_shape=[
            jax.ShapeDtypeStruct((rows, HD), jnp.bfloat16),
            jax.ShapeDtypeStruct((rows, 2 * HD), jnp.bfloat16),
        ],
        cost_estimate=pl.CostEstimate(flops=8 * rows * HD, transcendentals=0, bytes_accessed=14 * rows * HD),
    )(q, k, v, cos_wide, sin_forward)


def forward_kernel(key_block, q_ref, kv_ref, out_ref, lse_ref):
    q = q_ref[...]
    rows = q.shape[0]
    steps = kv_ref.shape[0] // key_block

    def body(step, carry):
        top, total, acc = carry
        start = pl.multiple_of(step * key_block, key_block)
        k = kv_ref[pl.ds(start, key_block), :HD]
        v = kv_ref[pl.ds(start, key_block), HD:]
        s = lax.dot_general(q, k, (((1,), (1,)), ((), ())), preferred_element_type=jnp.float32) * (SCALE * LOG2E)
        new_top = jnp.maximum(top, jnp.max(s, axis=1, keepdims=True))
        factor = jnp.exp2(top - new_top)
        w = jnp.exp2(s - new_top)
        total = total * factor + jnp.sum(w, axis=1, keepdims=True)
        acc = acc * factor + jnp.dot(w.astype(jnp.bfloat16), v, preferred_element_type=jnp.float32)
        return new_top, total, acc

    start_state = (
        jnp.full((rows, 1), -1e30, jnp.float32),
        jnp.zeros((rows, 1), jnp.float32),
        jnp.zeros((rows, HD), jnp.float32),
    )
    top, total, acc = lax.fori_loop(0, steps, body, start_state, unroll=4)
    out_ref[...] = (acc / total).astype(out_ref.dtype)
    lse_ref[...] = top * LN2 + jnp.log(total)


def attention_forward(q, kv_all, query_block=512, key_block=2048):
    rows = q.shape[0]
    keys = kv_all.shape[0]
    cost = pl.CostEstimate(
        flops=4 * rows * keys * HD, transcendentals=rows * keys, bytes_accessed=2 * HD * (2 * rows + 2 * keys)
    )
    return pl.pallas_call(
        functools.partial(forward_kernel, key_block),
        grid=(rows // query_block,),
        in_specs=[
            pl.BlockSpec((query_block, HD), lambda i: (i, 0)),
            pl.BlockSpec((keys, 2 * HD), lambda i: (0, 0)),
        ],
        out_specs=[
            pl.BlockSpec((query_block, HD), lambda i: (i, 0)),
            pl.BlockSpec((query_block, 1), lambda i: (i, 0)),
        ],
        out_shape=[
            jax.ShapeDtypeStruct((rows, HD), jnp.bfloat16),
            jax.ShapeDtypeStruct((rows, 1), jnp.float32),
        ],
        compiler_params=pltpu.CompilerParams(dimension_semantics=("arbitrary",)),
        cost_estimate=cost,
    )(q, kv_all)


def query_grad_kernel(key_block, q_ref, g_ref, lse_ref, delta_ref, kv_ref, cos_ref, sin_ref, dq_ref):
    q = q_ref[...]
    g = g_ref[...]
    lse = lse_ref[...] * LOG2E
    delta = delta_ref[...]
    steps = kv_ref.shape[0] // key_block

    def body(step, acc):
        start = pl.multiple_of(step * key_block, key_block)
        k = kv_ref[pl.ds(start, key_block), :HD]
        v = kv_ref[pl.ds(start, key_block), HD:]
        s = lax.dot_general(q, k, (((1,), (1,)), ((), ())), preferred_element_type=jnp.float32) * (SCALE * LOG2E)
        w = jnp.exp2(s - lse)
        gw = lax.dot_general(g, v, (((1,), (1,)), ((), ())), preferred_element_type=jnp.float32)
        gs = (w * (gw - delta)).astype(jnp.bfloat16)
        return acc + jnp.dot(gs, k, preferred_element_type=jnp.float32)

    acc = lax.fori_loop(0, steps, body, jnp.zeros(dq_ref.shape, jnp.float32), unroll=4)
    dq_ref[...] = rotate_back_rows(acc * SCALE, cos_ref, sin_ref).astype(dq_ref.dtype)


def attention_query_grad(q, g, lse_col, delta_col, kv_all, cos_wide, sin_wide, query_block=512, key_block=1024):
    rows = q.shape[0]
    keys = kv_all.shape[0]
    cost = pl.CostEstimate(
        flops=6 * rows * keys * HD, transcendentals=rows * keys, bytes_accessed=2 * HD * (3 * rows + 2 * keys)
    )
    row_spec = pl.BlockSpec((query_block, HD), lambda i: (i, 0))
    col_spec = pl.BlockSpec((query_block, 1), lambda i: (i, 0))
    whole = pl.BlockSpec((keys, 2 * HD), lambda i: (0, 0))
    return pl.pallas_call(
        functools.partial(query_grad_kernel, key_block),
        grid=(rows // query_block,),
        in_specs=[row_spec, row_spec, col_spec, col_spec, whole, row_spec, row_spec],
        out_specs=pl.BlockSpec((query_block, HD), lambda i: (i, 0)),
        out_shape=jax.ShapeDtypeStruct((rows, HD), jnp.bfloat16),
        compiler_params=pltpu.CompilerParams(dimension_semantics=("arbitrary",)),
        cost_estimate=cost,
    )(q, g, lse_col, delta_col, kv_all, cos_wide, sin_wide)


def key_grad_kernel(query_block, block_stride, k_ref, v_ref, qg_ref, lse_ref, delta_ref, cos_ref, sin_ref, dk_ref, dv_ref):
    k = k_ref[...]
    v = v_ref[...]
    steps = lse_ref.shape[1] // query_block

    def body(step, carry):
        dk, dv = carry
        start = pl.multiple_of(step * block_stride, 16)
        column = pl.multiple_of(step * query_block, query_block)
        q = qg_ref[pl.ds(start, query_block), :HD]
        g = qg_ref[pl.ds(start, query_block), HD:]
        lse = lse_ref[:, pl.ds(column, query_block)]
        delta = delta_ref[:, pl.ds(column, query_block)]
        s = lax.dot_general(k, q, (((1,), (1,)), ((), ())), preferred_element_type=jnp.float32) * (SCALE * LOG2E)
        w = jnp.exp2(s - lse * LOG2E)
        gw = lax.dot_general(v, g, (((1,), (1,)), ((), ())), preferred_element_type=jnp.float32)
        gs = (w * (gw - delta)).astype(jnp.bfloat16)
        dk = dk + jnp.dot(gs, q, preferred_element_type=jnp.float32)
        dv = dv + jnp.dot(w.astype(jnp.bfloat16), g, preferred_element_type=jnp.float32)
        return dk, dv

    zero = jnp.zeros(dk_ref.shape, jnp.float32)
    dk, dv = lax.fori_loop(0, steps, body, (zero, zero), unroll=4)
    dk_ref[...] = rotate_back_rows(dk * SCALE, cos_ref, sin_ref).astype(dk_ref.dtype)
    dv_ref[...] = dv.astype(dv_ref.dtype)


def attention_key_grad(k, v, qg_all, lse_row, delta_row, cos_wide, sin_wide, query_block, block_stride, key_rows=512):
    rows = k.shape[0]
    queries = lse_row.shape[1]
    cost = pl.CostEstimate(
        flops=8 * rows * queries * HD, transcendentals=rows * queries, bytes_accessed=2 * HD * (2 * rows + 2 * queries)
    )
    row_spec = pl.BlockSpec((key_rows, HD), lambda i: (i, 0))
    whole = pl.BlockSpec(qg_all.shape, lambda i: (0, 0))
    stat = pl.BlockSpec((1, queries), lambda i: (0, 0))
    return pl.pallas_call(
        functools.partial(key_grad_kernel, query_block, block_stride),
        grid=(rows // key_rows,),
        in_specs=[row_spec, row_spec, whole, stat, stat, row_spec, row_spec],
        out_specs=[row_spec, row_spec],
        out_shape=[jax.ShapeDtypeStruct((rows, HD), jnp.bfloat16)] * 2,
        compiler_params=pltpu.CompilerParams(dimension_semantics=("arbitrary",)),
        cost_estimate=cost,
    )(k, v, qg_all, lse_row, delta_row, cos_wide, sin_wide)


def shifted(value, axis, steps):
    count = lax.axis_size(axis)
    initial, last = (max(0, -steps), min(count, count - steps))
    return lax.ppermute(value, axis, [(source, source + steps) for source in range(initial, last)])


def frequencies(pair_count):
    return 1.0 / 10000.0 ** (jnp.arange(pair_count, dtype=jnp.float32) / pair_count)


def rope_tables(frame_pos, cell_ids):
    pair_count = HD // 2
    part_side = pair_count // 3
    part_time = pair_count - 2 * part_side
    grid_row = (cell_ids // GRID_W).astype(jnp.float32)
    grid_col = (cell_ids % GRID_W).astype(jnp.float32)
    angles = jnp.concatenate(
        [
            frame_pos.astype(jnp.float32)[:, None] * frequencies(part_time)[None, :],
            grid_row[:, None] * frequencies(part_side)[None, :],
            grid_col[:, None] * frequencies(part_side)[None, :],
        ],
        axis=1,
    )
    return (jnp.cos(angles), jnp.sin(angles))


def wide_tables(frame_pos, cell_ids):
    pair_count = HD // 2
    part_side = pair_count // 3
    part_time = pair_count - 2 * part_side
    freq = jnp.repeat(
        jnp.concatenate(
            [frequencies(part_time), frequencies(part_side), frequencies(part_side)]
        ),
        2,
    )
    pair = jnp.arange(HD, dtype=jnp.int32)[None, :] // 2
    grid_row = (cell_ids // GRID_W).astype(jnp.float32)[:, None]
    grid_col = (cell_ids % GRID_W).astype(jnp.float32)[:, None]
    position = jnp.where(
        pair < part_time,
        frame_pos.astype(jnp.float32)[:, None],
        jnp.where(pair < part_time + part_side, grid_row, grid_col),
    )
    angles = position * freq[None, :]
    even = jnp.arange(HD, dtype=jnp.int32)[None, :] % 2 == 0
    sin_angles = jnp.sin(angles)
    return (jnp.cos(angles), jnp.where(even, sin_angles, -sin_angles))


def rotate(vectors, cos_table, sin_table, direction):
    layout = vectors.shape
    paired = vectors.reshape(layout[:-1] + (layout[-1] // 2, 2))
    former = paired[..., 0]
    latter = paired[..., 1]
    out_former = former * cos_table - direction * latter * sin_table
    out_latter = direction * former * sin_table + latter * cos_table
    return jnp.stack([out_former, out_latter], axis=-1).reshape(layout)


def tap_mask(frame_clip):
    frame_total = frame_clip.shape[0]
    frame_ids = jnp.arange(frame_total, dtype=jnp.int32)
    columns = []
    for offset in range(3):
        target = frame_ids + offset
        inside = target < frame_total
        same_clip = frame_clip[jnp.minimum(target, frame_total - 1)] == frame_clip
        columns.append(jnp.logical_and(inside, same_clip).astype(jnp.float32))
    return jnp.stack(columns, axis=1)


def split_exact(values):
    high = lax.reduce_precision(values, exponent_bits=8, mantissa_bits=7)
    rest = values - high
    middle = lax.reduce_precision(rest, exponent_bits=8, mantissa_bits=7)
    low = rest - middle
    return jnp.stack([high, middle, low]).astype(jnp.bfloat16)


def cross(left, right):
    return lax.dot_general(
        left, right, (((1,), (1,)), ((), ())), preferred_element_type=jnp.float32
    )


def inner(left, right):
    return lax.dot_general(
        left, right, (((0,), (0,)), ((), ())), preferred_element_type=jnp.float32
    )


def on_device(
    queries, keys, values, token_cell, head_weight, norm_gain, time_weight, frame_clip, cotangent
):
    score_scale = HD ** (-0.5)
    tok_local = queries.shape[0]
    slab_cells = token_cell.shape[0]
    span_frames = cotangent.shape[0]
    channels = head_weight.shape[2]
    frame_pos = jnp.arange(tok_local, dtype=jnp.int32) // slab_cells
    cell_ids = jnp.tile(token_cell, tok_local // slab_cells)
    cos_wide, sin_wide = wide_tables(frame_pos, cell_ids)
    rot_q, pair = prepare(queries[:, 0, :], keys[:, 0, :], values[:, 0, :], cos_wide, -sin_wide)
    pair_all = lax.all_gather(pair, "seq", axis=0, tiled=True)
    all_weights = lax.all_gather(head_weight[0], "tm", axis=0, tiled=False)
    rot_k = pair[:, :HD]
    plain_v = values[:, 0, :]
    attended, log_col = attention_forward(rot_q, pair_all)
    log_total = log_col[:, 0]
    span_rows = span_frames * slab_cells
    head_count = lax.axis_size("tm")
    projected = jnp.dot(attended, head_weight[0], preferred_element_type=jnp.float32).astype(
        jnp.bfloat16
    )
    exchanged = lax.all_to_all(
        projected.reshape(head_count, span_frames * slab_cells, channels), "tm", 0, 0, tiled=False
    )
    mixed = jnp.sum(exchanged.astype(jnp.float32), axis=0).reshape(
        span_frames, slab_cells, channels
    )
    inverse = lax.rsqrt(jnp.mean(mixed * mixed, axis=2, keepdims=True) + 1e-06)
    normed = mixed * inverse * norm_gain
    mask_table = tap_mask(frame_clip)
    first_frame = lax.axis_index("tm") * span_frames
    local_mask = lax.dynamic_slice_in_dim(mask_table, first_frame, span_frames, 0)
    following = shifted(cotangent, "tm", -1)
    extended = jnp.concatenate([cotangent, following], axis=0)
    grad_act = jnp.zeros((span_frames, slab_cells, channels), jnp.float32)
    for offset in range(3):
        term = jnp.einsum(
            "fco,io->fci",
            extended[offset : offset + span_frames],
            time_weight[offset],
            preferred_element_type=jnp.float32,
        )
        grad_act = grad_act + local_mask[:, offset][:, None, None] * term
    sigmoid_n = jax.nn.sigmoid(normed)
    grad_normed = grad_act * sigmoid_n * (1.0 + normed * (1.0 - sigmoid_n))
    gained = grad_normed * norm_gain
    grad_mixed = (
        inverse * gained
        - inverse * inverse * inverse * mixed * jnp.mean(gained * mixed, axis=2, keepdims=True)
    ).astype(jnp.bfloat16)
    grad_mixed = grad_mixed.reshape(span_rows, channels)
    grad_heads = jnp.einsum(
        "re,hde->hrd", grad_mixed, all_weights, preferred_element_type=jnp.float32
    ).astype(jnp.bfloat16)
    grad_out = lax.all_to_all(grad_heads, "tm", 0, 0, tiled=False).reshape(tok_local, HD)
    row_delta = jnp.sum(grad_out.astype(jnp.float32) * attended.astype(jnp.float32), axis=1)

    grad_q = attention_query_grad(
        rot_q, grad_out, log_col, row_delta[:, None], pair_all, cos_wide, sin_wide
    )
    stat_rows = split_exact(jnp.stack([log_total, row_delta]))
    stat_rows = stat_rows.reshape(-1, 2 * HD)
    stat_pad = (-stat_rows.shape[0]) % 16
    stat_rows = jnp.pad(stat_rows, ((0, stat_pad), (0, 0)))
    packed = jnp.concatenate([jnp.concatenate([rot_q, grad_out], axis=1), stat_rows], axis=0)
    block_rows = packed.shape[0]
    seq_count = lax.axis_size("seq")
    gathered = lax.all_gather(packed, "seq", axis=0, tiled=True).reshape(
        seq_count, block_rows, 2 * HD
    )
    stat_all = gathered[:, tok_local:, :].reshape(seq_count, -1)[:, : 6 * tok_local]
    stat_all = stat_all.reshape(seq_count, 3, 2, tok_local).astype(jnp.float32)
    stat_all = (stat_all[:, 0] + stat_all[:, 1]) + stat_all[:, 2]
    piece_log = stat_all[:, 0, :].reshape(-1)
    piece_delta = stat_all[:, 1, :].reshape(-1)
    grad_k, grad_v = attention_key_grad(
        rot_k,
        plain_v,
        gathered.reshape(seq_count * block_rows, 2 * HD),
        piece_log[None, :],
        piece_delta[None, :],
        cos_wide,
        sin_wide,
        tok_local,
        block_rows,
    )
    grad_queries = grad_q[:, None, :]
    grad_keys = grad_k[:, None, :]
    grad_values = grad_v[:, None, :]
    return (grad_queries, grad_keys, grad_values)


def solution(mesh):
    in_specs = (
        P(("dp", "seq"), "tm", None),
        P(("dp", "seq"), "tm", None),
        P(("dp", "seq"), "tm", None),
        P("seq"),
        P("tm", None, None),
        P(),
        P(),
        P("dp"),
        P(("dp", "tm"), "seq", None),
    )
    out_specs = (
        P(("dp", "seq"), "tm", None),
        P(("dp", "seq"), "tm", None),
        P(("dp", "seq"), "tm", None),
    )
    return jax.shard_map(
        on_device, mesh=mesh, in_specs=in_specs, out_specs=out_specs, check_vma=False
    )
```

```python
import functools
import math

import jax
import jax.numpy as jnp
from jax import lax
from jax.experimental import pallas as pl
from jax.experimental.pallas import tpu as pltpu
from jax.sharding import PartitionSpec as P

HD = 128
GRID_W = 32
SCALE = HD ** (-0.5)
LOG2E = 1.4426950408889634
LN2 = 0.6931471805599453


def rotate_back_rows(x, cos_ref, sin_ref):
    lanes = lax.broadcasted_iota(jnp.int32, x.shape, 1)
    ahead = pltpu.roll(x, x.shape[1] - 1, 1)
    behind = pltpu.roll(x, 1, 1)
    ahead_lane = pltpu.roll(lanes, x.shape[1] - 1, 1)
    partner_lane = jnp.where(lanes % 2 == 0, lanes + 1, lanes - 1)
    partner = jnp.where(ahead_lane == partner_lane, ahead, behind)
    return x * cos_ref[...] + partner * sin_ref[...]


def prepare_kernel(q_ref, k_ref, v_ref, cos_ref, sin_ref, rq_ref, kv_ref):
    rq_ref[...] = rotate_back_rows(q_ref[...].astype(jnp.float32), cos_ref, sin_ref).astype(
        rq_ref.dtype
    )
    kv_ref[:, :HD] = rotate_back_rows(k_ref[...].astype(jnp.float32), cos_ref, sin_ref).astype(
        kv_ref.dtype
    )
    kv_ref[:, HD:] = v_ref[...]


def prepare(q, k, v, cos_wide, sin_forward):
    rows = q.shape[0]
    return pl.pallas_call(
        prepare_kernel,
        out_shape=[
            jax.ShapeDtypeStruct((rows, HD), jnp.bfloat16),
            jax.ShapeDtypeStruct((rows, 2 * HD), jnp.bfloat16),
        ],
        cost_estimate=pl.CostEstimate(flops=8 * rows * HD, transcendentals=0, bytes_accessed=14 * rows * HD),
    )(q, k, v, cos_wide, sin_forward)


def forward_kernel(key_block, q_ref, kv_ref, w_ref, out_ref, lse_ref, proj_ref):
    q = q_ref[...]
    rows = q.shape[0]
    steps = kv_ref.shape[0] // key_block

    def body(step, carry):
        top, total, acc = carry
        start = pl.multiple_of(step * key_block, key_block)
        k = kv_ref[pl.ds(start, key_block), :HD]
        v = kv_ref[pl.ds(start, key_block), HD:]
        s = lax.dot_general(q, k, (((1,), (1,)), ((), ())), preferred_element_type=jnp.float32) * (SCALE * LOG2E)
        new_top = jnp.maximum(top, jnp.max(s, axis=1, keepdims=True))
        factor = jnp.exp2(top - new_top)
        w = jnp.exp2(s - new_top)
        total = total * factor + jnp.sum(w, axis=1, keepdims=True)
        acc = acc * factor + jnp.dot(w.astype(jnp.bfloat16), v, preferred_element_type=jnp.float32)
        return new_top, total, acc

    start_state = (
        jnp.full((rows, 1), -1e30, jnp.float32),
        jnp.zeros((rows, 1), jnp.float32),
        jnp.zeros((rows, HD), jnp.float32),
    )
    top, total, acc = lax.fori_loop(0, steps, body, start_state, unroll=4)
    attended = (acc / total).astype(out_ref.dtype)
    out_ref[...] = attended
    proj_ref[...] = jnp.dot(attended, w_ref[...], preferred_element_type=jnp.float32).astype(
        proj_ref.dtype
    )
    lse_ref[...] = top * LN2 + jnp.log(total)


def attention_forward(q, kv_all, weight, query_block=512, key_block=2048):
    rows = q.shape[0]
    keys = kv_all.shape[0]
    cost = pl.CostEstimate(
        flops=4 * rows * keys * HD, transcendentals=rows * keys, bytes_accessed=2 * HD * (2 * rows + 2 * keys)
    )
    return pl.pallas_call(
        functools.partial(forward_kernel, key_block),
        grid=(rows // query_block,),
        in_specs=[
            pl.BlockSpec((query_block, HD), lambda i: (i, 0)),
            pl.BlockSpec((keys, 2 * HD), lambda i: (0, 0)),
            pl.BlockSpec(weight.shape, lambda i: (0, 0)),
        ],
        out_specs=[
            pl.BlockSpec((query_block, HD), lambda i: (i, 0)),
            pl.BlockSpec((query_block, 1), lambda i: (i, 0)),
            pl.BlockSpec((query_block, weight.shape[1]), lambda i: (i, 0)),
        ],
        out_shape=[
            jax.ShapeDtypeStruct((rows, HD), jnp.bfloat16),
            jax.ShapeDtypeStruct((rows, 1), jnp.float32),
            jax.ShapeDtypeStruct((rows, weight.shape[1]), jnp.bfloat16),
        ],
        compiler_params=pltpu.CompilerParams(dimension_semantics=("arbitrary",)),
        cost_estimate=cost,
    )(q, kv_all, weight)


def query_grad_kernel(key_block, q_ref, g_ref, lse_ref, delta_ref, kv_ref, cos_ref, sin_ref, dq_ref):
    q = q_ref[...]
    g = g_ref[...]
    lse = lse_ref[...] * LOG2E
    delta = delta_ref[...]
    steps = kv_ref.shape[0] // key_block

    def body(step, acc):
        start = pl.multiple_of(step * key_block, key_block)
        k = kv_ref[pl.ds(start, key_block), :HD]
        v = kv_ref[pl.ds(start, key_block), HD:]
        s = lax.dot_general(q, k, (((1,), (1,)), ((), ())), preferred_element_type=jnp.float32) * (SCALE * LOG2E)
        w = jnp.exp2(s - lse)
        gw = lax.dot_general(g, v, (((1,), (1,)), ((), ())), preferred_element_type=jnp.float32)
        gs = (w * (gw - delta)).astype(jnp.bfloat16)
        return acc + jnp.dot(gs, k, preferred_element_type=jnp.float32)

    acc = lax.fori_loop(0, steps, body, jnp.zeros(dq_ref.shape, jnp.float32), unroll=4)
    dq_ref[...] = rotate_back_rows(acc * SCALE, cos_ref, sin_ref).astype(dq_ref.dtype)


def attention_query_grad(q, g, lse_col, delta_col, kv_all, cos_wide, sin_wide, query_block=512, key_block=1024):
    rows = q.shape[0]
    keys = kv_all.shape[0]
    cost = pl.CostEstimate(
        flops=6 * rows * keys * HD, transcendentals=rows * keys, bytes_accessed=2 * HD * (3 * rows + 2 * keys)
    )
    row_spec = pl.BlockSpec((query_block, HD), lambda i: (i, 0))
    col_spec = pl.BlockSpec((query_block, 1), lambda i: (i, 0))
    whole = pl.BlockSpec((keys, 2 * HD), lambda i: (0, 0))
    return pl.pallas_call(
        functools.partial(query_grad_kernel, key_block),
        grid=(rows // query_block,),
        in_specs=[row_spec, row_spec, col_spec, col_spec, whole, row_spec, row_spec],
        out_specs=pl.BlockSpec((query_block, HD), lambda i: (i, 0)),
        out_shape=jax.ShapeDtypeStruct((rows, HD), jnp.bfloat16),
        compiler_params=pltpu.CompilerParams(dimension_semantics=("arbitrary",)),
        cost_estimate=cost,
    )(q, g, lse_col, delta_col, kv_all, cos_wide, sin_wide)


def key_grad_kernel(query_block, block_stride, k_ref, v_ref, qg_ref, lse_ref, delta_ref, cos_ref, sin_ref, dk_ref, dv_ref):
    k = k_ref[...]
    v = v_ref[...]
    steps = lse_ref.shape[1] // query_block

    def body(step, carry):
        dk, dv = carry
        start = pl.multiple_of(step * block_stride, 16)
        column = pl.multiple_of(step * query_block, query_block)
        q = qg_ref[pl.ds(start, query_block), :HD]
        g = qg_ref[pl.ds(start, query_block), HD:]
        lse = lse_ref[:, pl.ds(column, query_block)]
        delta = delta_ref[:, pl.ds(column, query_block)]
        s = lax.dot_general(k, q, (((1,), (1,)), ((), ())), preferred_element_type=jnp.float32) * (SCALE * LOG2E)
        w = jnp.exp2(s - lse * LOG2E)
        gw = lax.dot_general(v, g, (((1,), (1,)), ((), ())), preferred_element_type=jnp.float32)
        gs = (w * (gw - delta)).astype(jnp.bfloat16)
        dk = dk + jnp.dot(gs, q, preferred_element_type=jnp.float32)
        dv = dv + jnp.dot(w.astype(jnp.bfloat16), g, preferred_element_type=jnp.float32)
        return dk, dv

    zero = jnp.zeros(dk_ref.shape, jnp.float32)
    dk, dv = lax.fori_loop(0, steps, body, (zero, zero), unroll=4)
    dk_ref[...] = rotate_back_rows(dk * SCALE, cos_ref, sin_ref).astype(dk_ref.dtype)
    dv_ref[...] = dv.astype(dv_ref.dtype)


def attention_key_grad(k, v, qg_all, lse_row, delta_row, cos_wide, sin_wide, query_block, block_stride, key_rows=512):
    rows = k.shape[0]
    queries = lse_row.shape[1]
    cost = pl.CostEstimate(
        flops=8 * rows * queries * HD, transcendentals=rows * queries, bytes_accessed=2 * HD * (2 * rows + 2 * queries)
    )
    row_spec = pl.BlockSpec((key_rows, HD), lambda i: (i, 0))
    whole = pl.BlockSpec(qg_all.shape, lambda i: (0, 0))
    stat = pl.BlockSpec((1, queries), lambda i: (0, 0))
    return pl.pallas_call(
        functools.partial(key_grad_kernel, query_block, block_stride),
        grid=(rows // key_rows,),
        in_specs=[row_spec, row_spec, whole, stat, stat, row_spec, row_spec],
        out_specs=[row_spec, row_spec],
        out_shape=[jax.ShapeDtypeStruct((rows, HD), jnp.bfloat16)] * 2,
        compiler_params=pltpu.CompilerParams(dimension_semantics=("arbitrary",)),
        cost_estimate=cost,
    )(k, v, qg_all, lse_row, delta_row, cos_wide, sin_wide)


def shifted(value, axis, steps):
    count = lax.axis_size(axis)
    initial, last = (max(0, -steps), min(count, count - steps))
    return lax.ppermute(value, axis, [(source, source + steps) for source in range(initial, last)])


def frequencies(pair_count):
    return 1.0 / 10000.0 ** (jnp.arange(pair_count, dtype=jnp.float32) / pair_count)


def rope_tables(frame_pos, cell_ids):
    pair_count = HD // 2
    part_side = pair_count // 3
    part_time = pair_count - 2 * part_side
    grid_row = (cell_ids // GRID_W).astype(jnp.float32)
    grid_col = (cell_ids % GRID_W).astype(jnp.float32)
    angles = jnp.concatenate(
        [
            frame_pos.astype(jnp.float32)[:, None] * frequencies(part_time)[None, :],
            grid_row[:, None] * frequencies(part_side)[None, :],
            grid_col[:, None] * frequencies(part_side)[None, :],
        ],
        axis=1,
    )
    return (jnp.cos(angles), jnp.sin(angles))


def wide_tables(frame_pos, cell_ids):
    pair_count = HD // 2
    part_side = pair_count // 3
    part_time = pair_count - 2 * part_side
    freq = jnp.repeat(
        jnp.concatenate(
            [frequencies(part_time), frequencies(part_side), frequencies(part_side)]
        ),
        2,
    )
    pair = jnp.arange(HD, dtype=jnp.int32)[None, :] // 2
    grid_row = (cell_ids // GRID_W).astype(jnp.float32)[:, None]
    grid_col = (cell_ids % GRID_W).astype(jnp.float32)[:, None]
    position = jnp.where(
        pair < part_time,
        frame_pos.astype(jnp.float32)[:, None],
        jnp.where(pair < part_time + part_side, grid_row, grid_col),
    )
    angles = position * freq[None, :]
    even = jnp.arange(HD, dtype=jnp.int32)[None, :] % 2 == 0
    sin_angles = jnp.sin(angles)
    return (jnp.cos(angles), jnp.where(even, sin_angles, -sin_angles))


def rotate(vectors, cos_table, sin_table, direction):
    layout = vectors.shape
    paired = vectors.reshape(layout[:-1] + (layout[-1] // 2, 2))
    former = paired[..., 0]
    latter = paired[..., 1]
    out_former = former * cos_table - direction * latter * sin_table
    out_latter = direction * former * sin_table + latter * cos_table
    return jnp.stack([out_former, out_latter], axis=-1).reshape(layout)


def tap_mask(frame_clip):
    frame_total = frame_clip.shape[0]
    frame_ids = jnp.arange(frame_total, dtype=jnp.int32)
    columns = []
    for offset in range(3):
        target = frame_ids + offset
        inside = target < frame_total
        same_clip = frame_clip[jnp.minimum(target, frame_total - 1)] == frame_clip
        columns.append(jnp.logical_and(inside, same_clip).astype(jnp.float32))
    return jnp.stack(columns, axis=1)


def split_exact(values):
    high = lax.reduce_precision(values, exponent_bits=8, mantissa_bits=7)
    rest = values - high
    middle = lax.reduce_precision(rest, exponent_bits=8, mantissa_bits=7)
    low = rest - middle
    return jnp.stack([high, middle, low]).astype(jnp.bfloat16)


def cross(left, right):
    return lax.dot_general(
        left, right, (((1,), (1,)), ((), ())), preferred_element_type=jnp.float32
    )


def inner(left, right):
    return lax.dot_general(
        left, right, (((0,), (0,)), ((), ())), preferred_element_type=jnp.float32
    )


def on_device(
    queries, keys, values, token_cell, head_weight, norm_gain, time_weight, frame_clip, cotangent
):
    score_scale = HD ** (-0.5)
    tok_local = queries.shape[0]
    slab_cells = token_cell.shape[0]
    span_frames = cotangent.shape[0]
    channels = head_weight.shape[2]
    frame_pos = jnp.arange(tok_local, dtype=jnp.int32) // slab_cells
    cell_ids = jnp.tile(token_cell, tok_local // slab_cells)
    cos_wide, sin_wide = wide_tables(frame_pos, cell_ids)
    rot_q, pair = prepare(queries[:, 0, :], keys[:, 0, :], values[:, 0, :], cos_wide, -sin_wide)
    pair_all = lax.all_gather(pair, "seq", axis=0, tiled=True)
    all_weights = lax.all_gather(head_weight[0], "tm", axis=0, tiled=False)
    rot_k = pair[:, :HD]
    plain_v = values[:, 0, :]
    attended, log_col, projected = attention_forward(rot_q, pair_all, head_weight[0])
    log_total = log_col[:, 0]
    span_rows = span_frames * slab_cells
    head_count = lax.axis_size("tm")
    exchanged = lax.all_to_all(
        projected.reshape(head_count, span_frames * slab_cells, channels), "tm", 0, 0, tiled=False
    )
    mixed = jnp.sum(exchanged.astype(jnp.float32), axis=0).reshape(
        span_frames, slab_cells, channels
    )
    inverse = lax.rsqrt(jnp.mean(mixed * mixed, axis=2, keepdims=True) + 1e-06)
    normed = mixed * inverse * norm_gain
    mask_table = tap_mask(frame_clip)
    first_frame = lax.axis_index("tm") * span_frames
    local_mask = lax.dynamic_slice_in_dim(mask_table, first_frame, span_frames, 0)
    following = shifted(cotangent, "tm", -1)
    extended = jnp.concatenate([cotangent, following], axis=0)
    grad_act = jnp.zeros((span_frames, slab_cells, channels), jnp.float32)
    for offset in range(3):
        term = jnp.einsum(
            "fco,io->fci",
            extended[offset : offset + span_frames],
            time_weight[offset],
            preferred_element_type=jnp.float32,
        )
        grad_act = grad_act + local_mask[:, offset][:, None, None] * term
    sigmoid_n = jax.nn.sigmoid(normed)
    grad_normed = grad_act * sigmoid_n * (1.0 + normed * (1.0 - sigmoid_n))
    gained = grad_normed * norm_gain
    grad_mixed = (
        inverse * gained
        - inverse * inverse * inverse * mixed * jnp.mean(gained * mixed, axis=2, keepdims=True)
    ).astype(jnp.bfloat16)
    grad_mixed = grad_mixed.reshape(span_rows, channels)
    grad_heads = jnp.einsum(
        "re,hde->hrd", grad_mixed, all_weights, preferred_element_type=jnp.float32
    ).astype(jnp.bfloat16)
    grad_out = lax.all_to_all(grad_heads, "tm", 0, 0, tiled=False).reshape(tok_local, HD)
    row_delta = jnp.sum(grad_out.astype(jnp.float32) * attended.astype(jnp.float32), axis=1)

    grad_q = attention_query_grad(
        rot_q, grad_out, log_col, row_delta[:, None], pair_all, cos_wide, sin_wide
    )
    stat_rows = split_exact(jnp.stack([log_total, row_delta]))
    stat_rows = stat_rows.reshape(-1, 2 * HD)
    stat_pad = (-stat_rows.shape[0]) % 16
    stat_rows = jnp.pad(stat_rows, ((0, stat_pad), (0, 0)))
    packed = jnp.concatenate([jnp.concatenate([rot_q, grad_out], axis=1), stat_rows], axis=0)
    block_rows = packed.shape[0]
    seq_count = lax.axis_size("seq")
    gathered = lax.all_gather(packed, "seq", axis=0, tiled=True).reshape(
        seq_count, block_rows, 2 * HD
    )
    stat_all = gathered[:, tok_local:, :].reshape(seq_count, -1)[:, : 6 * tok_local]
    stat_all = stat_all.reshape(seq_count, 3, 2, tok_local).astype(jnp.float32)
    stat_all = (stat_all[:, 0] + stat_all[:, 1]) + stat_all[:, 2]
    piece_log = stat_all[:, 0, :].reshape(-1)
    piece_delta = stat_all[:, 1, :].reshape(-1)
    grad_k, grad_v = attention_key_grad(
        rot_k,
        plain_v,
        gathered.reshape(seq_count * block_rows, 2 * HD),
        piece_log[None, :],
        piece_delta[None, :],
        cos_wide,
        sin_wide,
        tok_local,
        block_rows,
    )
    grad_queries = grad_q[:, None, :]
    grad_keys = grad_k[:, None, :]
    grad_values = grad_v[:, None, :]
    return (grad_queries, grad_keys, grad_values)


def solution(mesh):
    in_specs = (
        P(("dp", "seq"), "tm", None),
        P(("dp", "seq"), "tm", None),
        P(("dp", "seq"), "tm", None),
        P("seq"),
        P("tm", None, None),
        P(),
        P(),
        P("dp"),
        P(("dp", "tm"), "seq", None),
    )
    out_specs = (
        P(("dp", "seq"), "tm", None),
        P(("dp", "seq"), "tm", None),
        P(("dp", "seq"), "tm", None),
    )
    return jax.shard_map(
        on_device, mesh=mesh, in_specs=in_specs, out_specs=out_specs, check_vma=False
    )
```

```python
import functools
import math

import jax
import jax.numpy as jnp
from jax import lax
from jax.experimental import pallas as pl
from jax.experimental.pallas import tpu as pltpu
from jax.sharding import PartitionSpec as P

HD = 128
GRID_W = 32
SCALE = HD ** (-0.5)
LOG2E = 1.4426950408889634
LN2 = 0.6931471805599453


def rotate_back_rows(x, cos_ref, sin_ref):
    lanes = lax.broadcasted_iota(jnp.int32, x.shape, 1)
    ahead = pltpu.roll(x, x.shape[1] - 1, 1)
    behind = pltpu.roll(x, 1, 1)
    ahead_lane = pltpu.roll(lanes, x.shape[1] - 1, 1)
    partner_lane = jnp.where(lanes % 2 == 0, lanes + 1, lanes - 1)
    partner = jnp.where(ahead_lane == partner_lane, ahead, behind)
    return x * cos_ref[...] + partner * sin_ref[...]


def prepare_kernel(q_ref, k_ref, v_ref, cos_ref, sin_ref, rq_ref, kv_ref):
    rq_ref[...] = rotate_back_rows(q_ref[...].astype(jnp.float32), cos_ref, sin_ref).astype(
        rq_ref.dtype
    )
    kv_ref[:, :HD] = rotate_back_rows(k_ref[...].astype(jnp.float32), cos_ref, sin_ref).astype(
        kv_ref.dtype
    )
    kv_ref[:, HD:] = v_ref[...]


def prepare(q, k, v, cos_wide, sin_forward):
    rows = q.shape[0]
    return pl.pallas_call(
        prepare_kernel,
        out_shape=[
            jax.ShapeDtypeStruct((rows, HD), jnp.bfloat16),
            jax.ShapeDtypeStruct((rows, 2 * HD), jnp.bfloat16),
        ],
        cost_estimate=pl.CostEstimate(flops=8 * rows * HD, transcendentals=0, bytes_accessed=14 * rows * HD),
    )(q, k, v, cos_wide, sin_forward)


def forward_kernel(key_block, q_ref, kv_ref, w_ref, out_ref, lse_ref, proj_ref):
    q = q_ref[...]
    rows = q.shape[0]
    steps = kv_ref.shape[0] // key_block

    def body(step, carry):
        top, total, acc = carry
        start = pl.multiple_of(step * key_block, key_block)
        k = kv_ref[pl.ds(start, key_block), :HD]
        v = kv_ref[pl.ds(start, key_block), HD:]
        s = lax.dot_general(q, k, (((1,), (1,)), ((), ())), preferred_element_type=jnp.float32) * (SCALE * LOG2E)
        new_top = jnp.maximum(top, jnp.max(s, axis=1, keepdims=True))
        factor = jnp.exp2(top - new_top)
        w = jnp.exp2(s - new_top)
        total = total * factor + jnp.sum(w, axis=1, keepdims=True)
        acc = acc * factor + jnp.dot(w.astype(jnp.bfloat16), v, preferred_element_type=jnp.float32)
        return new_top, total, acc

    start_state = (
        jnp.full((rows, 1), -1e30, jnp.float32),
        jnp.zeros((rows, 1), jnp.float32),
        jnp.zeros((rows, HD), jnp.float32),
    )
    top, total, acc = lax.fori_loop(0, steps, body, start_state, unroll=4)
    attended = (acc / total).astype(out_ref.dtype)
    out_ref[...] = attended
    proj_ref[...] = jnp.dot(attended, w_ref[...], preferred_element_type=jnp.float32).astype(
        proj_ref.dtype
    )
    lse_ref[...] = top * LN2 + jnp.log(total)


def attention_forward(q, kv_all, weight, query_block=512, key_block=2048):
    rows = q.shape[0]
    keys = kv_all.shape[0]
    cost = pl.CostEstimate(
        flops=4 * rows * keys * HD, transcendentals=rows * keys, bytes_accessed=2 * HD * (2 * rows + 2 * keys)
    )
    return pl.pallas_call(
        functools.partial(forward_kernel, key_block),
        grid=(rows // query_block,),
        in_specs=[
            pl.BlockSpec((query_block, HD), lambda i: (i, 0)),
            pl.BlockSpec((keys, 2 * HD), lambda i: (0, 0)),
            pl.BlockSpec(weight.shape, lambda i: (0, 0)),
        ],
        out_specs=[
            pl.BlockSpec((query_block, HD), lambda i: (i, 0)),
            pl.BlockSpec((query_block, 1), lambda i: (i, 0)),
            pl.BlockSpec((query_block, weight.shape[1]), lambda i: (i, 0)),
        ],
        out_shape=[
            jax.ShapeDtypeStruct((rows, HD), jnp.bfloat16),
            jax.ShapeDtypeStruct((rows, 1), jnp.float32),
            jax.ShapeDtypeStruct((rows, weight.shape[1]), jnp.bfloat16),
        ],
        compiler_params=pltpu.CompilerParams(dimension_semantics=("arbitrary",)),
        cost_estimate=cost,
    )(q, kv_all, weight)


def query_grad_kernel(key_block, q_ref, g_ref, lse_ref, delta_ref, kv_ref, cos_ref, sin_ref, dq_ref):
    q = q_ref[...]
    g = g_ref[...]
    lse = lse_ref[...] * LOG2E
    delta = delta_ref[...]
    steps = kv_ref.shape[0] // key_block

    def body(step, acc):
        start = pl.multiple_of(step * key_block, key_block)
        k = kv_ref[pl.ds(start, key_block), :HD]
        v = kv_ref[pl.ds(start, key_block), HD:]
        s = lax.dot_general(q, k, (((1,), (1,)), ((), ())), preferred_element_type=jnp.float32) * (SCALE * LOG2E)
        w = jnp.exp2(s - lse)
        gw = lax.dot_general(g, v, (((1,), (1,)), ((), ())), preferred_element_type=jnp.float32)
        gs = (w * (gw - delta)).astype(jnp.bfloat16)
        return acc + jnp.dot(gs, k, preferred_element_type=jnp.float32)

    acc = lax.fori_loop(0, steps, body, jnp.zeros(dq_ref.shape, jnp.float32), unroll=4)
    dq_ref[...] = rotate_back_rows(acc * SCALE, cos_ref, sin_ref).astype(dq_ref.dtype)


def attention_query_grad(q, g, lse_col, delta_col, kv_all, cos_wide, sin_wide, query_block=512, key_block=1024):
    rows = q.shape[0]
    keys = kv_all.shape[0]
    cost = pl.CostEstimate(
        flops=6 * rows * keys * HD, transcendentals=rows * keys, bytes_accessed=2 * HD * (3 * rows + 2 * keys)
    )
    row_spec = pl.BlockSpec((query_block, HD), lambda i: (i, 0))
    col_spec = pl.BlockSpec((query_block, 1), lambda i: (i, 0))
    whole = pl.BlockSpec((keys, 2 * HD), lambda i: (0, 0))
    return pl.pallas_call(
        functools.partial(query_grad_kernel, key_block),
        grid=(rows // query_block,),
        in_specs=[row_spec, row_spec, col_spec, col_spec, whole, row_spec, row_spec],
        out_specs=pl.BlockSpec((query_block, HD), lambda i: (i, 0)),
        out_shape=jax.ShapeDtypeStruct((rows, HD), jnp.bfloat16),
        compiler_params=pltpu.CompilerParams(dimension_semantics=("arbitrary",)),
        cost_estimate=cost,
    )(q, g, lse_col, delta_col, kv_all, cos_wide, sin_wide)


def stat_row(tile, stat, halves):
    parts = []
    for half in range(halves):
        row = stat * halves + half
        step = 2 * halves
        parts.append((tile[row : row + 1] + tile[step + row : step + row + 1]) + tile[2 * step + row : 2 * step + row + 1])
    return jnp.concatenate(parts, axis=1)


def key_grad_kernel(query_block, block_stride, blocks, k_ref, v_ref, qg_ref, cos_ref, sin_ref, dk_ref, dv_ref):
    k = k_ref[...]
    v = v_ref[...]
    steps = blocks
    halves = query_block // (2 * HD)

    def body(step, carry):
        dk, dv = carry
        start = pl.multiple_of(step * block_stride, 16)
        q = qg_ref[pl.ds(start, query_block), :HD]
        g = qg_ref[pl.ds(start, query_block), HD:]
        tile = qg_ref[pl.ds(start + query_block, 16), :].astype(jnp.float32)
        lse = stat_row(tile, 0, halves)
        delta = stat_row(tile, 1, halves)
        s = lax.dot_general(k, q, (((1,), (1,)), ((), ())), preferred_element_type=jnp.float32) * (SCALE * LOG2E)
        w = jnp.exp2(s - lse * LOG2E)
        gw = lax.dot_general(v, g, (((1,), (1,)), ((), ())), preferred_element_type=jnp.float32)
        gs = (w * (gw - delta)).astype(jnp.bfloat16)
        dk = dk + jnp.dot(gs, q, preferred_element_type=jnp.float32)
        dv = dv + jnp.dot(w.astype(jnp.bfloat16), g, preferred_element_type=jnp.float32)
        return dk, dv

    zero = jnp.zeros(dk_ref.shape, jnp.float32)
    dk, dv = lax.fori_loop(0, steps, body, (zero, zero), unroll=4)
    dk_ref[...] = rotate_back_rows(dk * SCALE, cos_ref, sin_ref).astype(dk_ref.dtype)
    dv_ref[...] = dv.astype(dv_ref.dtype)


def attention_key_grad(k, v, qg_all, cos_wide, sin_wide, query_block, block_stride, key_rows=512):
    rows = k.shape[0]
    blocks = qg_all.shape[0] // block_stride
    queries = blocks * query_block
    cost = pl.CostEstimate(
        flops=8 * rows * queries * HD, transcendentals=rows * queries, bytes_accessed=2 * HD * (2 * rows + 2 * queries)
    )
    row_spec = pl.BlockSpec((key_rows, HD), lambda i: (i, 0))
    whole = pl.BlockSpec(qg_all.shape, lambda i: (0, 0))
    return pl.pallas_call(
        functools.partial(key_grad_kernel, query_block, block_stride, blocks),
        grid=(rows // key_rows,),
        in_specs=[row_spec, row_spec, whole, row_spec, row_spec],
        out_specs=[row_spec, row_spec],
        out_shape=[jax.ShapeDtypeStruct((rows, HD), jnp.bfloat16)] * 2,
        compiler_params=pltpu.CompilerParams(dimension_semantics=("arbitrary",)),
        cost_estimate=cost,
    )(k, v, qg_all, cos_wide, sin_wide)


def shifted(value, axis, steps):
    count = lax.axis_size(axis)
    initial, last = (max(0, -steps), min(count, count - steps))
    return lax.ppermute(value, axis, [(source, source + steps) for source in range(initial, last)])


def frequencies(pair_count):
    return 1.0 / 10000.0 ** (jnp.arange(pair_count, dtype=jnp.float32) / pair_count)


def rope_tables(frame_pos, cell_ids):
    pair_count = HD // 2
    part_side = pair_count // 3
    part_time = pair_count - 2 * part_side
    grid_row = (cell_ids // GRID_W).astype(jnp.float32)
    grid_col = (cell_ids % GRID_W).astype(jnp.float32)
    angles = jnp.concatenate(
        [
            frame_pos.astype(jnp.float32)[:, None] * frequencies(part_time)[None, :],
            grid_row[:, None] * frequencies(part_side)[None, :],
            grid_col[:, None] * frequencies(part_side)[None, :],
        ],
        axis=1,
    )
    return (jnp.cos(angles), jnp.sin(angles))


def wide_tables(frame_pos, cell_ids):
    pair_count = HD // 2
    part_side = pair_count // 3
    part_time = pair_count - 2 * part_side
    freq = jnp.repeat(
        jnp.concatenate(
            [frequencies(part_time), frequencies(part_side), frequencies(part_side)]
        ),
        2,
    )
    pair = jnp.arange(HD, dtype=jnp.int32)[None, :] // 2
    grid_row = (cell_ids // GRID_W).astype(jnp.float32)[:, None]
    grid_col = (cell_ids % GRID_W).astype(jnp.float32)[:, None]
    position = jnp.where(
        pair < part_time,
        frame_pos.astype(jnp.float32)[:, None],
        jnp.where(pair < part_time + part_side, grid_row, grid_col),
    )
    angles = position * freq[None, :]
    even = jnp.arange(HD, dtype=jnp.int32)[None, :] % 2 == 0
    sin_angles = jnp.sin(angles)
    return (jnp.cos(angles), jnp.where(even, sin_angles, -sin_angles))


def rotate(vectors, cos_table, sin_table, direction):
    layout = vectors.shape
    paired = vectors.reshape(layout[:-1] + (layout[-1] // 2, 2))
    former = paired[..., 0]
    latter = paired[..., 1]
    out_former = former * cos_table - direction * latter * sin_table
    out_latter = direction * former * sin_table + latter * cos_table
    return jnp.stack([out_former, out_latter], axis=-1).reshape(layout)


def tap_mask(frame_clip):
    frame_total = frame_clip.shape[0]
    frame_ids = jnp.arange(frame_total, dtype=jnp.int32)
    columns = []
    for offset in range(3):
        target = frame_ids + offset
        inside = target < frame_total
        same_clip = frame_clip[jnp.minimum(target, frame_total - 1)] == frame_clip
        columns.append(jnp.logical_and(inside, same_clip).astype(jnp.float32))
    return jnp.stack(columns, axis=1)


def split_exact(values):
    high = lax.reduce_precision(values, exponent_bits=8, mantissa_bits=7)
    rest = values - high
    middle = lax.reduce_precision(rest, exponent_bits=8, mantissa_bits=7)
    low = rest - middle
    return jnp.stack([high, middle, low]).astype(jnp.bfloat16)


def cross(left, right):
    return lax.dot_general(
        left, right, (((1,), (1,)), ((), ())), preferred_element_type=jnp.float32
    )


def inner(left, right):
    return lax.dot_general(
        left, right, (((0,), (0,)), ((), ())), preferred_element_type=jnp.float32
    )


def on_device(
    queries, keys, values, token_cell, head_weight, norm_gain, time_weight, frame_clip, cotangent
):
    score_scale = HD ** (-0.5)
    tok_local = queries.shape[0]
    slab_cells = token_cell.shape[0]
    span_frames = cotangent.shape[0]
    channels = head_weight.shape[2]
    frame_pos = jnp.arange(tok_local, dtype=jnp.int32) // slab_cells
    cell_ids = jnp.tile(token_cell, tok_local // slab_cells)
    cos_wide, sin_wide = wide_tables(frame_pos, cell_ids)
    rot_q, pair = prepare(queries[:, 0, :], keys[:, 0, :], values[:, 0, :], cos_wide, -sin_wide)
    pair_all = lax.all_gather(pair, "seq", axis=0, tiled=True)
    all_weights = lax.all_gather(head_weight[0], "tm", axis=0, tiled=False)
    rot_k = pair[:, :HD]
    plain_v = values[:, 0, :]
    attended, log_col, projected = attention_forward(rot_q, pair_all, head_weight[0])
    log_total = log_col[:, 0]
    span_rows = span_frames * slab_cells
    head_count = lax.axis_size("tm")
    exchanged = lax.all_to_all(
        projected.reshape(head_count, span_frames * slab_cells, channels), "tm", 0, 0, tiled=False
    )
    mixed = jnp.sum(exchanged.astype(jnp.float32), axis=0).reshape(
        span_frames, slab_cells, channels
    )
    inverse = lax.rsqrt(jnp.mean(mixed * mixed, axis=2, keepdims=True) + 1e-06)
    normed = mixed * inverse * norm_gain
    mask_table = tap_mask(frame_clip)
    first_frame = lax.axis_index("tm") * span_frames
    local_mask = lax.dynamic_slice_in_dim(mask_table, first_frame, span_frames, 0)
    following = shifted(cotangent, "tm", -1)
    extended = jnp.concatenate([cotangent, following], axis=0)
    grad_act = jnp.zeros((span_frames, slab_cells, channels), jnp.float32)
    for offset in range(3):
        term = jnp.einsum(
            "fco,io->fci",
            extended[offset : offset + span_frames],
            time_weight[offset],
            preferred_element_type=jnp.float32,
        )
        grad_act = grad_act + local_mask[:, offset][:, None, None] * term
    sigmoid_n = jax.nn.sigmoid(normed)
    grad_normed = grad_act * sigmoid_n * (1.0 + normed * (1.0 - sigmoid_n))
    gained = grad_normed * norm_gain
    grad_mixed = (
        inverse * gained
        - inverse * inverse * inverse * mixed * jnp.mean(gained * mixed, axis=2, keepdims=True)
    ).astype(jnp.bfloat16)
    grad_mixed = grad_mixed.reshape(span_rows, channels)
    grad_heads = jnp.einsum(
        "re,hde->hrd", grad_mixed, all_weights, preferred_element_type=jnp.float32
    ).astype(jnp.bfloat16)
    grad_out = lax.all_to_all(grad_heads, "tm", 0, 0, tiled=False).reshape(tok_local, HD)
    row_delta = jnp.sum(grad_out.astype(jnp.float32) * attended.astype(jnp.float32), axis=1)

    grad_q = attention_query_grad(
        rot_q, grad_out, log_col, row_delta[:, None], pair_all, cos_wide, sin_wide
    )
    stat_rows = split_exact(jnp.stack([log_total, row_delta]))
    stat_rows = stat_rows.reshape(-1, 2 * HD)
    stat_pad = (-stat_rows.shape[0]) % 16
    stat_rows = jnp.pad(stat_rows, ((0, stat_pad), (0, 0)))
    packed = jnp.concatenate([jnp.concatenate([rot_q, grad_out], axis=1), stat_rows], axis=0)
    block_rows = packed.shape[0]
    seq_count = lax.axis_size("seq")
    gathered = lax.all_gather(packed, "seq", axis=0, tiled=True).reshape(
        seq_count, block_rows, 2 * HD
    )
    grad_k, grad_v = attention_key_grad(
        rot_k,
        plain_v,
        gathered.reshape(seq_count * block_rows, 2 * HD),
        cos_wide,
        sin_wide,
        tok_local,
        block_rows,
    )
    grad_queries = grad_q[:, None, :]
    grad_keys = grad_k[:, None, :]
    grad_values = grad_v[:, None, :]
    return (grad_queries, grad_keys, grad_values)


def solution(mesh):
    in_specs = (
        P(("dp", "seq"), "tm", None),
        P(("dp", "seq"), "tm", None),
        P(("dp", "seq"), "tm", None),
        P("seq"),
        P("tm", None, None),
        P(),
        P(),
        P("dp"),
        P(("dp", "tm"), "seq", None),
    )
    out_specs = (
        P(("dp", "seq"), "tm", None),
        P(("dp", "seq"), "tm", None),
        P(("dp", "seq"), "tm", None),
    )
    return jax.shard_map(
        on_device, mesh=mesh, in_specs=in_specs, out_specs=out_specs, check_vma=False
    )
```

```python
import functools
import math

import jax
import jax.numpy as jnp
from jax import lax
from jax.experimental import pallas as pl
from jax.experimental.pallas import tpu as pltpu
from jax.sharding import PartitionSpec as P

HD = 128
GRID_W = 32
SCALE = HD ** (-0.5)
LOG2E = 1.4426950408889634
LN2 = 0.6931471805599453


def rotate_back_rows(x, cos_ref, sin_ref):
    lanes = lax.broadcasted_iota(jnp.int32, x.shape, 1)
    ahead = pltpu.roll(x, x.shape[1] - 1, 1)
    behind = pltpu.roll(x, 1, 1)
    ahead_lane = pltpu.roll(lanes, x.shape[1] - 1, 1)
    partner_lane = jnp.where(lanes % 2 == 0, lanes + 1, lanes - 1)
    partner = jnp.where(ahead_lane == partner_lane, ahead, behind)
    return x * cos_ref[...] + partner * sin_ref[...]


def prepare_kernel(q_ref, k_ref, v_ref, cos_ref, sin_ref, rq_ref, kv_ref):
    rq_ref[...] = rotate_back_rows(q_ref[...].astype(jnp.float32), cos_ref, sin_ref).astype(
        rq_ref.dtype
    )
    kv_ref[:, :HD] = rotate_back_rows(k_ref[...].astype(jnp.float32), cos_ref, sin_ref).astype(
        kv_ref.dtype
    )
    kv_ref[:, HD:] = v_ref[...]


def prepare(q, k, v, cos_wide, sin_forward):
    rows = q.shape[0]
    return pl.pallas_call(
        prepare_kernel,
        out_shape=[
            jax.ShapeDtypeStruct((rows, HD), jnp.bfloat16),
            jax.ShapeDtypeStruct((rows, 2 * HD), jnp.bfloat16),
        ],
        cost_estimate=pl.CostEstimate(flops=8 * rows * HD, transcendentals=0, bytes_accessed=14 * rows * HD),
    )(q, k, v, cos_wide, sin_forward)


def forward_kernel(key_block, q_ref, kv_ref, w_ref, out_ref, lse_ref, proj_ref):
    q = q_ref[...]
    rows = q.shape[0]
    steps = kv_ref.shape[0] // key_block

    def body(step, carry):
        top, total, acc = carry
        start = pl.multiple_of(step * key_block, key_block)
        k = kv_ref[pl.ds(start, key_block), :HD]
        v = kv_ref[pl.ds(start, key_block), HD:]
        s = lax.dot_general(q, k, (((1,), (1,)), ((), ())), preferred_element_type=jnp.float32) * (SCALE * LOG2E)
        new_top = jnp.maximum(top, jnp.max(s, axis=1, keepdims=True))
        factor = jnp.exp2(top - new_top)
        w = jnp.exp2(s - new_top)
        total = total * factor + jnp.sum(w, axis=1, keepdims=True)
        acc = acc * factor + jnp.dot(w.astype(jnp.bfloat16), v, preferred_element_type=jnp.float32)
        return new_top, total, acc

    start_state = (
        jnp.full((rows, 1), -1e30, jnp.float32),
        jnp.zeros((rows, 1), jnp.float32),
        jnp.zeros((rows, HD), jnp.float32),
    )
    top, total, acc = lax.fori_loop(0, steps, body, start_state, unroll=4)
    attended = (acc / total).astype(out_ref.dtype)
    out_ref[...] = attended
    proj_ref[...] = jnp.dot(attended, w_ref[...], preferred_element_type=jnp.float32).astype(
        proj_ref.dtype
    )
    lse_ref[...] = top * LN2 + jnp.log(total)


def attention_forward(q, kv_all, weight, query_block=512, key_block=2048):
    rows = q.shape[0]
    keys = kv_all.shape[0]
    cost = pl.CostEstimate(
        flops=4 * rows * keys * HD, transcendentals=rows * keys, bytes_accessed=2 * HD * (2 * rows + 2 * keys)
    )
    return pl.pallas_call(
        functools.partial(forward_kernel, key_block),
        grid=(rows // query_block,),
        in_specs=[
            pl.BlockSpec((query_block, HD), lambda i: (i, 0)),
            pl.BlockSpec((keys, 2 * HD), lambda i: (0, 0)),
            pl.BlockSpec(weight.shape, lambda i: (0, 0)),
        ],
        out_specs=[
            pl.BlockSpec((query_block, HD), lambda i: (i, 0)),
            pl.BlockSpec((query_block, 1), lambda i: (i, 0)),
            pl.BlockSpec((query_block, weight.shape[1]), lambda i: (i, 0)),
        ],
        out_shape=[
            jax.ShapeDtypeStruct((rows, HD), jnp.bfloat16),
            jax.ShapeDtypeStruct((rows, 1), jnp.float32),
            jax.ShapeDtypeStruct((rows, weight.shape[1]), jnp.bfloat16),
        ],
        compiler_params=pltpu.CompilerParams(dimension_semantics=("arbitrary",)),
        cost_estimate=cost,
    )(q, kv_all, weight)


def query_grad_kernel(key_block, q_ref, g_ref, lse_ref, delta_ref, kv_ref, cos_ref, sin_ref, dq_ref):
    q = q_ref[...]
    g = g_ref[...]
    lse = lse_ref[...] * LOG2E
    delta = delta_ref[...]
    steps = kv_ref.shape[0] // key_block

    def body(step, acc):
        start = pl.multiple_of(step * key_block, key_block)
        k = kv_ref[pl.ds(start, key_block), :HD]
        v = kv_ref[pl.ds(start, key_block), HD:]
        s = lax.dot_general(q, k, (((1,), (1,)), ((), ())), preferred_element_type=jnp.float32) * (SCALE * LOG2E)
        w = jnp.exp2(s - lse)
        gw = lax.dot_general(g, v, (((1,), (1,)), ((), ())), preferred_element_type=jnp.float32)
        gs = (w * (gw - delta)).astype(jnp.bfloat16)
        return acc + jnp.dot(gs, k, preferred_element_type=jnp.float32)

    acc = lax.fori_loop(0, steps, body, jnp.zeros(dq_ref.shape, jnp.float32), unroll=4)
    dq_ref[...] = rotate_back_rows(acc * SCALE, cos_ref, sin_ref).astype(dq_ref.dtype)


def attention_query_grad(q, g, lse_col, delta_col, kv_all, cos_wide, sin_wide, query_block=512, key_block=1024):
    rows = q.shape[0]
    keys = kv_all.shape[0]
    cost = pl.CostEstimate(
        flops=6 * rows * keys * HD, transcendentals=rows * keys, bytes_accessed=2 * HD * (3 * rows + 2 * keys)
    )
    row_spec = pl.BlockSpec((query_block, HD), lambda i: (i, 0))
    col_spec = pl.BlockSpec((query_block, 1), lambda i: (i, 0))
    whole = pl.BlockSpec((keys, 2 * HD), lambda i: (0, 0))
    return pl.pallas_call(
        functools.partial(query_grad_kernel, key_block),
        grid=(rows // query_block,),
        in_specs=[row_spec, row_spec, col_spec, col_spec, whole, row_spec, row_spec],
        out_specs=pl.BlockSpec((query_block, HD), lambda i: (i, 0)),
        out_shape=jax.ShapeDtypeStruct((rows, HD), jnp.bfloat16),
        compiler_params=pltpu.CompilerParams(dimension_semantics=("arbitrary",)),
        cost_estimate=cost,
    )(q, g, lse_col, delta_col, kv_all, cos_wide, sin_wide)


def stat_row(tile, stat, halves):
    parts = []
    for half in range(halves):
        row = stat * halves + half
        step = 2 * halves
        parts.append((tile[row : row + 1] + tile[step + row : step + row + 1]) + tile[2 * step + row : 2 * step + row + 1])
    return jnp.concatenate(parts, axis=1)


def key_grad_kernel(query_block, block_stride, blocks, k_ref, v_ref, qg_ref, cos_ref, sin_ref, dk_ref, dv_ref):
    k = k_ref[...]
    v = v_ref[...]
    steps = blocks
    halves = query_block // (2 * HD)

    def body(step, carry):
        dk, dv = carry
        start = pl.multiple_of(step * block_stride, 16)
        q = qg_ref[pl.ds(start, query_block), :HD]
        g = qg_ref[pl.ds(start, query_block), HD:]
        tile = qg_ref[pl.ds(start + query_block, 16), :].astype(jnp.float32)
        lse = stat_row(tile, 0, halves)
        delta = stat_row(tile, 1, halves)
        s = lax.dot_general(k, q, (((1,), (1,)), ((), ())), preferred_element_type=jnp.float32) * (SCALE * LOG2E)
        w = jnp.exp2(s - lse * LOG2E)
        gw = lax.dot_general(v, g, (((1,), (1,)), ((), ())), preferred_element_type=jnp.float32)
        gs = (w * (gw - delta)).astype(jnp.bfloat16)
        dk = dk + jnp.dot(gs, q, preferred_element_type=jnp.float32)
        dv = dv + jnp.dot(w.astype(jnp.bfloat16), g, preferred_element_type=jnp.float32)
        return dk, dv

    zero = jnp.zeros(dk_ref.shape, jnp.float32)
    dk, dv = lax.fori_loop(0, steps, body, (zero, zero), unroll=4)
    dk_ref[...] = rotate_back_rows(dk * SCALE, cos_ref, sin_ref).astype(dk_ref.dtype)
    dv_ref[...] = dv.astype(dv_ref.dtype)


def attention_key_grad(k, v, qg_all, cos_wide, sin_wide, query_block, block_stride, key_rows=512):
    rows = k.shape[0]
    blocks = qg_all.shape[0] // block_stride
    queries = blocks * query_block
    cost = pl.CostEstimate(
        flops=8 * rows * queries * HD, transcendentals=rows * queries, bytes_accessed=2 * HD * (2 * rows + 2 * queries)
    )
    row_spec = pl.BlockSpec((key_rows, HD), lambda i: (i, 0))
    whole = pl.BlockSpec(qg_all.shape, lambda i: (0, 0))
    return pl.pallas_call(
        functools.partial(key_grad_kernel, query_block, block_stride, blocks),
        grid=(rows // key_rows,),
        in_specs=[row_spec, row_spec, whole, row_spec, row_spec],
        out_specs=[row_spec, row_spec],
        out_shape=[jax.ShapeDtypeStruct((rows, HD), jnp.bfloat16)] * 2,
        compiler_params=pltpu.CompilerParams(dimension_semantics=("arbitrary",)),
        cost_estimate=cost,
    )(k, v, qg_all, cos_wide, sin_wide)


def shifted(value, axis, steps):
    count = lax.axis_size(axis)
    initial, last = (max(0, -steps), min(count, count - steps))
    return lax.ppermute(value, axis, [(source, source + steps) for source in range(initial, last)])


def frequencies(pair_count):
    return 1.0 / 10000.0 ** (jnp.arange(pair_count, dtype=jnp.float32) / pair_count)


def rope_tables(frame_pos, cell_ids):
    pair_count = HD // 2
    part_side = pair_count // 3
    part_time = pair_count - 2 * part_side
    grid_row = (cell_ids // GRID_W).astype(jnp.float32)
    grid_col = (cell_ids % GRID_W).astype(jnp.float32)
    angles = jnp.concatenate(
        [
            frame_pos.astype(jnp.float32)[:, None] * frequencies(part_time)[None, :],
            grid_row[:, None] * frequencies(part_side)[None, :],
            grid_col[:, None] * frequencies(part_side)[None, :],
        ],
        axis=1,
    )
    return (jnp.cos(angles), jnp.sin(angles))


def wide_tables(frame_pos, cell_ids):
    pair_count = HD // 2
    part_side = pair_count // 3
    part_time = pair_count - 2 * part_side
    freq = jnp.repeat(
        jnp.concatenate(
            [frequencies(part_time), frequencies(part_side), frequencies(part_side)]
        ),
        2,
    )
    pair = jnp.arange(HD, dtype=jnp.int32)[None, :] // 2
    grid_row = (cell_ids // GRID_W).astype(jnp.float32)[:, None]
    grid_col = (cell_ids % GRID_W).astype(jnp.float32)[:, None]
    cell_angles = jnp.where(pair < part_time + part_side, grid_row, grid_col) * freq[None, :]
    frame_angles = frame_pos.astype(jnp.float32)[:, None] * freq[None, :]
    frames = frame_angles.shape[0]
    cells = cell_angles.shape[0]
    time_lane = (pair < part_time)[None]
    even = jnp.arange(HD, dtype=jnp.int32)[None, :] % 2 == 0

    def spread(table_fn):
        by_frame = table_fn(frame_angles)[:, None, :]
        by_cell = table_fn(cell_angles)[None, :, :]
        return jnp.where(time_lane, by_frame, by_cell).reshape(frames * cells, HD)

    sin_wide = spread(jnp.sin)
    return (spread(jnp.cos), jnp.where(even, sin_wide, -sin_wide))


def rotate(vectors, cos_table, sin_table, direction):
    layout = vectors.shape
    paired = vectors.reshape(layout[:-1] + (layout[-1] // 2, 2))
    former = paired[..., 0]
    latter = paired[..., 1]
    out_former = former * cos_table - direction * latter * sin_table
    out_latter = direction * former * sin_table + latter * cos_table
    return jnp.stack([out_former, out_latter], axis=-1).reshape(layout)


def tap_mask(frame_clip):
    frame_total = frame_clip.shape[0]
    frame_ids = jnp.arange(frame_total, dtype=jnp.int32)
    columns = []
    for offset in range(3):
        target = frame_ids + offset
        inside = target < frame_total
        same_clip = frame_clip[jnp.minimum(target, frame_total - 1)] == frame_clip
        columns.append(jnp.logical_and(inside, same_clip).astype(jnp.float32))
    return jnp.stack(columns, axis=1)


def split_exact(values):
    high = lax.reduce_precision(values, exponent_bits=8, mantissa_bits=7)
    rest = values - high
    middle = lax.reduce_precision(rest, exponent_bits=8, mantissa_bits=7)
    low = rest - middle
    return jnp.stack([high, middle, low]).astype(jnp.bfloat16)


def cross(left, right):
    return lax.dot_general(
        left, right, (((1,), (1,)), ((), ())), preferred_element_type=jnp.float32
    )


def inner(left, right):
    return lax.dot_general(
        left, right, (((0,), (0,)), ((), ())), preferred_element_type=jnp.float32
    )


def on_device(
    queries, keys, values, token_cell, head_weight, norm_gain, time_weight, frame_clip, cotangent
):
    score_scale = HD ** (-0.5)
    tok_local = queries.shape[0]
    slab_cells = token_cell.shape[0]
    span_frames = cotangent.shape[0]
    channels = head_weight.shape[2]
    frame_pos = jnp.arange(tok_local, dtype=jnp.int32) // slab_cells
    cell_ids = jnp.tile(token_cell, tok_local // slab_cells)
    cos_wide, sin_wide = wide_tables(
        jnp.arange(tok_local // slab_cells, dtype=jnp.int32), token_cell
    )
    rot_q, pair = prepare(queries[:, 0, :], keys[:, 0, :], values[:, 0, :], cos_wide, -sin_wide)
    pair_all = lax.all_gather(pair, "seq", axis=0, tiled=True)
    all_weights = lax.all_gather(head_weight[0], "tm", axis=0, tiled=False)
    rot_k = pair[:, :HD]
    plain_v = values[:, 0, :]
    attended, log_col, projected = attention_forward(rot_q, pair_all, head_weight[0])
    log_total = log_col[:, 0]
    span_rows = span_frames * slab_cells
    head_count = lax.axis_size("tm")
    exchanged = lax.all_to_all(
        projected.reshape(head_count, span_frames * slab_cells, channels), "tm", 0, 0, tiled=False
    )
    mixed = jnp.sum(exchanged.astype(jnp.float32), axis=0).reshape(
        span_frames, slab_cells, channels
    )
    inverse = lax.rsqrt(jnp.mean(mixed * mixed, axis=2, keepdims=True) + 1e-06)
    normed = mixed * inverse * norm_gain
    mask_table = tap_mask(frame_clip)
    first_frame = lax.axis_index("tm") * span_frames
    local_mask = lax.dynamic_slice_in_dim(mask_table, first_frame, span_frames, 0)
    following = shifted(cotangent, "tm", -1)
    extended = jnp.concatenate([cotangent, following], axis=0)
    grad_act = jnp.zeros((span_frames, slab_cells, channels), jnp.float32)
    for offset in range(3):
        term = jnp.einsum(
            "fco,io->fci",
            extended[offset : offset + span_frames],
            time_weight[offset],
            preferred_element_type=jnp.float32,
        )
        grad_act = grad_act + local_mask[:, offset][:, None, None] * term
    sigmoid_n = jax.nn.sigmoid(normed)
    grad_normed = grad_act * sigmoid_n * (1.0 + normed * (1.0 - sigmoid_n))
    gained = grad_normed * norm_gain
    grad_mixed = (
        inverse * gained
        - inverse * inverse * inverse * mixed * jnp.mean(gained * mixed, axis=2, keepdims=True)
    ).astype(jnp.bfloat16)
    grad_mixed = grad_mixed.reshape(span_rows, channels)
    grad_heads = jnp.einsum(
        "re,hde->hrd", grad_mixed, all_weights, preferred_element_type=jnp.float32
    ).astype(jnp.bfloat16)
    grad_out = lax.all_to_all(grad_heads, "tm", 0, 0, tiled=False).reshape(tok_local, HD)
    row_delta = jnp.sum(grad_out.astype(jnp.float32) * attended.astype(jnp.float32), axis=1)

    grad_q = attention_query_grad(
        rot_q, grad_out, log_col, row_delta[:, None], pair_all, cos_wide, sin_wide
    )
    stat_rows = split_exact(jnp.stack([log_total, row_delta]))
    stat_rows = stat_rows.reshape(-1, 2 * HD)
    stat_pad = (-stat_rows.shape[0]) % 16
    stat_rows = jnp.pad(stat_rows, ((0, stat_pad), (0, 0)))
    packed = jnp.concatenate([jnp.concatenate([rot_q, grad_out], axis=1), stat_rows], axis=0)
    block_rows = packed.shape[0]
    seq_count = lax.axis_size("seq")
    gathered = lax.all_gather(packed, "seq", axis=0, tiled=True).reshape(
        seq_count, block_rows, 2 * HD
    )
    grad_k, grad_v = attention_key_grad(
        rot_k,
        plain_v,
        gathered.reshape(seq_count * block_rows, 2 * HD),
        cos_wide,
        sin_wide,
        tok_local,
        block_rows,
    )
    grad_queries = grad_q[:, None, :]
    grad_keys = grad_k[:, None, :]
    grad_values = grad_v[:, None, :]
    return (grad_queries, grad_keys, grad_values)


def solution(mesh):
    in_specs = (
        P(("dp", "seq"), "tm", None),
        P(("dp", "seq"), "tm", None),
        P(("dp", "seq"), "tm", None),
        P("seq"),
        P("tm", None, None),
        P(),
        P(),
        P("dp"),
        P(("dp", "tm"), "seq", None),
    )
    out_specs = (
        P(("dp", "seq"), "tm", None),
        P(("dp", "seq"), "tm", None),
        P(("dp", "seq"), "tm", None),
    )
    return jax.shard_map(
        on_device, mesh=mesh, in_specs=in_specs, out_specs=out_specs, check_vma=False
    )
```

```python
import functools
import math

import jax
import jax.numpy as jnp
from jax import lax
from jax.experimental import pallas as pl
from jax.experimental.pallas import tpu as pltpu
from jax.sharding import PartitionSpec as P

HD = 128
GRID_W = 32
SCALE = HD ** (-0.5)
LOG2E = 1.4426950408889634
LN2 = 0.6931471805599453


def rotate_back_rows(x, cos_ref, sin_ref):
    lanes = lax.broadcasted_iota(jnp.int32, x.shape, 1)
    ahead = pltpu.roll(x, x.shape[1] - 1, 1)
    behind = pltpu.roll(x, 1, 1)
    ahead_lane = pltpu.roll(lanes, x.shape[1] - 1, 1)
    partner_lane = jnp.where(lanes % 2 == 0, lanes + 1, lanes - 1)
    partner = jnp.where(ahead_lane == partner_lane, ahead, behind)
    return x * cos_ref[...] + partner * sin_ref[...]


def rotate_kernel(q_ref, cos_ref, sin_ref, rq_ref):
    rq_ref[...] = rotate_back_rows(q_ref[...].astype(jnp.float32), cos_ref, sin_ref).astype(
        rq_ref.dtype
    )


def pair_kernel(k_ref, v_ref, cos_ref, sin_ref, kv_ref):
    kv_ref[:, :HD] = rotate_back_rows(k_ref[...].astype(jnp.float32), cos_ref, sin_ref).astype(
        kv_ref.dtype
    )
    kv_ref[:, HD:] = v_ref[...]


def prepare(q, k, v, cos_wide, sin_forward):
    rows = q.shape[0]
    pair = pl.pallas_call(
        pair_kernel,
        out_shape=jax.ShapeDtypeStruct((rows, 2 * HD), jnp.bfloat16),
        cost_estimate=pl.CostEstimate(flops=4 * rows * HD, transcendentals=0, bytes_accessed=16 * rows * HD),
    )(k, v, cos_wide, sin_forward)
    rot_q = pl.pallas_call(
        rotate_kernel,
        out_shape=jax.ShapeDtypeStruct((rows, HD), jnp.bfloat16),
        cost_estimate=pl.CostEstimate(flops=4 * rows * HD, transcendentals=0, bytes_accessed=12 * rows * HD),
    )(q, cos_wide, sin_forward)
    return rot_q, pair


def forward_kernel(key_block, q_ref, kv_ref, w_ref, out_ref, lse_ref, proj_ref):
    q = q_ref[...]
    rows = q.shape[0]
    steps = kv_ref.shape[0] // key_block

    def body(step, carry):
        top, total, acc = carry
        start = pl.multiple_of(step * key_block, key_block)
        k = kv_ref[pl.ds(start, key_block), :HD]
        v = kv_ref[pl.ds(start, key_block), HD:]
        s = lax.dot_general(q, k, (((1,), (1,)), ((), ())), preferred_element_type=jnp.float32) * (SCALE * LOG2E)
        new_top = jnp.maximum(top, jnp.max(s, axis=1, keepdims=True))
        factor = jnp.exp2(top - new_top)
        w = jnp.exp2(s - new_top)
        total = total * factor + jnp.sum(w, axis=1, keepdims=True)
        acc = acc * factor + jnp.dot(w.astype(jnp.bfloat16), v, preferred_element_type=jnp.float32)
        return new_top, total, acc

    start_state = (
        jnp.full((rows, 1), -1e30, jnp.float32),
        jnp.zeros((rows, 1), jnp.float32),
        jnp.zeros((rows, HD), jnp.float32),
    )
    top, total, acc = lax.fori_loop(0, steps, body, start_state, unroll=4)
    attended = (acc / total).astype(out_ref.dtype)
    out_ref[...] = attended
    proj_ref[...] = jnp.dot(attended, w_ref[...], preferred_element_type=jnp.float32).astype(
        proj_ref.dtype
    )
    lse_ref[...] = top * LN2 + jnp.log(total)


def attention_forward(q, kv_all, weight, query_block=512, key_block=2048):
    rows = q.shape[0]
    keys = kv_all.shape[0]
    cost = pl.CostEstimate(
        flops=4 * rows * keys * HD, transcendentals=rows * keys, bytes_accessed=2 * HD * (2 * rows + 2 * keys)
    )
    return pl.pallas_call(
        functools.partial(forward_kernel, key_block),
        grid=(rows // query_block,),
        in_specs=[
            pl.BlockSpec((query_block, HD), lambda i: (i, 0)),
            pl.BlockSpec((keys, 2 * HD), lambda i: (0, 0)),
            pl.BlockSpec(weight.shape, lambda i: (0, 0)),
        ],
        out_specs=[
            pl.BlockSpec((query_block, HD), lambda i: (i, 0)),
            pl.BlockSpec((query_block, 1), lambda i: (i, 0)),
            pl.BlockSpec((query_block, weight.shape[1]), lambda i: (i, 0)),
        ],
        out_shape=[
            jax.ShapeDtypeStruct((rows, HD), jnp.bfloat16),
            jax.ShapeDtypeStruct((rows, 1), jnp.float32),
            jax.ShapeDtypeStruct((rows, weight.shape[1]), jnp.bfloat16),
        ],
        compiler_params=pltpu.CompilerParams(dimension_semantics=("arbitrary",)),
        cost_estimate=cost,
    )(q, kv_all, weight)


def query_grad_kernel(key_block, q_ref, g_ref, lse_ref, delta_ref, kv_ref, cos_ref, sin_ref, dq_ref):
    q = q_ref[...]
    g = g_ref[...]
    lse = lse_ref[...] * LOG2E
    delta = delta_ref[...]
    steps = kv_ref.shape[0] // key_block

    def body(step, acc):
        start = pl.multiple_of(step * key_block, key_block)
        k = kv_ref[pl.ds(start, key_block), :HD]
        v = kv_ref[pl.ds(start, key_block), HD:]
        s = lax.dot_general(q, k, (((1,), (1,)), ((), ())), preferred_element_type=jnp.float32) * (SCALE * LOG2E)
        w = jnp.exp2(s - lse)
        gw = lax.dot_general(g, v, (((1,), (1,)), ((), ())), preferred_element_type=jnp.float32)
        gs = (w * (gw - delta)).astype(jnp.bfloat16)
        return acc + jnp.dot(gs, k, preferred_element_type=jnp.float32)

    acc = lax.fori_loop(0, steps, body, jnp.zeros(dq_ref.shape, jnp.float32), unroll=4)
    dq_ref[...] = rotate_back_rows(acc * SCALE, cos_ref, sin_ref).astype(dq_ref.dtype)


def attention_query_grad(q, g, lse_col, delta_col, kv_all, cos_wide, sin_wide, query_block=512, key_block=1024):
    rows = q.shape[0]
    keys = kv_all.shape[0]
    cost = pl.CostEstimate(
        flops=6 * rows * keys * HD, transcendentals=rows * keys, bytes_accessed=2 * HD * (3 * rows + 2 * keys)
    )
    row_spec = pl.BlockSpec((query_block, HD), lambda i: (i, 0))
    col_spec = pl.BlockSpec((query_block, 1), lambda i: (i, 0))
    whole = pl.BlockSpec((keys, 2 * HD), lambda i: (0, 0))
    return pl.pallas_call(
        functools.partial(query_grad_kernel, key_block),
        grid=(rows // query_block,),
        in_specs=[row_spec, row_spec, col_spec, col_spec, whole, row_spec, row_spec],
        out_specs=pl.BlockSpec((query_block, HD), lambda i: (i, 0)),
        out_shape=jax.ShapeDtypeStruct((rows, HD), jnp.bfloat16),
        compiler_params=pltpu.CompilerParams(dimension_semantics=("arbitrary",)),
        cost_estimate=cost,
    )(q, g, lse_col, delta_col, kv_all, cos_wide, sin_wide)


def stat_row(tile, stat, halves):
    parts = []
    for half in range(halves):
        row = stat * halves + half
        step = 2 * halves
        parts.append((tile[row : row + 1] + tile[step + row : step + row + 1]) + tile[2 * step + row : 2 * step + row + 1])
    return jnp.concatenate(parts, axis=1)


def key_grad_kernel(query_block, block_stride, blocks, k_ref, v_ref, qg_ref, cos_ref, sin_ref, dk_ref, dv_ref):
    k = k_ref[...]
    v = v_ref[...]
    steps = blocks
    halves = query_block // (2 * HD)

    def body(step, carry):
        dk, dv = carry
        start = pl.multiple_of(step * block_stride, 16)
        q = qg_ref[pl.ds(start, query_block), :HD]
        g = qg_ref[pl.ds(start, query_block), HD:]
        tile = qg_ref[pl.ds(start + query_block, 16), :].astype(jnp.float32)
        lse = stat_row(tile, 0, halves)
        delta = stat_row(tile, 1, halves)
        s = lax.dot_general(k, q, (((1,), (1,)), ((), ())), preferred_element_type=jnp.float32) * (SCALE * LOG2E)
        w = jnp.exp2(s - lse * LOG2E)
        gw = lax.dot_general(v, g, (((1,), (1,)), ((), ())), preferred_element_type=jnp.float32)
        gs = (w * (gw - delta)).astype(jnp.bfloat16)
        dk = dk + jnp.dot(gs, q, preferred_element_type=jnp.float32)
        dv = dv + jnp.dot(w.astype(jnp.bfloat16), g, preferred_element_type=jnp.float32)
        return dk, dv

    zero = jnp.zeros(dk_ref.shape, jnp.float32)
    dk, dv = lax.fori_loop(0, steps, body, (zero, zero), unroll=8)
    dk_ref[...] = rotate_back_rows(dk * SCALE, cos_ref, sin_ref).astype(dk_ref.dtype)
    dv_ref[...] = dv.astype(dv_ref.dtype)


def attention_key_grad(k, v, qg_all, cos_wide, sin_wide, query_block, block_stride, key_rows=512):
    rows = k.shape[0]
    blocks = qg_all.shape[0] // block_stride
    queries = blocks * query_block
    cost = pl.CostEstimate(
        flops=8 * rows * queries * HD, transcendentals=rows * queries, bytes_accessed=2 * HD * (2 * rows + 2 * queries)
    )
    row_spec = pl.BlockSpec((key_rows, HD), lambda i: (i, 0))
    whole = pl.BlockSpec(qg_all.shape, lambda i: (0, 0))
    return pl.pallas_call(
        functools.partial(key_grad_kernel, query_block, block_stride, blocks),
        grid=(rows // key_rows,),
        in_specs=[row_spec, row_spec, whole, row_spec, row_spec],
        out_specs=[row_spec, row_spec],
        out_shape=[jax.ShapeDtypeStruct((rows, HD), jnp.bfloat16)] * 2,
        compiler_params=pltpu.CompilerParams(dimension_semantics=("arbitrary",)),
        cost_estimate=cost,
    )(k, v, qg_all, cos_wide, sin_wide)


def shifted(value, axis, steps):
    count = lax.axis_size(axis)
    initial, last = (max(0, -steps), min(count, count - steps))
    return lax.ppermute(value, axis, [(source, source + steps) for source in range(initial, last)])


def frequencies(pair_count):
    return 1.0 / 10000.0 ** (jnp.arange(pair_count, dtype=jnp.float32) / pair_count)


def rope_tables(frame_pos, cell_ids):
    pair_count = HD // 2
    part_side = pair_count // 3
    part_time = pair_count - 2 * part_side
    grid_row = (cell_ids // GRID_W).astype(jnp.float32)
    grid_col = (cell_ids % GRID_W).astype(jnp.float32)
    angles = jnp.concatenate(
        [
            frame_pos.astype(jnp.float32)[:, None] * frequencies(part_time)[None, :],
            grid_row[:, None] * frequencies(part_side)[None, :],
            grid_col[:, None] * frequencies(part_side)[None, :],
        ],
        axis=1,
    )
    return (jnp.cos(angles), jnp.sin(angles))


def wide_tables(frame_pos, cell_ids):
    pair_count = HD // 2
    part_side = pair_count // 3
    part_time = pair_count - 2 * part_side
    freq = jnp.repeat(
        jnp.concatenate(
            [frequencies(part_time), frequencies(part_side), frequencies(part_side)]
        ),
        2,
    )
    pair = jnp.arange(HD, dtype=jnp.int32)[None, :] // 2
    grid_row = (cell_ids // GRID_W).astype(jnp.float32)[:, None]
    grid_col = (cell_ids % GRID_W).astype(jnp.float32)[:, None]
    cell_angles = jnp.where(pair < part_time + part_side, grid_row, grid_col) * freq[None, :]
    frame_angles = frame_pos.astype(jnp.float32)[:, None] * freq[None, :]
    frames = frame_angles.shape[0]
    cells = cell_angles.shape[0]
    time_lane = (pair < part_time)[None]
    even = jnp.arange(HD, dtype=jnp.int32)[None, :] % 2 == 0

    def spread(table_fn):
        by_frame = table_fn(frame_angles)[:, None, :]
        by_cell = table_fn(cell_angles)[None, :, :]
        return jnp.where(time_lane, by_frame, by_cell).reshape(frames * cells, HD)

    sin_wide = spread(jnp.sin)
    return (spread(jnp.cos), jnp.where(even, sin_wide, -sin_wide))


def rotate(vectors, cos_table, sin_table, direction):
    layout = vectors.shape
    paired = vectors.reshape(layout[:-1] + (layout[-1] // 2, 2))
    former = paired[..., 0]
    latter = paired[..., 1]
    out_former = former * cos_table - direction * latter * sin_table
    out_latter = direction * former * sin_table + latter * cos_table
    return jnp.stack([out_former, out_latter], axis=-1).reshape(layout)


def tap_mask(frame_clip):
    frame_total = frame_clip.shape[0]
    frame_ids = jnp.arange(frame_total, dtype=jnp.int32)
    columns = []
    for offset in range(3):
        target = frame_ids + offset
        inside = target < frame_total
        same_clip = frame_clip[jnp.minimum(target, frame_total - 1)] == frame_clip
        columns.append(jnp.logical_and(inside, same_clip).astype(jnp.float32))
    return jnp.stack(columns, axis=1)


def split_exact(values):
    high = lax.reduce_precision(values, exponent_bits=8, mantissa_bits=7)
    rest = values - high
    middle = lax.reduce_precision(rest, exponent_bits=8, mantissa_bits=7)
    low = rest - middle
    return jnp.stack([high, middle, low]).astype(jnp.bfloat16)


def cross(left, right):
    return lax.dot_general(
        left, right, (((1,), (1,)), ((), ())), preferred_element_type=jnp.float32
    )


def inner(left, right):
    return lax.dot_general(
        left, right, (((0,), (0,)), ((), ())), preferred_element_type=jnp.float32
    )


def on_device(
    queries, keys, values, token_cell, head_weight, norm_gain, time_weight, frame_clip, cotangent
):
    score_scale = HD ** (-0.5)
    tok_local = queries.shape[0]
    slab_cells = token_cell.shape[0]
    span_frames = cotangent.shape[0]
    channels = head_weight.shape[2]
    frame_pos = jnp.arange(tok_local, dtype=jnp.int32) // slab_cells
    cell_ids = jnp.tile(token_cell, tok_local // slab_cells)
    cos_wide, sin_wide = wide_tables(
        jnp.arange(tok_local // slab_cells, dtype=jnp.int32), token_cell
    )
    rot_q, pair = prepare(queries[:, 0, :], keys[:, 0, :], values[:, 0, :], cos_wide, -sin_wide)
    pair_all = lax.all_gather(pair, "seq", axis=0, tiled=True)
    all_weights = lax.all_gather(head_weight[0], "tm", axis=0, tiled=False)
    rot_k = pair[:, :HD]
    plain_v = values[:, 0, :]
    attended, log_col, projected = attention_forward(rot_q, pair_all, head_weight[0])
    log_total = log_col[:, 0]
    span_rows = span_frames * slab_cells
    head_count = lax.axis_size("tm")
    exchanged = lax.all_to_all(
        projected.reshape(head_count, span_frames * slab_cells, channels), "tm", 0, 0, tiled=False
    )
    mixed = jnp.sum(exchanged.astype(jnp.float32), axis=0).reshape(
        span_frames, slab_cells, channels
    )
    inverse = lax.rsqrt(jnp.mean(mixed * mixed, axis=2, keepdims=True) + 1e-06)
    normed = mixed * inverse * norm_gain
    mask_table = tap_mask(frame_clip)
    first_frame = lax.axis_index("tm") * span_frames
    local_mask = lax.dynamic_slice_in_dim(mask_table, first_frame, span_frames, 0)
    following = shifted(cotangent, "tm", -1)
    extended = jnp.concatenate([cotangent, following], axis=0)
    grad_act = jnp.zeros((span_frames, slab_cells, channels), jnp.float32)
    for offset in range(3):
        term = jnp.einsum(
            "fco,io->fci",
            extended[offset : offset + span_frames],
            time_weight[offset],
            preferred_element_type=jnp.float32,
        )
        grad_act = grad_act + local_mask[:, offset][:, None, None] * term
    sigmoid_n = jax.nn.sigmoid(normed)
    grad_normed = grad_act * sigmoid_n * (1.0 + normed * (1.0 - sigmoid_n))
    gained = grad_normed * norm_gain
    grad_mixed = (
        inverse * gained
        - inverse * inverse * inverse * mixed * jnp.mean(gained * mixed, axis=2, keepdims=True)
    ).astype(jnp.bfloat16)
    grad_mixed = grad_mixed.reshape(span_rows, channels)
    grad_heads = jnp.einsum(
        "re,hde->hrd", grad_mixed, all_weights, preferred_element_type=jnp.float32
    ).astype(jnp.bfloat16)
    grad_out = lax.all_to_all(grad_heads, "tm", 0, 0, tiled=False).reshape(tok_local, HD)
    row_delta = jnp.sum(grad_out.astype(jnp.float32) * attended.astype(jnp.float32), axis=1)

    grad_q = attention_query_grad(
        rot_q, grad_out, log_col, row_delta[:, None], pair_all, cos_wide, sin_wide
    )
    stat_rows = split_exact(jnp.stack([log_total, row_delta]))
    stat_rows = stat_rows.reshape(-1, 2 * HD)
    stat_pad = (-stat_rows.shape[0]) % 16
    stat_rows = jnp.pad(stat_rows, ((0, stat_pad), (0, 0)))
    packed = jnp.concatenate([jnp.concatenate([rot_q, grad_out], axis=1), stat_rows], axis=0)
    block_rows = packed.shape[0]
    seq_count = lax.axis_size("seq")
    gathered = lax.all_gather(packed, "seq", axis=0, tiled=True).reshape(
        seq_count, block_rows, 2 * HD
    )
    grad_k, grad_v = attention_key_grad(
        rot_k,
        plain_v,
        gathered.reshape(seq_count * block_rows, 2 * HD),
        cos_wide,
        sin_wide,
        tok_local,
        block_rows,
    )
    grad_queries = grad_q[:, None, :]
    grad_keys = grad_k[:, None, :]
    grad_values = grad_v[:, None, :]
    return (grad_queries, grad_keys, grad_values)


def solution(mesh):
    in_specs = (
        P(("dp", "seq"), "tm", None),
        P(("dp", "seq"), "tm", None),
        P(("dp", "seq"), "tm", None),
        P("seq"),
        P("tm", None, None),
        P(),
        P(),
        P("dp"),
        P(("dp", "tm"), "seq", None),
    )
    out_specs = (
        P(("dp", "seq"), "tm", None),
        P(("dp", "seq"), "tm", None),
        P(("dp", "seq"), "tm", None),
    )
    return jax.shard_map(
        on_device, mesh=mesh, in_specs=in_specs, out_specs=out_specs, check_vma=False
    )
```

```python
import functools
import math

import jax
import jax.numpy as jnp
from jax import lax
from jax.experimental import pallas as pl
from jax.experimental.pallas import tpu as pltpu
from jax.sharding import PartitionSpec as P

HD = 128
GRID_W = 32
SCALE = HD ** (-0.5)
LOG2E = 1.4426950408889634
LN2 = 0.6931471805599453


def rotate_back_rows(x, cos_ref, sin_ref):
    lanes = lax.broadcasted_iota(jnp.int32, x.shape, 1)
    ahead = pltpu.roll(x, x.shape[1] - 1, 1)
    behind = pltpu.roll(x, 1, 1)
    ahead_lane = pltpu.roll(lanes, x.shape[1] - 1, 1)
    partner_lane = jnp.where(lanes % 2 == 0, lanes + 1, lanes - 1)
    partner = jnp.where(ahead_lane == partner_lane, ahead, behind)
    return x * cos_ref[...] + partner * sin_ref[...]


def rotate_kernel(q_ref, cos_ref, sin_ref, rq_ref):
    rq_ref[...] = rotate_back_rows(q_ref[...].astype(jnp.float32), cos_ref, sin_ref).astype(
        rq_ref.dtype
    )


def pair_kernel(k_ref, v_ref, cos_ref, sin_ref, kv_ref):
    kv_ref[:, :HD] = rotate_back_rows(k_ref[...].astype(jnp.float32), cos_ref, sin_ref).astype(
        kv_ref.dtype
    )
    kv_ref[:, HD:] = v_ref[...]


def prepare(q, k, v, cos_wide, sin_forward):
    rows = q.shape[0]
    pair = pl.pallas_call(
        pair_kernel,
        out_shape=jax.ShapeDtypeStruct((rows, 2 * HD), jnp.bfloat16),
        cost_estimate=pl.CostEstimate(flops=4 * rows * HD, transcendentals=0, bytes_accessed=16 * rows * HD),
    )(k, v, cos_wide, sin_forward)
    rot_q = pl.pallas_call(
        rotate_kernel,
        out_shape=jax.ShapeDtypeStruct((rows, HD), jnp.bfloat16),
        cost_estimate=pl.CostEstimate(flops=4 * rows * HD, transcendentals=0, bytes_accessed=12 * rows * HD),
    )(q, cos_wide, sin_forward)
    return rot_q, pair


def forward_kernel(key_block, q_ref, kv_ref, w_ref, out_ref, lse_ref, proj_ref):
    q = q_ref[...]
    rows = q.shape[0]
    steps = kv_ref.shape[0] // key_block

    def body(step, carry):
        top, total, acc = carry
        start = pl.multiple_of(step * key_block, key_block)
        k = kv_ref[pl.ds(start, key_block), :HD]
        v = kv_ref[pl.ds(start, key_block), HD:]
        s = lax.dot_general(q, k, (((1,), (1,)), ((), ())), preferred_element_type=jnp.float32) * (SCALE * LOG2E)
        new_top = jnp.maximum(top, jnp.max(s, axis=1, keepdims=True))
        factor = jnp.exp2(top - new_top)
        w = jnp.exp2(s - new_top)
        total = total * factor + jnp.sum(w, axis=1, keepdims=True)
        acc = acc * factor + jnp.dot(w.astype(jnp.bfloat16), v, preferred_element_type=jnp.float32)
        return new_top, total, acc

    start_state = (
        jnp.full((rows, 1), -1e30, jnp.float32),
        jnp.zeros((rows, 1), jnp.float32),
        jnp.zeros((rows, HD), jnp.float32),
    )
    top, total, acc = lax.fori_loop(0, steps, body, start_state, unroll=4)
    attended = (acc / total).astype(out_ref.dtype)
    out_ref[...] = attended
    proj_ref[...] = jnp.dot(attended, w_ref[...], preferred_element_type=jnp.float32).astype(
        proj_ref.dtype
    )
    lse_ref[...] = top * LN2 + jnp.log(total)


def attention_forward(q, kv_all, weight, query_block=512, key_block=2048):
    rows = q.shape[0]
    keys = kv_all.shape[0]
    cost = pl.CostEstimate(
        flops=4 * rows * keys * HD, transcendentals=rows * keys, bytes_accessed=2 * HD * (2 * rows + 2 * keys)
    )
    return pl.pallas_call(
        functools.partial(forward_kernel, key_block),
        grid=(rows // query_block,),
        in_specs=[
            pl.BlockSpec((query_block, HD), lambda i: (i, 0)),
            pl.BlockSpec((keys, 2 * HD), lambda i: (0, 0)),
            pl.BlockSpec(weight.shape, lambda i: (0, 0)),
        ],
        out_specs=[
            pl.BlockSpec((query_block, HD), lambda i: (i, 0)),
            pl.BlockSpec((query_block, 1), lambda i: (i, 0)),
            pl.BlockSpec((query_block, weight.shape[1]), lambda i: (i, 0)),
        ],
        out_shape=[
            jax.ShapeDtypeStruct((rows, HD), jnp.bfloat16),
            jax.ShapeDtypeStruct((rows, 1), jnp.float32),
            jax.ShapeDtypeStruct((rows, weight.shape[1]), jnp.bfloat16),
        ],
        compiler_params=pltpu.CompilerParams(dimension_semantics=("arbitrary",)),
        cost_estimate=cost,
    )(q, kv_all, weight)


def query_grad_kernel(key_block, q_ref, g_ref, lse_ref, delta_ref, kv_ref, cos_ref, sin_ref, dq_ref):
    q = q_ref[...]
    g = g_ref[...]
    lse = lse_ref[...] * LOG2E
    delta = delta_ref[...]
    steps = kv_ref.shape[0] // key_block

    def body(step, acc):
        start = pl.multiple_of(step * key_block, key_block)
        k = kv_ref[pl.ds(start, key_block), :HD]
        v = kv_ref[pl.ds(start, key_block), HD:]
        s = lax.dot_general(q, k, (((1,), (1,)), ((), ())), preferred_element_type=jnp.float32) * (SCALE * LOG2E)
        w = jnp.exp2(s - lse)
        gw = lax.dot_general(g, v, (((1,), (1,)), ((), ())), preferred_element_type=jnp.float32)
        gs = (w * (gw - delta)).astype(jnp.bfloat16)
        return acc + jnp.dot(gs, k, preferred_element_type=jnp.float32)

    acc = lax.fori_loop(0, steps, body, jnp.zeros(dq_ref.shape, jnp.float32), unroll=4)
    dq_ref[...] = rotate_back_rows(acc * SCALE, cos_ref, sin_ref).astype(dq_ref.dtype)


def attention_query_grad(q, g, lse_col, delta_col, kv_all, cos_wide, sin_wide, query_block=512, key_block=1024):
    rows = q.shape[0]
    keys = kv_all.shape[0]
    cost = pl.CostEstimate(
        flops=6 * rows * keys * HD, transcendentals=rows * keys, bytes_accessed=2 * HD * (3 * rows + 2 * keys)
    )
    row_spec = pl.BlockSpec((query_block, HD), lambda i: (i, 0))
    col_spec = pl.BlockSpec((query_block, 1), lambda i: (i, 0))
    whole = pl.BlockSpec((keys, 2 * HD), lambda i: (0, 0))
    return pl.pallas_call(
        functools.partial(query_grad_kernel, key_block),
        grid=(rows // query_block,),
        in_specs=[row_spec, row_spec, col_spec, col_spec, whole, row_spec, row_spec],
        out_specs=pl.BlockSpec((query_block, HD), lambda i: (i, 0)),
        out_shape=jax.ShapeDtypeStruct((rows, HD), jnp.bfloat16),
        compiler_params=pltpu.CompilerParams(dimension_semantics=("arbitrary",)),
        cost_estimate=cost,
    )(q, g, lse_col, delta_col, kv_all, cos_wide, sin_wide)


def stat_row(tile, stat, halves):
    parts = []
    for half in range(halves):
        row = stat * halves + half
        step = 2 * halves
        parts.append((tile[row : row + 1] + tile[step + row : step + row + 1]) + tile[2 * step + row : 2 * step + row + 1])
    return jnp.concatenate(parts, axis=1)


def key_grad_kernel(query_block, block_stride, blocks, k_ref, v_ref, qg_ref, cos_ref, sin_ref, dk_ref, dv_ref):
    k = k_ref[...]
    v = v_ref[...]
    steps = blocks
    halves = query_block // (2 * HD)

    def body(step, carry):
        dk, dv = carry
        start = pl.multiple_of(step * block_stride, 16)
        q = qg_ref[pl.ds(start, query_block), :HD]
        g = qg_ref[pl.ds(start, query_block), HD:]
        tile = qg_ref[pl.ds(start + query_block, 16), :].astype(jnp.float32)
        lse = stat_row(tile, 0, halves)
        delta = stat_row(tile, 1, halves)
        s = lax.dot_general(k, q, (((1,), (1,)), ((), ())), preferred_element_type=jnp.float32) * (SCALE * LOG2E)
        w = jnp.exp2(s - lse * LOG2E)
        gw = lax.dot_general(v, g, (((1,), (1,)), ((), ())), preferred_element_type=jnp.float32)
        gs = (w * (gw - delta)).astype(jnp.bfloat16)
        dk = dk + jnp.dot(gs, q, preferred_element_type=jnp.float32)
        dv = dv + jnp.dot(w.astype(jnp.bfloat16), g, preferred_element_type=jnp.float32)
        return dk, dv

    zero = jnp.zeros(dk_ref.shape, jnp.float32)
    dk, dv = lax.fori_loop(0, steps, body, (zero, zero), unroll=True)
    dk_ref[...] = rotate_back_rows(dk * SCALE, cos_ref, sin_ref).astype(dk_ref.dtype)
    dv_ref[...] = dv.astype(dv_ref.dtype)


def attention_key_grad(k, v, qg_all, cos_wide, sin_wide, query_block, block_stride, key_rows=512):
    rows = k.shape[0]
    blocks = qg_all.shape[0] // block_stride
    queries = blocks * query_block
    cost = pl.CostEstimate(
        flops=8 * rows * queries * HD, transcendentals=rows * queries, bytes_accessed=2 * HD * (2 * rows + 2 * queries)
    )
    row_spec = pl.BlockSpec((key_rows, HD), lambda i: (i, 0))
    whole = pl.BlockSpec(qg_all.shape, lambda i: (0, 0))
    return pl.pallas_call(
        functools.partial(key_grad_kernel, query_block, block_stride, blocks),
        grid=(rows // key_rows,),
        in_specs=[row_spec, row_spec, whole, row_spec, row_spec],
        out_specs=[row_spec, row_spec],
        out_shape=[jax.ShapeDtypeStruct((rows, HD), jnp.bfloat16)] * 2,
        compiler_params=pltpu.CompilerParams(dimension_semantics=("arbitrary",)),
        cost_estimate=cost,
    )(k, v, qg_all, cos_wide, sin_wide)


def shifted(value, axis, steps):
    count = lax.axis_size(axis)
    initial, last = (max(0, -steps), min(count, count - steps))
    return lax.ppermute(value, axis, [(source, source + steps) for source in range(initial, last)])


def frequencies(pair_count):
    return 1.0 / 10000.0 ** (jnp.arange(pair_count, dtype=jnp.float32) / pair_count)


def rope_tables(frame_pos, cell_ids):
    pair_count = HD // 2
    part_side = pair_count // 3
    part_time = pair_count - 2 * part_side
    grid_row = (cell_ids // GRID_W).astype(jnp.float32)
    grid_col = (cell_ids % GRID_W).astype(jnp.float32)
    angles = jnp.concatenate(
        [
            frame_pos.astype(jnp.float32)[:, None] * frequencies(part_time)[None, :],
            grid_row[:, None] * frequencies(part_side)[None, :],
            grid_col[:, None] * frequencies(part_side)[None, :],
        ],
        axis=1,
    )
    return (jnp.cos(angles), jnp.sin(angles))


def wide_tables(frame_pos, cell_ids):
    pair_count = HD // 2
    part_side = pair_count // 3
    part_time = pair_count - 2 * part_side
    freq = jnp.repeat(
        jnp.concatenate(
            [frequencies(part_time), frequencies(part_side), frequencies(part_side)]
        ),
        2,
    )
    pair = jnp.arange(HD, dtype=jnp.int32)[None, :] // 2
    grid_row = (cell_ids // GRID_W).astype(jnp.float32)[:, None]
    grid_col = (cell_ids % GRID_W).astype(jnp.float32)[:, None]
    cell_angles = jnp.where(pair < part_time + part_side, grid_row, grid_col) * freq[None, :]
    frame_angles = frame_pos.astype(jnp.float32)[:, None] * freq[None, :]
    frames = frame_angles.shape[0]
    cells = cell_angles.shape[0]
    time_lane = (pair < part_time)[None]
    even = jnp.arange(HD, dtype=jnp.int32)[None, :] % 2 == 0

    def spread(table_fn):
        by_frame = table_fn(frame_angles)[:, None, :]
        by_cell = table_fn(cell_angles)[None, :, :]
        return jnp.where(time_lane, by_frame, by_cell).reshape(frames * cells, HD)

    sin_wide = spread(jnp.sin)
    return (spread(jnp.cos), jnp.where(even, sin_wide, -sin_wide))


def rotate(vectors, cos_table, sin_table, direction):
    layout = vectors.shape
    paired = vectors.reshape(layout[:-1] + (layout[-1] // 2, 2))
    former = paired[..., 0]
    latter = paired[..., 1]
    out_former = former * cos_table - direction * latter * sin_table
    out_latter = direction * former * sin_table + latter * cos_table
    return jnp.stack([out_former, out_latter], axis=-1).reshape(layout)


def tap_mask(frame_clip):
    frame_total = frame_clip.shape[0]
    frame_ids = jnp.arange(frame_total, dtype=jnp.int32)
    columns = []
    for offset in range(3):
        target = frame_ids + offset
        inside = target < frame_total
        same_clip = frame_clip[jnp.minimum(target, frame_total - 1)] == frame_clip
        columns.append(jnp.logical_and(inside, same_clip).astype(jnp.float32))
    return jnp.stack(columns, axis=1)


def split_exact(values):
    high = lax.reduce_precision(values, exponent_bits=8, mantissa_bits=7)
    rest = values - high
    middle = lax.reduce_precision(rest, exponent_bits=8, mantissa_bits=7)
    low = rest - middle
    return jnp.stack([high, middle, low]).astype(jnp.bfloat16)


def cross(left, right):
    return lax.dot_general(
        left, right, (((1,), (1,)), ((), ())), preferred_element_type=jnp.float32
    )


def inner(left, right):
    return lax.dot_general(
        left, right, (((0,), (0,)), ((), ())), preferred_element_type=jnp.float32
    )


def on_device(
    queries, keys, values, token_cell, head_weight, norm_gain, time_weight, frame_clip, cotangent
):
    score_scale = HD ** (-0.5)
    tok_local = queries.shape[0]
    slab_cells = token_cell.shape[0]
    span_frames = cotangent.shape[0]
    channels = head_weight.shape[2]
    frame_pos = jnp.arange(tok_local, dtype=jnp.int32) // slab_cells
    cell_ids = jnp.tile(token_cell, tok_local // slab_cells)
    cos_wide, sin_wide = wide_tables(
        jnp.arange(tok_local // slab_cells, dtype=jnp.int32), token_cell
    )
    rot_q, pair = prepare(queries[:, 0, :], keys[:, 0, :], values[:, 0, :], cos_wide, -sin_wide)
    pair_all = lax.all_gather(pair, "seq", axis=0, tiled=True)
    all_weights = lax.all_gather(head_weight[0], "tm", axis=0, tiled=False)
    rot_k = pair[:, :HD]
    plain_v = values[:, 0, :]
    attended, log_col, projected = attention_forward(rot_q, pair_all, head_weight[0])
    log_total = log_col[:, 0]
    span_rows = span_frames * slab_cells
    head_count = lax.axis_size("tm")
    exchanged = lax.all_to_all(
        projected.reshape(head_count, span_frames * slab_cells, channels), "tm", 0, 0, tiled=False
    )
    mixed = jnp.sum(exchanged.astype(jnp.float32), axis=0).reshape(
        span_frames, slab_cells, channels
    )
    inverse = lax.rsqrt(jnp.mean(mixed * mixed, axis=2, keepdims=True) + 1e-06)
    normed = mixed * inverse * norm_gain
    mask_table = tap_mask(frame_clip)
    first_frame = lax.axis_index("tm") * span_frames
    local_mask = lax.dynamic_slice_in_dim(mask_table, first_frame, span_frames, 0)
    following = shifted(cotangent, "tm", -1)
    extended = jnp.concatenate([cotangent, following], axis=0)
    grad_act = jnp.zeros((span_frames, slab_cells, channels), jnp.float32)
    for offset in range(3):
        term = jnp.einsum(
            "fco,io->fci",
            extended[offset : offset + span_frames],
            time_weight[offset],
            preferred_element_type=jnp.float32,
        )
        grad_act = grad_act + local_mask[:, offset][:, None, None] * term
    sigmoid_n = jax.nn.sigmoid(normed)
    grad_normed = grad_act * sigmoid_n * (1.0 + normed * (1.0 - sigmoid_n))
    gained = grad_normed * norm_gain
    grad_mixed = (
        inverse * gained
        - inverse * inverse * inverse * mixed * jnp.mean(gained * mixed, axis=2, keepdims=True)
    ).astype(jnp.bfloat16)
    grad_mixed = grad_mixed.reshape(span_rows, channels)
    grad_heads = jnp.einsum(
        "re,hde->hrd", grad_mixed, all_weights, preferred_element_type=jnp.float32
    ).astype(jnp.bfloat16)
    grad_out = lax.all_to_all(grad_heads, "tm", 0, 0, tiled=False).reshape(tok_local, HD)
    row_delta = jnp.sum(grad_out.astype(jnp.float32) * attended.astype(jnp.float32), axis=1)

    grad_q = attention_query_grad(
        rot_q, grad_out, log_col, row_delta[:, None], pair_all, cos_wide, sin_wide
    )
    stat_rows = split_exact(jnp.stack([log_total, row_delta]))
    stat_rows = stat_rows.reshape(-1, 2 * HD)
    stat_pad = (-stat_rows.shape[0]) % 16
    stat_rows = jnp.pad(stat_rows, ((0, stat_pad), (0, 0)))
    packed = jnp.concatenate([jnp.concatenate([rot_q, grad_out], axis=1), stat_rows], axis=0)
    block_rows = packed.shape[0]
    seq_count = lax.axis_size("seq")
    gathered = lax.all_gather(packed, "seq", axis=0, tiled=True).reshape(
        seq_count, block_rows, 2 * HD
    )
    grad_k, grad_v = attention_key_grad(
        rot_k,
        plain_v,
        gathered.reshape(seq_count * block_rows, 2 * HD),
        cos_wide,
        sin_wide,
        tok_local,
        block_rows,
    )
    grad_queries = grad_q[:, None, :]
    grad_keys = grad_k[:, None, :]
    grad_values = grad_v[:, None, :]
    return (grad_queries, grad_keys, grad_values)


def solution(mesh):
    in_specs = (
        P(("dp", "seq"), "tm", None),
        P(("dp", "seq"), "tm", None),
        P(("dp", "seq"), "tm", None),
        P("seq"),
        P("tm", None, None),
        P(),
        P(),
        P("dp"),
        P(("dp", "tm"), "seq", None),
    )
    out_specs = (
        P(("dp", "seq"), "tm", None),
        P(("dp", "seq"), "tm", None),
        P(("dp", "seq"), "tm", None),
    )
    return jax.shard_map(
        on_device, mesh=mesh, in_specs=in_specs, out_specs=out_specs, check_vma=False
    )
```

```python
import functools
import math

import jax
import jax.numpy as jnp
from jax import lax
from jax.experimental import pallas as pl
from jax.experimental.pallas import tpu as pltpu
from jax.sharding import PartitionSpec as P

HD = 128
GRID_W = 32
SCALE = HD ** (-0.5)
LOG2E = 1.4426950408889634
LN2 = 0.6931471805599453


def rotate_back_rows(x, cos_ref, sin_ref):
    lanes = lax.broadcasted_iota(jnp.int32, x.shape, 1)
    ahead = pltpu.roll(x, x.shape[1] - 1, 1)
    behind = pltpu.roll(x, 1, 1)
    ahead_lane = pltpu.roll(lanes, x.shape[1] - 1, 1)
    partner_lane = jnp.where(lanes % 2 == 0, lanes + 1, lanes - 1)
    partner = jnp.where(ahead_lane == partner_lane, ahead, behind)
    return x * cos_ref[...] + partner * sin_ref[...]


def rotate_kernel(q_ref, cos_ref, sin_ref, rq_ref):
    rq_ref[...] = rotate_back_rows(q_ref[...].astype(jnp.float32), cos_ref, sin_ref).astype(
        rq_ref.dtype
    )


def pair_kernel(k_ref, v_ref, cos_ref, sin_ref, kv_ref):
    kv_ref[:, :HD] = rotate_back_rows(k_ref[...].astype(jnp.float32), cos_ref, sin_ref).astype(
        kv_ref.dtype
    )
    kv_ref[:, HD:] = v_ref[...]


def prepare(q, k, v, cos_wide, sin_forward):
    rows = q.shape[0]
    pair = pl.pallas_call(
        pair_kernel,
        out_shape=jax.ShapeDtypeStruct((rows, 2 * HD), jnp.bfloat16),
        cost_estimate=pl.CostEstimate(flops=4 * rows * HD, transcendentals=0, bytes_accessed=16 * rows * HD),
    )(k, v, cos_wide, sin_forward)
    rot_q = pl.pallas_call(
        rotate_kernel,
        out_shape=jax.ShapeDtypeStruct((rows, HD), jnp.bfloat16),
        cost_estimate=pl.CostEstimate(flops=4 * rows * HD, transcendentals=0, bytes_accessed=12 * rows * HD),
    )(q, cos_wide, sin_forward)
    return rot_q, pair


def forward_kernel(key_block, q_ref, kv_ref, w_ref, out_ref, lse_ref, proj_ref):
    q = q_ref[...]
    rows = q.shape[0]
    steps = kv_ref.shape[0] // key_block

    def body(step, carry):
        top, total, acc = carry
        start = pl.multiple_of(step * key_block, key_block)
        k = kv_ref[pl.ds(start, key_block), :HD]
        v = kv_ref[pl.ds(start, key_block), HD:]
        s = lax.dot_general(q, k, (((1,), (1,)), ((), ())), preferred_element_type=jnp.float32) * (SCALE * LOG2E)
        new_top = jnp.maximum(top, jnp.max(s, axis=1, keepdims=True))
        factor = jnp.exp2(top - new_top)
        w = jnp.exp2(s - new_top)
        total = total * factor + jnp.sum(w, axis=1, keepdims=True)
        acc = acc * factor + jnp.dot(w.astype(jnp.bfloat16), v, preferred_element_type=jnp.float32)
        return new_top, total, acc

    k = kv_ref[pl.ds(0, key_block), :HD]
    v = kv_ref[pl.ds(0, key_block), HD:]
    s = lax.dot_general(q, k, (((1,), (1,)), ((), ())), preferred_element_type=jnp.float32) * (SCALE * LOG2E)
    top = jnp.max(s, axis=1, keepdims=True)
    w = jnp.exp2(s - top)
    start_state = (
        top,
        jnp.sum(w, axis=1, keepdims=True),
        jnp.dot(w.astype(jnp.bfloat16), v, preferred_element_type=jnp.float32),
    )
    top, total, acc = lax.fori_loop(1, steps, body, start_state, unroll=True)
    attended = (acc / total).astype(out_ref.dtype)
    out_ref[...] = attended
    proj_ref[...] = jnp.dot(attended, w_ref[...], preferred_element_type=jnp.float32).astype(
        proj_ref.dtype
    )
    lse_ref[...] = top * LN2 + jnp.log(total)


def attention_forward(q, kv_all, weight, query_block=512, key_block=2048):
    rows = q.shape[0]
    keys = kv_all.shape[0]
    cost = pl.CostEstimate(
        flops=4 * rows * keys * HD, transcendentals=rows * keys, bytes_accessed=2 * HD * (2 * rows + 2 * keys)
    )
    return pl.pallas_call(
        functools.partial(forward_kernel, key_block),
        grid=(rows // query_block,),
        in_specs=[
            pl.BlockSpec((query_block, HD), lambda i: (i, 0)),
            pl.BlockSpec((keys, 2 * HD), lambda i: (0, 0)),
            pl.BlockSpec(weight.shape, lambda i: (0, 0)),
        ],
        out_specs=[
            pl.BlockSpec((query_block, HD), lambda i: (i, 0)),
            pl.BlockSpec((query_block, 1), lambda i: (i, 0)),
            pl.BlockSpec((query_block, weight.shape[1]), lambda i: (i, 0)),
        ],
        out_shape=[
            jax.ShapeDtypeStruct((rows, HD), jnp.bfloat16),
            jax.ShapeDtypeStruct((rows, 1), jnp.float32),
            jax.ShapeDtypeStruct((rows, weight.shape[1]), jnp.bfloat16),
        ],
        compiler_params=pltpu.CompilerParams(dimension_semantics=("arbitrary",)),
        cost_estimate=cost,
    )(q, kv_all, weight)


def query_grad_kernel(key_block, q_ref, g_ref, lse_ref, delta_ref, kv_ref, cos_ref, sin_ref, dq_ref):
    q = q_ref[...]
    g = g_ref[...]
    lse = lse_ref[...] * LOG2E
    delta = delta_ref[...]
    steps = kv_ref.shape[0] // key_block

    def body(step, acc):
        start = pl.multiple_of(step * key_block, key_block)
        k = kv_ref[pl.ds(start, key_block), :HD]
        v = kv_ref[pl.ds(start, key_block), HD:]
        s = lax.dot_general(q, k, (((1,), (1,)), ((), ())), preferred_element_type=jnp.float32) * (SCALE * LOG2E)
        w = jnp.exp2(s - lse)
        gw = lax.dot_general(g, v, (((1,), (1,)), ((), ())), preferred_element_type=jnp.float32)
        gs = (w * (gw - delta)).astype(jnp.bfloat16)
        return acc + jnp.dot(gs, k, preferred_element_type=jnp.float32)

    acc = lax.fori_loop(0, steps, body, jnp.zeros(dq_ref.shape, jnp.float32), unroll=4)
    dq_ref[...] = rotate_back_rows(acc * SCALE, cos_ref, sin_ref).astype(dq_ref.dtype)


def attention_query_grad(q, g, lse_col, delta_col, kv_all, cos_wide, sin_wide, query_block=512, key_block=1024):
    rows = q.shape[0]
    keys = kv_all.shape[0]
    cost = pl.CostEstimate(
        flops=6 * rows * keys * HD, transcendentals=rows * keys, bytes_accessed=2 * HD * (3 * rows + 2 * keys)
    )
    row_spec = pl.BlockSpec((query_block, HD), lambda i: (i, 0))
    col_spec = pl.BlockSpec((query_block, 1), lambda i: (i, 0))
    whole = pl.BlockSpec((keys, 2 * HD), lambda i: (0, 0))
    return pl.pallas_call(
        functools.partial(query_grad_kernel, key_block),
        grid=(rows // query_block,),
        in_specs=[row_spec, row_spec, col_spec, col_spec, whole, row_spec, row_spec],
        out_specs=pl.BlockSpec((query_block, HD), lambda i: (i, 0)),
        out_shape=jax.ShapeDtypeStruct((rows, HD), jnp.bfloat16),
        compiler_params=pltpu.CompilerParams(dimension_semantics=("arbitrary",)),
        cost_estimate=cost,
    )(q, g, lse_col, delta_col, kv_all, cos_wide, sin_wide)


def stat_row(tile, stat, halves):
    parts = []
    for half in range(halves):
        row = stat * halves + half
        step = 2 * halves
        parts.append((tile[row : row + 1] + tile[step + row : step + row + 1]) + tile[2 * step + row : 2 * step + row + 1])
    return jnp.concatenate(parts, axis=1)


def key_grad_kernel(query_block, block_stride, blocks, k_ref, v_ref, qg_ref, cos_ref, sin_ref, dk_ref, dv_ref):
    k = k_ref[...]
    v = v_ref[...]
    steps = blocks
    halves = query_block // (2 * HD)

    def body(step, carry):
        dk, dv = carry
        start = pl.multiple_of(step * block_stride, 16)
        q = qg_ref[pl.ds(start, query_block), :HD]
        g = qg_ref[pl.ds(start, query_block), HD:]
        tile = qg_ref[pl.ds(start + query_block, 16), :].astype(jnp.float32)
        lse = stat_row(tile, 0, halves)
        delta = stat_row(tile, 1, halves)
        s = lax.dot_general(k, q, (((1,), (1,)), ((), ())), preferred_element_type=jnp.float32) * (SCALE * LOG2E)
        w = jnp.exp2(s - lse * LOG2E)
        gw = lax.dot_general(v, g, (((1,), (1,)), ((), ())), preferred_element_type=jnp.float32)
        gs = (w * (gw - delta)).astype(jnp.bfloat16)
        dk = dk + jnp.dot(gs, q, preferred_element_type=jnp.float32)
        dv = dv + jnp.dot(w.astype(jnp.bfloat16), g, preferred_element_type=jnp.float32)
        return dk, dv

    zero = jnp.zeros(dk_ref.shape, jnp.float32)
    dk, dv = lax.fori_loop(0, steps, body, (zero, zero), unroll=8)
    dk_ref[...] = rotate_back_rows(dk * SCALE, cos_ref, sin_ref).astype(dk_ref.dtype)
    dv_ref[...] = dv.astype(dv_ref.dtype)


def attention_key_grad(k, v, qg_all, cos_wide, sin_wide, query_block, block_stride, key_rows=512):
    rows = k.shape[0]
    blocks = qg_all.shape[0] // block_stride
    queries = blocks * query_block
    cost = pl.CostEstimate(
        flops=8 * rows * queries * HD, transcendentals=rows * queries, bytes_accessed=2 * HD * (2 * rows + 2 * queries)
    )
    row_spec = pl.BlockSpec((key_rows, HD), lambda i: (i, 0))
    whole = pl.BlockSpec(qg_all.shape, lambda i: (0, 0))
    return pl.pallas_call(
        functools.partial(key_grad_kernel, query_block, block_stride, blocks),
        grid=(rows // key_rows,),
        in_specs=[row_spec, row_spec, whole, row_spec, row_spec],
        out_specs=[row_spec, row_spec],
        out_shape=[jax.ShapeDtypeStruct((rows, HD), jnp.bfloat16)] * 2,
        compiler_params=pltpu.CompilerParams(dimension_semantics=("arbitrary",)),
        cost_estimate=cost,
    )(k, v, qg_all, cos_wide, sin_wide)


def shifted(value, axis, steps):
    count = lax.axis_size(axis)
    initial, last = (max(0, -steps), min(count, count - steps))
    return lax.ppermute(value, axis, [(source, source + steps) for source in range(initial, last)])


def frequencies(pair_count):
    return 1.0 / 10000.0 ** (jnp.arange(pair_count, dtype=jnp.float32) / pair_count)


def rope_tables(frame_pos, cell_ids):
    pair_count = HD // 2
    part_side = pair_count // 3
    part_time = pair_count - 2 * part_side
    grid_row = (cell_ids // GRID_W).astype(jnp.float32)
    grid_col = (cell_ids % GRID_W).astype(jnp.float32)
    angles = jnp.concatenate(
        [
            frame_pos.astype(jnp.float32)[:, None] * frequencies(part_time)[None, :],
            grid_row[:, None] * frequencies(part_side)[None, :],
            grid_col[:, None] * frequencies(part_side)[None, :],
        ],
        axis=1,
    )
    return (jnp.cos(angles), jnp.sin(angles))


def wide_tables(frame_pos, cell_ids):
    pair_count = HD // 2
    part_side = pair_count // 3
    part_time = pair_count - 2 * part_side
    freq = jnp.repeat(
        jnp.concatenate(
            [frequencies(part_time), frequencies(part_side), frequencies(part_side)]
        ),
        2,
    )
    pair = jnp.arange(HD, dtype=jnp.int32)[None, :] // 2
    grid_row = (cell_ids // GRID_W).astype(jnp.float32)[:, None]
    grid_col = (cell_ids % GRID_W).astype(jnp.float32)[:, None]
    cell_angles = jnp.where(pair < part_time + part_side, grid_row, grid_col) * freq[None, :]
    frame_angles = frame_pos.astype(jnp.float32)[:, None] * freq[None, :]
    frames = frame_angles.shape[0]
    cells = cell_angles.shape[0]
    time_lane = (pair < part_time)[None]
    even = jnp.arange(HD, dtype=jnp.int32)[None, :] % 2 == 0

    def spread(table_fn):
        by_frame = table_fn(frame_angles)[:, None, :]
        by_cell = table_fn(cell_angles)[None, :, :]
        return jnp.where(time_lane, by_frame, by_cell).reshape(frames * cells, HD)

    sin_wide = spread(jnp.sin)
    return (spread(jnp.cos), jnp.where(even, sin_wide, -sin_wide))


def rotate(vectors, cos_table, sin_table, direction):
    layout = vectors.shape
    paired = vectors.reshape(layout[:-1] + (layout[-1] // 2, 2))
    former = paired[..., 0]
    latter = paired[..., 1]
    out_former = former * cos_table - direction * latter * sin_table
    out_latter = direction * former * sin_table + latter * cos_table
    return jnp.stack([out_former, out_latter], axis=-1).reshape(layout)


def tap_mask(frame_clip):
    frame_total = frame_clip.shape[0]
    frame_ids = jnp.arange(frame_total, dtype=jnp.int32)
    columns = []
    for offset in range(3):
        target = frame_ids + offset
        inside = target < frame_total
        same_clip = frame_clip[jnp.minimum(target, frame_total - 1)] == frame_clip
        columns.append(jnp.logical_and(inside, same_clip).astype(jnp.float32))
    return jnp.stack(columns, axis=1)


def split_exact(values):
    high = lax.reduce_precision(values, exponent_bits=8, mantissa_bits=7)
    rest = values - high
    middle = lax.reduce_precision(rest, exponent_bits=8, mantissa_bits=7)
    low = rest - middle
    return jnp.stack([high, middle, low]).astype(jnp.bfloat16)


def cross(left, right):
    return lax.dot_general(
        left, right, (((1,), (1,)), ((), ())), preferred_element_type=jnp.float32
    )


def inner(left, right):
    return lax.dot_general(
        left, right, (((0,), (0,)), ((), ())), preferred_element_type=jnp.float32
    )


def on_device(
    queries, keys, values, token_cell, head_weight, norm_gain, time_weight, frame_clip, cotangent
):
    score_scale = HD ** (-0.5)
    tok_local = queries.shape[0]
    slab_cells = token_cell.shape[0]
    span_frames = cotangent.shape[0]
    channels = head_weight.shape[2]
    frame_pos = jnp.arange(tok_local, dtype=jnp.int32) // slab_cells
    cell_ids = jnp.tile(token_cell, tok_local // slab_cells)
    cos_wide, sin_wide = wide_tables(
        jnp.arange(tok_local // slab_cells, dtype=jnp.int32), token_cell
    )
    rot_q, pair = prepare(queries[:, 0, :], keys[:, 0, :], values[:, 0, :], cos_wide, -sin_wide)
    pair_all = lax.all_gather(pair, "seq", axis=0, tiled=True)
    all_weights = lax.all_gather(head_weight[0], "tm", axis=0, tiled=False)
    rot_k = pair[:, :HD]
    plain_v = values[:, 0, :]
    attended, log_col, projected = attention_forward(rot_q, pair_all, head_weight[0])
    log_total = log_col[:, 0]
    span_rows = span_frames * slab_cells
    head_count = lax.axis_size("tm")
    exchanged = lax.all_to_all(
        projected.reshape(head_count, span_frames * slab_cells, channels), "tm", 0, 0, tiled=False
    )
    mixed = jnp.sum(exchanged.astype(jnp.float32), axis=0).reshape(
        span_frames, slab_cells, channels
    )
    inverse = lax.rsqrt(jnp.mean(mixed * mixed, axis=2, keepdims=True) + 1e-06)
    normed = mixed * inverse * norm_gain
    mask_table = tap_mask(frame_clip)
    first_frame = lax.axis_index("tm") * span_frames
    local_mask = lax.dynamic_slice_in_dim(mask_table, first_frame, span_frames, 0)
    following = shifted(cotangent, "tm", -1)
    extended = jnp.concatenate([cotangent, following], axis=0)
    grad_act = jnp.zeros((span_frames, slab_cells, channels), jnp.float32)
    for offset in range(3):
        term = jnp.einsum(
            "fco,io->fci",
            extended[offset : offset + span_frames],
            time_weight[offset],
            preferred_element_type=jnp.float32,
        )
        grad_act = grad_act + local_mask[:, offset][:, None, None] * term
    sigmoid_n = jax.nn.sigmoid(normed)
    grad_normed = grad_act * sigmoid_n * (1.0 + normed * (1.0 - sigmoid_n))
    gained = grad_normed * norm_gain
    grad_mixed = (
        inverse * gained
        - inverse * inverse * inverse * mixed * jnp.mean(gained * mixed, axis=2, keepdims=True)
    ).astype(jnp.bfloat16)
    grad_mixed = grad_mixed.reshape(span_rows, channels)
    grad_heads = jnp.einsum(
        "re,hde->hrd", grad_mixed, all_weights, preferred_element_type=jnp.float32
    ).astype(jnp.bfloat16)
    grad_out = lax.all_to_all(grad_heads, "tm", 0, 0, tiled=False).reshape(tok_local, HD)
    row_delta = jnp.sum(grad_out.astype(jnp.float32) * attended.astype(jnp.float32), axis=1)

    grad_q = attention_query_grad(
        rot_q, grad_out, log_col, row_delta[:, None], pair_all, cos_wide, sin_wide
    )
    stat_rows = split_exact(jnp.stack([log_total, row_delta]))
    stat_rows = stat_rows.reshape(-1, 2 * HD)
    stat_pad = (-stat_rows.shape[0]) % 16
    stat_rows = jnp.pad(stat_rows, ((0, stat_pad), (0, 0)))
    packed = jnp.concatenate([jnp.concatenate([rot_q, grad_out], axis=1), stat_rows], axis=0)
    block_rows = packed.shape[0]
    seq_count = lax.axis_size("seq")
    gathered = lax.all_gather(packed, "seq", axis=0, tiled=True).reshape(
        seq_count, block_rows, 2 * HD
    )
    grad_k, grad_v = attention_key_grad(
        rot_k,
        plain_v,
        gathered.reshape(seq_count * block_rows, 2 * HD),
        cos_wide,
        sin_wide,
        tok_local,
        block_rows,
    )
    grad_queries = grad_q[:, None, :]
    grad_keys = grad_k[:, None, :]
    grad_values = grad_v[:, None, :]
    return (grad_queries, grad_keys, grad_values)


def solution(mesh):
    in_specs = (
        P(("dp", "seq"), "tm", None),
        P(("dp", "seq"), "tm", None),
        P(("dp", "seq"), "tm", None),
        P("seq"),
        P("tm", None, None),
        P(),
        P(),
        P("dp"),
        P(("dp", "tm"), "seq", None),
    )
    out_specs = (
        P(("dp", "seq"), "tm", None),
        P(("dp", "seq"), "tm", None),
        P(("dp", "seq"), "tm", None),
    )
    return jax.shard_map(
        on_device, mesh=mesh, in_specs=in_specs, out_specs=out_specs, check_vma=False
    )
```
